128 devices in a mesh: row: 8 (over x_lo, z), col: 16 (over y, x_hi, core).
Axes of the slice: x: 4 (x_hi: 2, x_lo: 2; x = x_hi * 2 + x_lo), y: 4, z: 4, core: 2. Of those that a mesh axis runs over, the one named last changes fastest.
Arguments:
- hidden_input: bfloat16 [16384, 1536], P(('row', 'col')), may hold values from -6 to 6
- lengths: int32 [8, 4], replicated, may hold values from 1 to 1536, 2048 in all within a row
- prompt_adapter: int32 [8, 4], replicated, may hold values from 0 to 63
- routes: int32 [16384, 4], P(('row', 'col')), may hold values from 0 to 31, all different within a row; in each aligned block of 128 rows (0 to 127, 128 to 255, ...) at most 40 rows name the same one
- attention_norm_gain: bfloat16 [1536], replicated, may hold values from 0.5 to 1.5
- expert_norm_gain: bfloat16 [1536], replicated, may hold values from 0.5 to 1.5
- projection_weight: bfloat16 [1536, 2048], P('row', 'col')
- output_weight: bfloat16 [1536, 1536], P('row', 'col'), may hold values from -0.15625 to 0.15625
- router: bfloat16 [1536, 32], replicated, may hold values from -0.5 to 0.5
- adapter_projection_down: bfloat16 [64, 16, 1536], P('col'), may hold values from -0.15625 to 0.15625
- adapter_projection_up: bfloat16 [64, 16, 2048], P('col'), may hold values from -1.5 to 1.5
- adapter_output_down: bfloat16 [64, 16, 1536], P('col'), may hold values from -0.15625 to 0.15625
- adapter_output_up: bfloat16 [64, 16, 1536], P('col'), may hold values from -1.5 to 1.5
- expert_gate_weight: bfloat16 [32, 1536, 768], P('col'), may hold values from -0.15625 to 0.15625
- expert_up_weight: bfloat16 [32, 1536, 768], P('col'), may hold values from -0.15625 to 0.15625
- expert_down_weight: bfloat16 [32, 768, 1536], P('col'), may hold values from -0.21875 to 0.21875
Outputs:
- hidden_out: bfloat16 [16384, 1536], P(('row', 'col'))
The draws below stay inside these ranges and needn't reach their ends.
Inputs may be any that keep to these rules, and one draw needn't show every extreme that they name: The 4 lengths of a block sum to 2048; in every block the longest prompt has exactly 1536 tokens. `prompt_adapter`: adapter a is held by index a // 4 of col. `routes`: the 4 experts of a token differ; among the rows of one device no expert is named more than 40 times, a bound that some block reaches. Expert e is held by index e // 2 of col.
All inputs are finite; a program needn't handle non-finite values.
Results may differ from the reference program's by a relative error of at most 0.012.
Values may be sent and summed in bfloat16 or wider, within the bound.
No kernel may reach another device: no remote copies, remote signals or barrier semaphores. Data moves between devices by JAX's collectives and lax.ppermute only.
A program may use at most 128 MiB of HBM per device.

```python
import math
import jax
import jax.numpy as jnp
import numpy as np
from jax import lax

MODEL_DIM = 1536
QUERY_HEADS = 12
KEY_HEADS = 2
HEAD_SIZE = 128
FF = 768
TOPK = 4
ADAPTER_RANK = 16
PROMPTS = 4
TOK_DEV = 128
QUERY_PER_KEY = 6
PROJ_COLUMNS = 2048
EXPERTS = 32
ADAPTER_COUNT = 64
TOKEN_BLOCK = 2048
TOKENS = 16384
CAP = 40
N_ROW = 8


def draw_projection_weight(key, part):
    random_subkeys = jax.random.split(jax.random.fold_in(key, 7), 1)
    entire_sequence = jax.random.normal(random_subkeys[0], (MODEL_DIM, PROJ_COLUMNS), jnp.float32) / math.sqrt(MODEL_DIM)
    return entire_sequence.astype(jnp.bfloat16)


def set_ends(drawn, key, least, high):
    dims = drawn.shape
    spot = [jax.random.randint(jax.random.fold_in(key, axis), (), 0, dims[axis]) for axis in range(len(dims))]
    drawn = drawn.at[tuple(spot)].set(least)
    longest = dims.index(max(dims))
    spot[longest] = (spot[longest] + 1) % dims[longest]
    return drawn.at[tuple(spot)].set(high)


def steps_of(own_key, dims, cuts, least, high):
    def one(dim, blocks):
        heights = jax.random.uniform(jax.random.fold_in(jax.random.fold_in(own_key, 6), dim), (blocks,), jnp.float32, least / len(cuts), high / len(cuts))
        return jnp.repeat(jnp.exp(heights), dims[dim] // blocks).reshape((-1,) + (1,) * (len(dims) - dim - 1))

    factor_of = one(*cuts[0])
    for cut in cuts[1:]:
        factor_of = factor_of * one(*cut)
    return factor_of


def split_up(number_of, total, limit, lean):
    loads = [(1 << 20) // math.isqrt(standing ** lean) + 1 for standing in range(2, number_of + 1)]
    surplus, given = total - limit - (number_of - 1), [1] * (number_of - 1)
    while surplus > 0:
        free = [i for i in range(number_of - 1) if given[i] < limit]
        mass, left = sum([loads[i] for i in free]), surplus
        for i in free:
            extra = min(limit - given[i], max(1, left * loads[i] // mass), surplus)
            given[i] = given[i] + extra
            surplus = surplus - extra
    return np.array([limit] + given)


def ragged(key, amount, total, reach, skew):
    if amount == 2:
        one = jax.random.randint(key, (), max(1, total - reach), min(reach, total - 1) + 1)
        return jnp.stack([one, total - one])
    tallies = jnp.asarray(split_up(amount, total, reach, skew), jnp.int32)
    couples = (amount - 1) // 2
    source_of, taker = tallies[1:1 + 2 * couples:2], tallies[2:2 + 2 * couples:2]
    margin = jnp.minimum(source_of - 1, reach - taker)
    passed = jax.random.randint(jax.random.fold_in(key, 1), (couples,), 0, 1 << 20) % (margin + 1)
    tallies = tallies.at[1:1 + 2 * couples:2].set(source_of - passed).at[2:2 + 2 * couples:2].set(taker + passed)
    return tallies[jax.random.permutation(jax.random.fold_in(key, 2), amount)]


def assign_block(key, own, number, rows, count, top, reach, lean):
    sequence = jax.random.permutation(key, count)
    packed, common = shares(count, rows * top, reach, lean, True), shares(count, rows * top, reach, lean, False)
    places = jnp.arange(count)

    def named(sizes, offset_by):
        used = int((sizes > 0).sum())
        fixed = max(1, used // 4)
        shifted = fixed + (places - fixed + offset_by * (used - fixed)) % max(1, count - fixed)
        return jnp.zeros((count,), jnp.int32).at[sequence[jnp.where(places < fixed, places, shifted)]].set(jnp.asarray(sizes, jnp.int32))

    sizes = jnp.where(number % 4 == 0, named(packed, number // 4), named(common, number - number // 4 - 1))
    mixed = jax.random.permutation(jax.random.fold_in(own, 3), count)
    source_of, taker = mixed[0:count // 2 * 2:2], mixed[1:count // 2 * 2:2]
    room = jnp.minimum(sizes[source_of] - 1, reach - sizes[taker]) // 2
    room = jnp.where((source_of == sequence[0]) | (taker == sequence[0]) | (sizes[taker] == 0), 0, jnp.maximum(room, 0))
    shifted = jax.random.randint(jax.random.fold_in(own, 4), (count // 2,), 0, 1 << 20) % (room + 1)
    sizes = sizes.at[source_of].add(-shifted).at[taker].add(shifted)
    labels = jnp.searchsorted(jnp.cumsum(sizes), jnp.arange(rows * top), side="right").astype(jnp.int32)
    listing = labels.reshape(top, rows).T
    listing = listing[jax.random.permutation(jax.random.fold_in(own, 1), rows)]
    offset_by = jax.random.randint(jax.random.fold_in(own, 2), (rows, 1), 0, top)
    return jnp.take_along_axis(listing, (jnp.arange(top)[None, :] + offset_by) % top, axis=1)


def shares(number_of, total, most, slope, full):
    weights = [(1 << 20) // math.isqrt(standing ** slope) + 1 for standing in range(1, number_of + 1)]
    largest = most if full else min(most, max(-(-total // number_of), total * weights[0] // sum(weights)))
    least = 1 if total - largest >= number_of - 1 else 0
    holding, rest = [largest] + [least] * (number_of - 1), total - largest - least * (number_of - 1)
    while rest > 0:
        free = [i for i in range(1, number_of) if holding[i] < largest] or [i for i in range(1, number_of) if holding[i] < most]
        pool, budget = sum([weights[i] for i in free]), rest
        for i in free:
            extra = min(most - holding[i], max(1, budget * weights[i] // pool), rest)
            holding[i] = holding[i] + extra
            rest = rest - extra
    return np.array(holding)


def gaussian(key, extent, scale, bound, cuts=(), held_as=jnp.bfloat16):
    gain = steps_of(key, extent, cuts, -0.22, 0.18) if cuts else 1.0
    entries = jax.random.normal(key, extent, jnp.float32) * scale * gain
    return jnp.minimum(jnp.maximum(entries, -bound), bound).astype(held_as)


def setup_inputs(seed: int = 0) -> dict:
    key_list = jax.random.split(jax.random.key(seed), 17)
    hidden_input = gaussian(key_list[0], (TOKENS, MODEL_DIM), 1.0, 6.0, ((0, 128),))
    lengths = jax.vmap(lambda own: ragged(own, PROMPTS, TOKEN_BLOCK, 3 * TOKEN_BLOCK // 4, 2))(jax.random.split(key_list[1], N_ROW)).reshape((N_ROW, PROMPTS)).astype(jnp.int32)
    prompt_adapter = set_ends(jax.random.randint(key_list[2], (N_ROW, PROMPTS), 0, ADAPTER_COUNT), jax.random.fold_in(key_list[2], 1), 0, ADAPTER_COUNT - 1).astype(jnp.int32)
    routes_keys = jax.random.split(jax.random.fold_in(key_list[3], 1), TOKENS // TOK_DEV)
    routes_turns = jax.random.permutation(jax.random.fold_in(key_list[3], 3), TOKENS // TOK_DEV)
    routes = jax.vmap(lambda own, number: assign_block(jax.random.fold_in(key_list[3], 2), own, number, TOK_DEV, EXPERTS, TOPK, CAP, 2))(routes_keys, routes_turns).reshape((TOKENS, TOPK))
    attention_norm_gain = jnp.clip(1.0 + 0.1 * jax.random.normal(key_list[4], (MODEL_DIM,), jnp.float32), 0.5, 1.5).astype(jnp.bfloat16)
    expert_norm_gain = jnp.clip(1.0 + 0.1 * jax.random.normal(key_list[5], (MODEL_DIM,), jnp.float32), 0.5, 1.5).astype(jnp.bfloat16)
    projection_weight = draw_projection_weight(jax.random.fold_in(key_list[16], 71), 0)
    output_weight = gaussian(key_list[7], (QUERY_HEADS * HEAD_SIZE, MODEL_DIM), (QUERY_HEADS * HEAD_SIZE) ** -0.5, 0.15625, ((0, 8), (1, 16)))
    router = gaussian(key_list[8], (MODEL_DIM, EXPERTS), 0.08, 0.5)
    adapter_projection_down = gaussian(key_list[9], (ADAPTER_COUNT, ADAPTER_RANK, MODEL_DIM), MODEL_DIM ** -0.5, 0.15625, ((0, 16),))
    adapter_projection_up = gaussian(key_list[10], (ADAPTER_COUNT, ADAPTER_RANK, PROJ_COLUMNS), ADAPTER_RANK ** -0.5, 1.5, ((0, 16),))
    adapter_output_down = gaussian(key_list[11], (ADAPTER_COUNT, ADAPTER_RANK, QUERY_HEADS * HEAD_SIZE), (QUERY_HEADS * HEAD_SIZE) ** -0.5, 0.15625, ((0, 16),))
    adapter_output_up = gaussian(key_list[12], (ADAPTER_COUNT, ADAPTER_RANK, MODEL_DIM), ADAPTER_RANK ** -0.5, 1.5, ((0, 16),))
    expert_gate_weight = gaussian(key_list[13], (EXPERTS, MODEL_DIM, FF), MODEL_DIM ** -0.5, 0.15625, ((0, 16),))
    expert_up_weight = gaussian(key_list[14], (EXPERTS, MODEL_DIM, FF), MODEL_DIM ** -0.5, 0.15625, ((0, 16),))
    expert_down_weight = gaussian(key_list[15], (EXPERTS, FF, MODEL_DIM), FF ** -0.5, 0.21875, ((0, 16),))
    return {"hidden_input": hidden_input, "lengths": lengths, "prompt_adapter": prompt_adapter, "routes": routes, "attention_norm_gain": attention_norm_gain, "expert_norm_gain": expert_norm_gain, "projection_weight": projection_weight, "output_weight": output_weight, "router": router, "adapter_projection_down": adapter_projection_down, "adapter_projection_up": adapter_projection_up, "adapter_output_down": adapter_output_down, "adapter_output_up": adapter_output_up, "expert_gate_weight": expert_gate_weight, "expert_up_weight": expert_up_weight, "expert_down_weight": expert_down_weight}


norm_eps = 1e-06
rope_base = 1000000.0
adapter_scale = 0.5

def rms_scaled(value_tensor, norm_gain):
    widened = value_tensor.astype(jnp.float32)
    inverse = lax.rsqrt(lax.optimization_barrier(jnp.mean(widened * widened, axis=-1, keepdims=True)) + norm_eps)
    return (widened * inverse * norm_gain.astype(jnp.float32)).astype(jnp.bfloat16)

def prompt_layout(lengths_row, tok_index):
    prompt_ends = jnp.cumsum(lengths_row)
    starts = prompt_ends - lengths_row
    prompt_of = lax.optimization_barrier(jnp.sum((tok_index[:, None] >= prompt_ends[None, :]).astype(jnp.int32), axis=1))
    within_prompt = prompt_of[:, None] == jnp.arange(lengths_row.shape[0], dtype=jnp.int32)[None, :]
    token_positions = tok_index - lax.optimization_barrier(jnp.sum(jnp.where(within_prompt, starts[None, :], 0), axis=1))
    return (prompt_of, within_prompt, token_positions)

def apply_rotary(value_tensor, token_positions):
    half_width = value_tensor.shape[-1] // 2
    frequency = rope_base ** (-2.0 * jnp.arange(half_width, dtype=jnp.float32) / value_tensor.shape[-1])
    angles = token_positions.astype(jnp.float32)[:, None] * frequency[None, :]
    cosine = jnp.cos(angles)[:, None, :]
    sine_part = jnp.sin(angles)[:, None, :]
    front_half = value_tensor[..., :half_width]
    back_half = value_tensor[..., half_width:]
    return jnp.concatenate([front_half * cosine - back_half * sine_part, back_half * cosine + front_half * sine_part], axis=-1)

def adapter_change(inputs, within_prompt, downs, ups):
    low_rank = jnp.einsum('nk,prk->npr', inputs.astype(jnp.float32), downs.astype(jnp.float32))
    low_rank = lax.optimization_barrier(jnp.where(within_prompt[:, :, None], low_rank, 0.0).astype(jnp.bfloat16))
    return jnp.einsum('npr,pro->no', low_rank.astype(jnp.float32), ups.astype(jnp.float32))

def route_slots(flat_routes, expert_total):
    marks = (flat_routes[:, None] == jnp.arange(expert_total, dtype=jnp.int32)[None, :]).astype(jnp.int32)
    before = jnp.cumsum(marks, axis=0) - marks
    return lax.optimization_barrier(jnp.sum(before * marks, axis=1))

def reference(hidden_input, lengths, prompt_adapter, routes, attention_norm_gain, expert_norm_gain, projection_weight, output_weight, router, adapter_projection_down, adapter_projection_up, adapter_output_down, adapter_output_up, expert_gate_weight, expert_up_weight, expert_down_weight):
    blocks = hidden_input.reshape(N_ROW, TOKEN_BLOCK, MODEL_DIM)

    def attend_block(inputs):
        block_rows, lengths_row, adapter_row = inputs
        tok_index = jnp.arange(TOKEN_BLOCK, dtype=jnp.int32)
        prompt_of, within_prompt, token_positions = prompt_layout(lengths_row, tok_index)
        normalized = rms_scaled(block_rows, attention_norm_gain)
        projection_all = jnp.dot(normalized, projection_weight, preferred_element_type=jnp.float32)
        projection_all = projection_all + adapter_scale * adapter_change(normalized, within_prompt, adapter_projection_down[adapter_row], adapter_projection_up[adapter_row])
        query_rows = apply_rotary(projection_all[:, :QUERY_HEADS * HEAD_SIZE].reshape(TOKEN_BLOCK, QUERY_HEADS, HEAD_SIZE), token_positions).astype(jnp.bfloat16)
        every_key = apply_rotary(projection_all[:, QUERY_HEADS * HEAD_SIZE:(QUERY_HEADS + KEY_HEADS) * HEAD_SIZE].reshape(TOKEN_BLOCK, KEY_HEADS, HEAD_SIZE), token_positions).astype(jnp.bfloat16)
        every_value = projection_all[:, (QUERY_HEADS + KEY_HEADS) * HEAD_SIZE:].astype(jnp.bfloat16).reshape(TOKEN_BLOCK, KEY_HEADS, HEAD_SIZE)
        allowed = (prompt_of[:, None] == prompt_of[None, :]) & (tok_index[None, :] <= tok_index[:, None])
        outputs = []
        for group_number in range(KEY_HEADS):
            query_group = query_rows[:, group_number * QUERY_PER_KEY:(group_number + 1) * QUERY_PER_KEY].astype(jnp.float32).transpose(1, 0, 2)
            scores = jnp.einsum('gqd,kd->gqk', query_group, every_key[:, group_number].astype(jnp.float32)) * HEAD_SIZE ** (-0.5)
            masked = jnp.where(allowed[None], scores, -1e+30)
            highest = lax.optimization_barrier(jnp.max(masked, axis=-1, keepdims=True))
            weights = jnp.where(allowed[None], jnp.exp(scores - highest), 0.0)
            running_sum = lax.optimization_barrier(jnp.sum(weights, axis=-1, keepdims=True))
            rounded = lax.optimization_barrier(weights.astype(jnp.bfloat16))
            mixed_output = jnp.einsum('gqk,kd->gqd', rounded.astype(jnp.float32), every_value[:, group_number].astype(jnp.float32)) / running_sum
            outputs.append(mixed_output.transpose(1, 0, 2))
        attention_result = jnp.concatenate(outputs, axis=1).reshape(TOKEN_BLOCK, QUERY_HEADS * HEAD_SIZE).astype(jnp.bfloat16)
        projected_rows = jnp.dot(attention_result, output_weight, preferred_element_type=jnp.float32)
        projected_rows = projected_rows + adapter_scale * adapter_change(attention_result, within_prompt, adapter_output_down[adapter_row], adapter_output_up[adapter_row])
        return (block_rows.astype(jnp.float32) + projected_rows).astype(jnp.bfloat16)
    residual = lax.map(attend_block, (blocks, lengths, prompt_adapter)).reshape(TOKENS, MODEL_DIM)
    normed_two = rms_scaled(residual, expert_norm_gain)
    logits = jnp.dot(normed_two, router, preferred_element_type=jnp.float32)
    squashed = jax.nn.sigmoid(jnp.take_along_axis(logits, routes, axis=1))
    mixing = squashed / lax.optimization_barrier(jnp.sum(squashed, axis=1, keepdims=True))
    devices_all = TOKENS // TOK_DEV
    per_device = routes.reshape(devices_all, TOK_DEV * TOPK)
    slots = jax.vmap(lambda flat_rows: route_slots(flat_rows, EXPERTS))(per_device).reshape(TOKENS, TOPK)
    places = (jnp.arange(TOKENS, dtype=jnp.int32) // TOK_DEV)[:, None] * CAP + slots
    slot_limit = devices_all * CAP

    def expert_step(combined, expert_id):
        buffer_rows = jnp.zeros((slot_limit, MODEL_DIM), jnp.bfloat16)
        for route_k in range(TOPK):
            target = jnp.where(routes[:, route_k] == expert_id, places[:, route_k], slot_limit)
            buffer_rows = buffer_rows.at[target].set(normed_two, mode='drop')
        gate_vals = jnp.dot(buffer_rows, expert_gate_weight[expert_id], preferred_element_type=jnp.float32)
        up_vals = jnp.dot(buffer_rows, expert_up_weight[expert_id], preferred_element_type=jnp.float32)
        hidden_vals = (jnp.maximum(gate_vals, 0.0) * up_vals).astype(jnp.bfloat16)
        answer = jnp.dot(hidden_vals, expert_down_weight[expert_id], preferred_element_type=jnp.float32).astype(jnp.bfloat16)
        for route_k in range(TOPK):
            matches = routes[:, route_k] == expert_id
            fetched = answer[jnp.minimum(places[:, route_k], slot_limit - 1)].astype(jnp.float32)
            combined = combined + jnp.where(matches[:, None], fetched * mixing[:, route_k:route_k + 1], 0.0)
        return (combined, expert_id)
    combined = lax.scan(expert_step, jnp.zeros((TOKENS, MODEL_DIM), jnp.float32), jnp.arange(EXPERTS, dtype=jnp.int32))[0]
    return (residual.astype(jnp.float32) + combined).astype(jnp.bfloat16)
```

```python
import jax
import jax.numpy as jnp
from jax import lax
from jax.sharding import PartitionSpec as P

QUERY_HEADS = 12
KEY_HEADS = 2
HEAD_SIZE = 128
QUERY_PER_KEY = 6
CAP = 40


norm_eps = 1e-06
rope_base = 1000000.0
adapter_scale = 0.5


def rms_scaled(value_tensor, norm_gain):
    widened = value_tensor.astype(jnp.float32)
    inverse = lax.rsqrt(jnp.mean(widened * widened, axis=-1, keepdims=True) + norm_eps)
    return (widened * inverse * norm_gain.astype(jnp.float32)).astype(jnp.bfloat16)


def prompt_layout(lengths_row, tok_index):
    prompt_ends = jnp.cumsum(lengths_row)
    starts = prompt_ends - lengths_row
    prompt_of = jnp.sum((tok_index[:, None] >= prompt_ends[None, :]).astype(jnp.int32), axis=1)
    within_prompt = prompt_of[:, None] == jnp.arange(lengths_row.shape[0], dtype=jnp.int32)[None, :]
    token_positions = tok_index - jnp.sum(jnp.where(within_prompt, starts[None, :], 0), axis=1)
    return (prompt_of, within_prompt, token_positions)


def apply_rotary(value_tensor, token_positions):
    half_width = value_tensor.shape[-1] // 2
    frequency = rope_base ** (
        -2.0 * jnp.arange(half_width, dtype=jnp.float32) / value_tensor.shape[-1]
    )
    angles = token_positions.astype(jnp.float32)[:, None] * frequency[None, :]
    cosine = jnp.cos(angles)[:, None, :]
    sine_part = jnp.sin(angles)[:, None, :]
    front_half = value_tensor[..., :half_width]
    back_half = value_tensor[..., half_width:]
    return jnp.concatenate(
        [front_half * cosine - back_half * sine_part, back_half * cosine + front_half * sine_part],
        axis=-1,
    )


def adapter_change(inputs, within_prompt, downs, ups):
    low_rank = jnp.einsum("nk,prk->npr", inputs, downs, preferred_element_type=jnp.float32)
    low_rank = jnp.where(within_prompt[:, :, None], low_rank, 0.0).astype(jnp.bfloat16)
    return jnp.einsum("npr,pro->no", low_rank, ups, preferred_element_type=jnp.float32)


def route_slots(flat_routes, expert_total):
    marks = (flat_routes[:, None] == jnp.arange(expert_total, dtype=jnp.int32)[None, :]).astype(
        jnp.int32
    )
    before = jnp.cumsum(marks, axis=0) - marks
    return jnp.sum(before * marks, axis=1)


def local(
    hidden_input,
    lengths,
    prompt_adapter,
    routes,
    attention_norm_gain,
    expert_norm_gain,
    projection_weight,
    output_weight,
    router,
    adapter_projection_down,
    adapter_projection_up,
    adapter_output_down,
    adapter_output_up,
    expert_gate_weight,
    expert_up_weight,
    expert_down_weight,
):
    token_rows = hidden_input.shape[0]
    model_width = hidden_input.shape[1]
    columns = lax.axis_size("col")
    row_index = lax.axis_index("row")
    col_index = lax.axis_index("col")
    lengths_row = lax.dynamic_index_in_dim(lengths, row_index, 0, keepdims=False)
    adapter_row = lax.dynamic_index_in_dim(prompt_adapter, row_index, 0, keepdims=False)
    tok_index = col_index * token_rows + jnp.arange(token_rows, dtype=jnp.int32)
    prompt_of, within_prompt, token_positions = prompt_layout(lengths_row, tok_index)
    row_count = lax.axis_size("row")

    def gather_whole(block):
        rows_here, cols_here = block.shape
        pieces = lax.all_gather(block[None], ("row", "col"), axis=0, tiled=True)
        pieces = pieces.reshape(row_count, columns, rows_here, cols_here).transpose(0, 2, 1, 3)
        return pieces.reshape(row_count * rows_here, columns * cols_here)

    qkv_full = gather_whole(projection_weight)
    out_full = gather_whole(output_weight)
    local_adapters = adapter_projection_down.shape[0]
    owner_column = adapter_row // local_adapters
    nearby_slot = adapter_row % local_adapters
    owned_here = (owner_column == col_index)[:, None, None]
    tables = (adapter_projection_down, adapter_projection_up, adapter_output_down, adapter_output_up)
    picked = jnp.concatenate(
        [
            jnp.where(owned_here, jnp.take(table, nearby_slot, axis=0), jnp.zeros((), table.dtype))
            for table in tables
        ],
        axis=-1,
    )
    picked_shape = picked.shape
    chunks = picked.reshape(columns, -1)
    received = lax.all_to_all(chunks, "col", 0, 0, tiled=True)
    reduced = jnp.sum(received.astype(jnp.float32), axis=0).astype(jnp.bfloat16)
    spread = lax.all_to_all(
        jnp.broadcast_to(reduced[None], (columns, reduced.shape[0])), "col", 0, 0, tiled=True
    )
    maps = spread.reshape(picked_shape)
    widths = [table.shape[-1] for table in tables]
    bounds = [sum(widths[:i]) for i in range(len(widths) + 1)]
    projection_down_map, projection_up_map, output_down_map, output_up_map = [
        maps[..., bounds[i] : bounds[i + 1]] for i in range(len(tables))
    ]
    normalized = rms_scaled(hidden_input, attention_norm_gain)
    projection_all = jnp.dot(normalized, qkv_full, preferred_element_type=jnp.float32)
    projection_all = projection_all + adapter_scale * adapter_change(
        normalized, within_prompt, projection_down_map, projection_up_map
    )
    query_slice = apply_rotary(
        projection_all[:, : QUERY_HEADS * HEAD_SIZE].reshape(token_rows, QUERY_HEADS, HEAD_SIZE),
        token_positions,
    ).astype(jnp.bfloat16)
    key_slice = apply_rotary(
        projection_all[:, QUERY_HEADS * HEAD_SIZE : (QUERY_HEADS + KEY_HEADS) * HEAD_SIZE].reshape(
            token_rows, KEY_HEADS, HEAD_SIZE
        ),
        token_positions,
    ).astype(jnp.bfloat16)
    value_slice = projection_all[:, (QUERY_HEADS + KEY_HEADS) * HEAD_SIZE :].astype(jnp.bfloat16)
    flattened_keys = key_slice.reshape(token_rows, KEY_HEADS * HEAD_SIZE)
    grouped = (
        query_slice.reshape(token_rows, KEY_HEADS, QUERY_PER_KEY, HEAD_SIZE)
        .transpose(1, 2, 0, 3)
        .reshape(KEY_HEADS, QUERY_PER_KEY * token_rows, HEAD_SIZE)
    )
    query_index = jnp.tile(tok_index, QUERY_PER_KEY)
    query_prompt = jnp.tile(prompt_of, QUERY_PER_KEY)
    key_value = lax.all_gather(
        jnp.concatenate([flattened_keys, value_slice], axis=1), "col", axis=0, tiled=True
    )
    segments = (key_value[:, : KEY_HEADS * HEAD_SIZE], key_value[:, KEY_HEADS * HEAD_SIZE :])
    best_experts = jnp.full((KEY_HEADS, QUERY_PER_KEY * token_rows), -1e30, jnp.float32)
    segment_length = segments[0].shape[0]
    key_lines = segments[0].reshape(segment_length, KEY_HEADS, HEAD_SIZE).transpose(1, 0, 2)
    value_lines = segments[1].reshape(segment_length, KEY_HEADS, HEAD_SIZE).transpose(1, 0, 2)
    key_index = jnp.arange(segment_length, dtype=jnp.int32)
    key_prompt = prompt_layout(lengths_row, key_index)[0]
    allowed = (key_prompt[None, :] == query_prompt[:, None]) & (
        key_index[None, :] <= query_index[:, None]
    )
    scores = jnp.einsum(
        "hqd,hkd->hqk", grouped, key_lines, preferred_element_type=jnp.float32
    ) * HEAD_SIZE ** (-0.5)
    masked = jnp.where(allowed[None], scores, -1e30)
    fresh = jnp.maximum(best_experts, jnp.max(masked, axis=-1))
    weights = jnp.where(allowed[None], jnp.exp(scores - fresh[..., None]), 0.0)
    running_new = jnp.sum(weights, axis=-1)
    accum_new = jnp.einsum(
        "hqk,hkd->hqd",
        weights.astype(jnp.bfloat16),
        value_lines,
        preferred_element_type=jnp.float32,
    )
    mixed_output = accum_new / running_new[..., None]
    attention_result = (
        mixed_output.reshape(KEY_HEADS, QUERY_PER_KEY, token_rows, HEAD_SIZE)
        .transpose(2, 0, 1, 3)
        .reshape(token_rows, QUERY_HEADS * HEAD_SIZE)
        .astype(jnp.bfloat16)
    )
    projected_rows = jnp.dot(attention_result, out_full, preferred_element_type=jnp.float32)
    projected_rows = projected_rows + adapter_scale * adapter_change(
        attention_result, within_prompt, output_down_map, output_up_map
    )
    residual = (hidden_input.astype(jnp.float32) + projected_rows).astype(jnp.bfloat16)
    normed_two = rms_scaled(residual, expert_norm_gain)
    logits = jnp.dot(normed_two, router, preferred_element_type=jnp.float32)
    squashed = jax.nn.sigmoid(jnp.take_along_axis(logits, routes, axis=1))
    mixing = squashed / jnp.sum(squashed, axis=1, keepdims=True)
    expert_total = router.shape[1]
    local_experts = expert_gate_weight.shape[0]
    flat_routes = routes.reshape(-1)
    slots = route_slots(flat_routes, expert_total)
    slot_total = expert_total * CAP
    route_id = (flat_routes * CAP + slots).reshape(token_rows, routes.shape[1])
    matches = route_id[:, :, None] == jnp.arange(slot_total, dtype=jnp.int32)[None, None, :]
    picks = jnp.sum(matches.astype(jnp.float32), axis=1)
    dispatch_rows = jnp.dot(
        picks.T.astype(jnp.bfloat16), normed_two, preferred_element_type=jnp.float32
    ).astype(jnp.bfloat16)
    sending = dispatch_rows.reshape(columns, local_experts, CAP, model_width)
    arrived = lax.all_to_all(sending, "col", split_axis=0, concat_axis=0, tiled=True)
    gate_vals = jnp.einsum(
        "sjcd,jdf->sjcf", arrived, expert_gate_weight, preferred_element_type=jnp.float32
    )
    up_vals = jnp.einsum(
        "sjcd,jdf->sjcf", arrived, expert_up_weight, preferred_element_type=jnp.float32
    )
    hidden_vals = (jnp.maximum(gate_vals, 0.0) * up_vals).astype(jnp.bfloat16)
    answered = jnp.einsum(
        "sjcf,jfd->sjcd", hidden_vals, expert_down_weight, preferred_element_type=jnp.float32
    ).astype(jnp.bfloat16)
    returned = lax.all_to_all(answered, "col", split_axis=0, concat_axis=0, tiled=True)
    returned_rows = returned.reshape(slot_total, model_width)
    mix_matrix = jnp.sum(jnp.where(matches, mixing[:, :, None], 0.0), axis=1)
    mix_high = mix_matrix.astype(jnp.bfloat16)
    mix_low = (mix_matrix - mix_high.astype(jnp.float32)).astype(jnp.bfloat16)
    combined = jnp.dot(mix_high, returned_rows, preferred_element_type=jnp.float32) + jnp.dot(
        mix_low, returned_rows, preferred_element_type=jnp.float32
    )
    return (residual.astype(jnp.float32) + combined).astype(jnp.bfloat16)


def solution(mesh):
    placed = (
        P(("row", "col"), None),
        P(),
        P(),
        P(("row", "col"), None),
        P(),
        P(),
        P("row", "col"),
        P("row", "col"),
        P(),
        P("col", None, None),
        P("col", None, None),
        P("col", None, None),
        P("col", None, None),
        P("col", None, None),
        P("col", None, None),
        P("col", None, None),
    )
    return jax.shard_map(
        local, mesh=mesh, in_specs=placed, out_specs=P(("row", "col"), None), check_vma=False
    )
```

```python
import jax
import jax.numpy as jnp
from jax import lax
from jax.sharding import PartitionSpec as P

QUERY_HEADS = 12
KEY_HEADS = 2
HEAD_SIZE = 128
QUERY_PER_KEY = 6
CAP = 40


norm_eps = 1e-06
rope_base = 1000000.0
adapter_scale = 0.5


def rms_scaled(value_tensor, norm_gain):
    widened = value_tensor.astype(jnp.float32)
    inverse = lax.rsqrt(jnp.mean(widened * widened, axis=-1, keepdims=True) + norm_eps)
    return (widened * inverse * norm_gain.astype(jnp.float32)).astype(jnp.bfloat16)


def prompt_layout(lengths_row, tok_index):
    prompt_ends = jnp.cumsum(lengths_row)
    starts = prompt_ends - lengths_row
    prompt_of = jnp.sum((tok_index[:, None] >= prompt_ends[None, :]).astype(jnp.int32), axis=1)
    within_prompt = prompt_of[:, None] == jnp.arange(lengths_row.shape[0], dtype=jnp.int32)[None, :]
    token_positions = tok_index - jnp.sum(jnp.where(within_prompt, starts[None, :], 0), axis=1)
    return (prompt_of, within_prompt, token_positions)


def apply_rotary(value_tensor, token_positions):
    half_width = value_tensor.shape[-1] // 2
    frequency = rope_base ** (
        -2.0 * jnp.arange(half_width, dtype=jnp.float32) / value_tensor.shape[-1]
    )
    angles = token_positions.astype(jnp.float32)[:, None] * frequency[None, :]
    cosine = jnp.cos(angles)[:, None, :]
    sine_part = jnp.sin(angles)[:, None, :]
    front_half = value_tensor[..., :half_width]
    back_half = value_tensor[..., half_width:]
    return jnp.concatenate(
        [front_half * cosine - back_half * sine_part, back_half * cosine + front_half * sine_part],
        axis=-1,
    )


def adapter_change(inputs, within_prompt, downs, ups):
    low_rank = jnp.einsum("nk,prk->npr", inputs, downs, preferred_element_type=jnp.float32)
    low_rank = jnp.where(within_prompt[:, :, None], low_rank, 0.0).astype(jnp.bfloat16)
    return jnp.einsum("npr,pro->no", low_rank, ups, preferred_element_type=jnp.float32)


def route_slots(flat_routes, expert_total):
    marks = (flat_routes[:, None] == jnp.arange(expert_total, dtype=jnp.int32)[None, :]).astype(
        jnp.int32
    )
    before = jnp.cumsum(marks, axis=0) - marks
    return jnp.sum(before * marks, axis=1)


def local(
    hidden_input,
    lengths,
    prompt_adapter,
    routes,
    attention_norm_gain,
    expert_norm_gain,
    projection_weight,
    output_weight,
    router,
    adapter_projection_down,
    adapter_projection_up,
    adapter_output_down,
    adapter_output_up,
    expert_gate_weight,
    expert_up_weight,
    expert_down_weight,
):
    token_rows = hidden_input.shape[0]
    model_width = hidden_input.shape[1]
    columns = lax.axis_size("col")
    row_index = lax.axis_index("row")
    col_index = lax.axis_index("col")
    lengths_row = lax.dynamic_index_in_dim(lengths, row_index, 0, keepdims=False)
    adapter_row = lax.dynamic_index_in_dim(prompt_adapter, row_index, 0, keepdims=False)
    tok_index = col_index * token_rows + jnp.arange(token_rows, dtype=jnp.int32)
    prompt_of, within_prompt, token_positions = prompt_layout(lengths_row, tok_index)
    core_index = col_index % 2
    partner = [(c, c ^ 1) for c in range(columns)]

    def gather_halves(block):
        rows_here = block.shape[0]
        slab = lax.all_gather(block.T, "col", axis=0, tiled=True).T
        half = slab.shape[1] // 2
        own = lax.dynamic_slice_in_dim(slab, core_index * half, half, axis=1)
        own = lax.all_gather(own, "row", axis=0, tiled=True)
        other = lax.ppermute(own, "col", partner)
        return own, other

    def times_halves(inputs, halves):
        own, other = halves
        half = own.shape[1]
        placed = jnp.zeros((inputs.shape[0], 2 * half), jnp.float32)
        placed = lax.dynamic_update_slice_in_dim(
            placed, jnp.dot(inputs, own, preferred_element_type=jnp.float32), core_index * half, 1
        )
        return lax.dynamic_update_slice_in_dim(
            placed,
            jnp.dot(inputs, other, preferred_element_type=jnp.float32),
            (1 - core_index) * half,
            1,
        )

    qkv_halves = gather_halves(projection_weight)
    out_halves = gather_halves(output_weight)
    local_adapters = adapter_projection_down.shape[0]
    owner_column = adapter_row // local_adapters
    nearby_slot = adapter_row % local_adapters
    owned_here = (owner_column == col_index)[:, None, None]
    tables = (adapter_projection_down, adapter_projection_up, adapter_output_down, adapter_output_up)
    picked = jnp.concatenate(
        [
            jnp.where(owned_here, jnp.take(table, nearby_slot, axis=0), jnp.zeros((), table.dtype))
            for table in tables
        ],
        axis=-1,
    )
    picked_shape = picked.shape
    chunks = picked.reshape(columns, -1)
    received = lax.all_to_all(chunks, "col", 0, 0, tiled=True)
    reduced = jnp.sum(received.astype(jnp.float32), axis=0).astype(jnp.bfloat16)
    spread = lax.all_to_all(
        jnp.broadcast_to(reduced[None], (columns, reduced.shape[0])), "col", 0, 0, tiled=True
    )
    maps = spread.reshape(picked_shape)
    widths = [table.shape[-1] for table in tables]
    bounds = [sum(widths[:i]) for i in range(len(widths) + 1)]
    projection_down_map, projection_up_map, output_down_map, output_up_map = [
        maps[..., bounds[i] : bounds[i + 1]] for i in range(len(tables))
    ]
    normalized = rms_scaled(hidden_input, attention_norm_gain)
    projection_all = times_halves(normalized, qkv_halves)
    projection_all = projection_all + adapter_scale * adapter_change(
        normalized, within_prompt, projection_down_map, projection_up_map
    )
    query_slice = apply_rotary(
        projection_all[:, : QUERY_HEADS * HEAD_SIZE].reshape(token_rows, QUERY_HEADS, HEAD_SIZE),
        token_positions,
    ).astype(jnp.bfloat16)
    key_slice = apply_rotary(
        projection_all[:, QUERY_HEADS * HEAD_SIZE : (QUERY_HEADS + KEY_HEADS) * HEAD_SIZE].reshape(
            token_rows, KEY_HEADS, HEAD_SIZE
        ),
        token_positions,
    ).astype(jnp.bfloat16)
    value_slice = projection_all[:, (QUERY_HEADS + KEY_HEADS) * HEAD_SIZE :].astype(jnp.bfloat16)
    flattened_keys = key_slice.reshape(token_rows, KEY_HEADS * HEAD_SIZE)
    grouped = (
        query_slice.reshape(token_rows, KEY_HEADS, QUERY_PER_KEY, HEAD_SIZE)
        .transpose(1, 2, 0, 3)
        .reshape(KEY_HEADS, QUERY_PER_KEY * token_rows, HEAD_SIZE)
    )
    query_index = jnp.tile(tok_index, QUERY_PER_KEY)
    query_prompt = jnp.tile(prompt_of, QUERY_PER_KEY)
    key_value_piece = jnp.concatenate([flattened_keys, value_slice], axis=1)
    key_value = lax.all_to_all(
        jnp.broadcast_to(key_value_piece[None], (columns,) + key_value_piece.shape),
        "col",
        0,
        0,
        tiled=True,
    ).reshape(columns * token_rows, key_value_piece.shape[1])
    segments = (key_value[:, : KEY_HEADS * HEAD_SIZE], key_value[:, KEY_HEADS * HEAD_SIZE :])
    best_experts = jnp.full((KEY_HEADS, QUERY_PER_KEY * token_rows), -1e30, jnp.float32)
    segment_length = segments[0].shape[0]
    key_lines = segments[0].reshape(segment_length, KEY_HEADS, HEAD_SIZE).transpose(1, 0, 2)
    value_lines = segments[1].reshape(segment_length, KEY_HEADS, HEAD_SIZE).transpose(1, 0, 2)
    key_index = jnp.arange(segment_length, dtype=jnp.int32)
    key_prompt = prompt_layout(lengths_row, key_index)[0]
    allowed = (key_prompt[None, :] == query_prompt[:, None]) & (
        key_index[None, :] <= query_index[:, None]
    )
    scores = jnp.einsum(
        "hqd,hkd->hqk", grouped, key_lines, preferred_element_type=jnp.float32
    ) * HEAD_SIZE ** (-0.5)
    masked = jnp.where(allowed[None], scores, -1e30)
    fresh = jnp.maximum(best_experts, jnp.max(masked, axis=-1))
    weights = jnp.where(allowed[None], jnp.exp(scores - fresh[..., None]), 0.0)
    running_new = jnp.sum(weights, axis=-1)
    accum_new = jnp.einsum(
        "hqk,hkd->hqd",
        weights.astype(jnp.bfloat16),
        value_lines,
        preferred_element_type=jnp.float32,
    )
    mixed_output = accum_new / running_new[..., None]
    attention_result = (
        mixed_output.reshape(KEY_HEADS, QUERY_PER_KEY, token_rows, HEAD_SIZE)
        .transpose(2, 0, 1, 3)
        .reshape(token_rows, QUERY_HEADS * HEAD_SIZE)
        .astype(jnp.bfloat16)
    )
    projected_rows = times_halves(attention_result, out_halves)
    projected_rows = projected_rows + adapter_scale * adapter_change(
        attention_result, within_prompt, output_down_map, output_up_map
    )
    residual = (hidden_input.astype(jnp.float32) + projected_rows).astype(jnp.bfloat16)
    normed_two = rms_scaled(residual, expert_norm_gain)
    logits = jnp.dot(normed_two, router, preferred_element_type=jnp.float32)
    squashed = jax.nn.sigmoid(jnp.take_along_axis(logits, routes, axis=1))
    mixing = squashed / jnp.sum(squashed, axis=1, keepdims=True)
    expert_total = router.shape[1]
    local_experts = expert_gate_weight.shape[0]
    flat_routes = routes.reshape(-1)
    slots = route_slots(flat_routes, expert_total)
    slot_total = expert_total * CAP
    route_id = (flat_routes * CAP + slots).reshape(token_rows, routes.shape[1])
    matches = route_id[:, :, None] == jnp.arange(slot_total, dtype=jnp.int32)[None, None, :]
    picks = jnp.sum(matches.astype(jnp.float32), axis=1)
    dispatch_rows = jnp.dot(
        picks.T.astype(jnp.bfloat16), normed_two, preferred_element_type=jnp.float32
    ).astype(jnp.bfloat16)
    sending = dispatch_rows.reshape(columns, local_experts, CAP, model_width)
    arrived = lax.all_to_all(sending, "col", split_axis=0, concat_axis=0, tiled=True)
    gate_vals = jnp.einsum(
        "sjcd,jdf->sjcf", arrived, expert_gate_weight, preferred_element_type=jnp.float32
    )
    up_vals = jnp.einsum(
        "sjcd,jdf->sjcf", arrived, expert_up_weight, preferred_element_type=jnp.float32
    )
    hidden_vals = (jnp.maximum(gate_vals, 0.0) * up_vals).astype(jnp.bfloat16)
    answered = jnp.einsum(
        "sjcf,jfd->sjcd", hidden_vals, expert_down_weight, preferred_element_type=jnp.float32
    ).astype(jnp.bfloat16)
    returned = lax.all_to_all(answered, "col", split_axis=0, concat_axis=0, tiled=True)
    returned_rows = returned.reshape(slot_total, model_width)
    mix_matrix = jnp.sum(jnp.where(matches, mixing[:, :, None], 0.0), axis=1)
    mix_high = mix_matrix.astype(jnp.bfloat16)
    mix_low = (mix_matrix - mix_high.astype(jnp.float32)).astype(jnp.bfloat16)
    combined = jnp.dot(mix_high, returned_rows, preferred_element_type=jnp.float32) + jnp.dot(
        mix_low, returned_rows, preferred_element_type=jnp.float32
    )
    return (residual.astype(jnp.float32) + combined).astype(jnp.bfloat16)


def solution(mesh):
    placed = (
        P(("row", "col"), None),
        P(),
        P(),
        P(("row", "col"), None),
        P(),
        P(),
        P("row", "col"),
        P("row", "col"),
        P(),
        P("col", None, None),
        P("col", None, None),
        P("col", None, None),
        P("col", None, None),
        P("col", None, None),
        P("col", None, None),
        P("col", None, None),
    )
    return jax.shard_map(
        local, mesh=mesh, in_specs=placed, out_specs=P(("row", "col"), None), check_vma=False
    )
```

```python
import jax
import jax.numpy as jnp
from jax import lax
from jax.sharding import PartitionSpec as P

QUERY_HEADS = 12
KEY_HEADS = 2
HEAD_SIZE = 128
QUERY_PER_KEY = 6
CAP = 40


norm_eps = 1e-06
rope_base = 1000000.0
adapter_scale = 0.5


def rms_scaled(value_tensor, norm_gain):
    widened = value_tensor.astype(jnp.float32)
    inverse = lax.rsqrt(jnp.mean(widened * widened, axis=-1, keepdims=True) + norm_eps)
    return (widened * inverse * norm_gain.astype(jnp.float32)).astype(jnp.bfloat16)


def prompt_layout(lengths_row, tok_index):
    prompt_ends = jnp.cumsum(lengths_row)
    starts = prompt_ends - lengths_row
    prompt_of = jnp.sum((tok_index[:, None] >= prompt_ends[None, :]).astype(jnp.int32), axis=1)
    within_prompt = prompt_of[:, None] == jnp.arange(lengths_row.shape[0], dtype=jnp.int32)[None, :]
    token_positions = tok_index - jnp.sum(jnp.where(within_prompt, starts[None, :], 0), axis=1)
    return (prompt_of, within_prompt, token_positions)


def apply_rotary(value_tensor, token_positions):
    half_width = value_tensor.shape[-1] // 2
    frequency = rope_base ** (
        -2.0 * jnp.arange(half_width, dtype=jnp.float32) / value_tensor.shape[-1]
    )
    angles = token_positions.astype(jnp.float32)[:, None] * frequency[None, :]
    cosine = jnp.cos(angles)[:, None, :]
    sine_part = jnp.sin(angles)[:, None, :]
    front_half = value_tensor[..., :half_width]
    back_half = value_tensor[..., half_width:]
    return jnp.concatenate(
        [front_half * cosine - back_half * sine_part, back_half * cosine + front_half * sine_part],
        axis=-1,
    )


def adapter_change(inputs, within_prompt, downs, ups):
    low_rank = jnp.einsum("nk,prk->npr", inputs, downs, preferred_element_type=jnp.float32)
    low_rank = jnp.where(within_prompt[:, :, None], low_rank, 0.0).astype(jnp.bfloat16)
    return jnp.einsum("npr,pro->no", low_rank, ups, preferred_element_type=jnp.float32)


def route_slots(flat_routes, expert_total):
    marks = (flat_routes[:, None] == jnp.arange(expert_total, dtype=jnp.int32)[None, :]).astype(
        jnp.int32
    )
    before = jnp.cumsum(marks, axis=0) - marks
    return jnp.sum(before * marks, axis=1)


def local(
    hidden_input,
    lengths,
    prompt_adapter,
    routes,
    attention_norm_gain,
    expert_norm_gain,
    projection_weight,
    output_weight,
    router,
    adapter_projection_down,
    adapter_projection_up,
    adapter_output_down,
    adapter_output_up,
    expert_gate_weight,
    expert_up_weight,
    expert_down_weight,
):
    token_rows = hidden_input.shape[0]
    model_width = hidden_input.shape[1]
    columns = lax.axis_size("col")
    row_index = lax.axis_index("row")
    col_index = lax.axis_index("col")
    lengths_row = lax.dynamic_index_in_dim(lengths, row_index, 0, keepdims=False)
    adapter_row = lax.dynamic_index_in_dim(prompt_adapter, row_index, 0, keepdims=False)
    tok_index = col_index * token_rows + jnp.arange(token_rows, dtype=jnp.int32)
    prompt_of, within_prompt, token_positions = prompt_layout(lengths_row, tok_index)
    core_index = col_index % 2
    partner = [(c, c ^ 1) for c in range(columns)]

    def gather_halves(block):
        rows_here, cols_here = block.shape
        slab = lax.all_to_all(
            jnp.broadcast_to(block[None], (columns, rows_here, cols_here)), "col", 0, 0, tiled=True
        )
        slab = slab.transpose(1, 0, 2).reshape(rows_here, columns * cols_here)
        half = slab.shape[1] // 2
        own = lax.dynamic_slice_in_dim(slab, core_index * half, half, axis=1)
        own = lax.all_gather(own, "row", axis=0, tiled=True)
        other = lax.ppermute(own, "col", partner)
        return own, other

    def times_halves(inputs, halves):
        own, other = halves
        half = own.shape[1]
        placed = jnp.zeros((inputs.shape[0], 2 * half), jnp.float32)
        placed = lax.dynamic_update_slice_in_dim(
            placed, jnp.dot(inputs, own, preferred_element_type=jnp.float32), core_index * half, 1
        )
        return lax.dynamic_update_slice_in_dim(
            placed,
            jnp.dot(inputs, other, preferred_element_type=jnp.float32),
            (1 - core_index) * half,
            1,
        )

    qkv_halves = gather_halves(projection_weight)
    out_halves = gather_halves(output_weight)
    local_adapters = adapter_projection_down.shape[0]
    owner_column = adapter_row // local_adapters
    nearby_slot = adapter_row % local_adapters
    owned_here = (owner_column == col_index)[:, None, None]
    tables = (adapter_projection_down, adapter_projection_up, adapter_output_down, adapter_output_up)
    picked = jnp.concatenate(
        [
            jnp.where(owned_here, jnp.take(table, nearby_slot, axis=0), jnp.zeros((), table.dtype))
            for table in tables
        ],
        axis=-1,
    )
    picked_shape = picked.shape
    chunks = picked.reshape(columns, -1)
    received = lax.all_to_all(chunks, "col", 0, 0, tiled=True)
    reduced = jnp.sum(received.astype(jnp.float32), axis=0).astype(jnp.bfloat16)
    spread = lax.all_to_all(
        jnp.broadcast_to(reduced[None], (columns, reduced.shape[0])), "col", 0, 0, tiled=True
    )
    maps = spread.reshape(picked_shape)
    widths = [table.shape[-1] for table in tables]
    bounds = [sum(widths[:i]) for i in range(len(widths) + 1)]
    projection_down_map, projection_up_map, output_down_map, output_up_map = [
        maps[..., bounds[i] : bounds[i + 1]] for i in range(len(tables))
    ]
    normalized = rms_scaled(hidden_input, attention_norm_gain)
    projection_all = times_halves(normalized, qkv_halves)
    projection_all = projection_all + adapter_scale * adapter_change(
        normalized, within_prompt, projection_down_map, projection_up_map
    )
    query_slice = apply_rotary(
        projection_all[:, : QUERY_HEADS * HEAD_SIZE].reshape(token_rows, QUERY_HEADS, HEAD_SIZE),
        token_positions,
    ).astype(jnp.bfloat16)
    key_slice = apply_rotary(
        projection_all[:, QUERY_HEADS * HEAD_SIZE : (QUERY_HEADS + KEY_HEADS) * HEAD_SIZE].reshape(
            token_rows, KEY_HEADS, HEAD_SIZE
        ),
        token_positions,
    ).astype(jnp.bfloat16)
    value_slice = projection_all[:, (QUERY_HEADS + KEY_HEADS) * HEAD_SIZE :].astype(jnp.bfloat16)
    flattened_keys = key_slice.reshape(token_rows, KEY_HEADS * HEAD_SIZE)
    grouped = (
        query_slice.reshape(token_rows, KEY_HEADS, QUERY_PER_KEY, HEAD_SIZE)
        .transpose(1, 2, 0, 3)
        .reshape(KEY_HEADS, QUERY_PER_KEY * token_rows, HEAD_SIZE)
    )
    query_index = jnp.tile(tok_index, QUERY_PER_KEY)
    query_prompt = jnp.tile(prompt_of, QUERY_PER_KEY)
    key_value_piece = jnp.concatenate([flattened_keys, value_slice], axis=1)
    key_value = lax.all_to_all(
        jnp.broadcast_to(key_value_piece[None], (columns,) + key_value_piece.shape),
        "col",
        0,
        0,
        tiled=True,
    ).reshape(columns * token_rows, key_value_piece.shape[1])
    segments = (key_value[:, : KEY_HEADS * HEAD_SIZE], key_value[:, KEY_HEADS * HEAD_SIZE :])
    best_experts = jnp.full((KEY_HEADS, QUERY_PER_KEY * token_rows), -1e30, jnp.float32)
    segment_length = segments[0].shape[0]
    key_lines = segments[0].reshape(segment_length, KEY_HEADS, HEAD_SIZE).transpose(1, 0, 2)
    value_lines = segments[1].reshape(segment_length, KEY_HEADS, HEAD_SIZE).transpose(1, 0, 2)
    key_index = jnp.arange(segment_length, dtype=jnp.int32)
    key_prompt = prompt_layout(lengths_row, key_index)[0]
    allowed = (key_prompt[None, :] == query_prompt[:, None]) & (
        key_index[None, :] <= query_index[:, None]
    )
    scores = jnp.einsum(
        "hqd,hkd->hqk", grouped, key_lines, preferred_element_type=jnp.float32
    ) * HEAD_SIZE ** (-0.5)
    masked = jnp.where(allowed[None], scores, -1e30)
    fresh = jnp.maximum(best_experts, jnp.max(masked, axis=-1))
    weights = jnp.where(allowed[None], jnp.exp(scores - fresh[..., None]), 0.0)
    running_new = jnp.sum(weights, axis=-1)
    accum_new = jnp.einsum(
        "hqk,hkd->hqd",
        weights.astype(jnp.bfloat16),
        value_lines,
        preferred_element_type=jnp.float32,
    )
    mixed_output = accum_new / running_new[..., None]
    attention_result = (
        mixed_output.reshape(KEY_HEADS, QUERY_PER_KEY, token_rows, HEAD_SIZE)
        .transpose(2, 0, 1, 3)
        .reshape(token_rows, QUERY_HEADS * HEAD_SIZE)
        .astype(jnp.bfloat16)
    )
    projected_rows = times_halves(attention_result, out_halves)
    projected_rows = projected_rows + adapter_scale * adapter_change(
        attention_result, within_prompt, output_down_map, output_up_map
    )
    residual = (hidden_input.astype(jnp.float32) + projected_rows).astype(jnp.bfloat16)
    normed_two = rms_scaled(residual, expert_norm_gain)
    logits = jnp.dot(normed_two, router, preferred_element_type=jnp.float32)
    squashed = jax.nn.sigmoid(jnp.take_along_axis(logits, routes, axis=1))
    mixing = squashed / jnp.sum(squashed, axis=1, keepdims=True)
    expert_total = router.shape[1]
    local_experts = expert_gate_weight.shape[0]
    flat_routes = routes.reshape(-1)
    slots = route_slots(flat_routes, expert_total)
    slot_total = expert_total * CAP
    route_id = (flat_routes * CAP + slots).reshape(token_rows, routes.shape[1])
    matches = route_id[:, :, None] == jnp.arange(slot_total, dtype=jnp.int32)[None, None, :]
    picks = jnp.sum(matches.astype(jnp.float32), axis=1)
    dispatch_rows = jnp.dot(
        picks.T.astype(jnp.bfloat16), normed_two, preferred_element_type=jnp.float32
    ).astype(jnp.bfloat16)
    sending = dispatch_rows.reshape(columns, local_experts, CAP, model_width)
    arrived = lax.all_to_all(sending, "col", split_axis=0, concat_axis=0, tiled=True)
    gate_vals = jnp.einsum(
        "sjcd,jdf->sjcf", arrived, expert_gate_weight, preferred_element_type=jnp.float32
    )
    up_vals = jnp.einsum(
        "sjcd,jdf->sjcf", arrived, expert_up_weight, preferred_element_type=jnp.float32
    )
    hidden_vals = (jnp.maximum(gate_vals, 0.0) * up_vals).astype(jnp.bfloat16)
    answered = jnp.einsum(
        "sjcf,jfd->sjcd", hidden_vals, expert_down_weight, preferred_element_type=jnp.float32
    ).astype(jnp.bfloat16)
    returned = lax.all_to_all(answered, "col", split_axis=0, concat_axis=0, tiled=True)
    returned_rows = returned.reshape(slot_total, model_width)
    mix_matrix = jnp.sum(jnp.where(matches, mixing[:, :, None], 0.0), axis=1)
    mix_high = mix_matrix.astype(jnp.bfloat16)
    mix_low = (mix_matrix - mix_high.astype(jnp.float32)).astype(jnp.bfloat16)
    combined = jnp.dot(mix_high, returned_rows, preferred_element_type=jnp.float32) + jnp.dot(
        mix_low, returned_rows, preferred_element_type=jnp.float32
    )
    return (residual.astype(jnp.float32) + combined).astype(jnp.bfloat16)


def solution(mesh):
    placed = (
        P(("row", "col"), None),
        P(),
        P(),
        P(("row", "col"), None),
        P(),
        P(),
        P("row", "col"),
        P("row", "col"),
        P(),
        P("col", None, None),
        P("col", None, None),
        P("col", None, None),
        P("col", None, None),
        P("col", None, None),
        P("col", None, None),
        P("col", None, None),
    )
    return jax.shard_map(
        local, mesh=mesh, in_specs=placed, out_specs=P(("row", "col"), None), check_vma=False
    )
```

```python
import jax
import jax.numpy as jnp
from jax import lax
from jax.sharding import PartitionSpec as P

QUERY_HEADS = 12
KEY_HEADS = 2
HEAD_SIZE = 128
QUERY_PER_KEY = 6
CAP = 40


norm_eps = 1e-06
rope_base = 1000000.0
adapter_scale = 0.5


def rms_scaled(value_tensor, norm_gain):
    widened = value_tensor.astype(jnp.float32)
    inverse = lax.rsqrt(jnp.mean(widened * widened, axis=-1, keepdims=True) + norm_eps)
    return (widened * inverse * norm_gain.astype(jnp.float32)).astype(jnp.bfloat16)


def prompt_layout(lengths_row, tok_index):
    prompt_ends = jnp.cumsum(lengths_row)
    starts = prompt_ends - lengths_row
    prompt_of = jnp.sum((tok_index[:, None] >= prompt_ends[None, :]).astype(jnp.int32), axis=1)
    within_prompt = prompt_of[:, None] == jnp.arange(lengths_row.shape[0], dtype=jnp.int32)[None, :]
    token_positions = tok_index - jnp.sum(jnp.where(within_prompt, starts[None, :], 0), axis=1)
    return (prompt_of, within_prompt, token_positions)


def apply_rotary(value_tensor, token_positions):
    half_width = value_tensor.shape[-1] // 2
    frequency = rope_base ** (
        -2.0 * jnp.arange(half_width, dtype=jnp.float32) / value_tensor.shape[-1]
    )
    angles = token_positions.astype(jnp.float32)[:, None] * frequency[None, :]
    cosine = jnp.cos(angles)[:, None, :]
    sine_part = jnp.sin(angles)[:, None, :]
    front_half = value_tensor[..., :half_width]
    back_half = value_tensor[..., half_width:]
    return jnp.concatenate(
        [front_half * cosine - back_half * sine_part, back_half * cosine + front_half * sine_part],
        axis=-1,
    )


def adapter_change(inputs, within_prompt, downs, ups):
    low_rank = jnp.einsum("nk,prk->npr", inputs, downs, preferred_element_type=jnp.float32)
    low_rank = jnp.where(within_prompt[:, :, None], low_rank, 0.0).astype(jnp.bfloat16)
    return jnp.einsum("npr,pro->no", low_rank, ups, preferred_element_type=jnp.float32)


def route_slots(flat_routes, expert_total):
    marks = (flat_routes[:, None] == jnp.arange(expert_total, dtype=jnp.int32)[None, :]).astype(
        jnp.int32
    )
    before = jnp.cumsum(marks, axis=0) - marks
    return jnp.sum(before * marks, axis=1)


def local(
    hidden_input,
    lengths,
    prompt_adapter,
    routes,
    attention_norm_gain,
    expert_norm_gain,
    projection_weight,
    output_weight,
    router,
    adapter_projection_down,
    adapter_projection_up,
    adapter_output_down,
    adapter_output_up,
    expert_gate_weight,
    expert_up_weight,
    expert_down_weight,
):
    token_rows = hidden_input.shape[0]
    model_width = hidden_input.shape[1]
    columns = lax.axis_size("col")
    row_index = lax.axis_index("row")
    col_index = lax.axis_index("col")
    lengths_row = lax.dynamic_index_in_dim(lengths, row_index, 0, keepdims=False)
    adapter_row = lax.dynamic_index_in_dim(prompt_adapter, row_index, 0, keepdims=False)
    tok_index = col_index * token_rows + jnp.arange(token_rows, dtype=jnp.int32)
    prompt_of, within_prompt, token_positions = prompt_layout(lengths_row, tok_index)
    local_adapters = adapter_projection_down.shape[0]
    owner_column = adapter_row // local_adapters
    nearby_slot = adapter_row % local_adapters
    owned_here = (owner_column == col_index)[:, None, None]
    tables = (adapter_projection_down, adapter_projection_up, adapter_output_down, adapter_output_up)
    picked = jnp.concatenate(
        [
            jnp.where(owned_here, jnp.take(table, nearby_slot, axis=0), jnp.zeros((), table.dtype))
            for table in tables
        ],
        axis=-1,
    )
    picked_shape = picked.shape
    lane = 128
    chunks = picked.reshape(columns, -1, lane)
    received = lax.all_to_all(chunks, "col", 0, 0, tiled=True)
    reduced = jnp.sum(received.astype(jnp.float32), axis=0).astype(jnp.bfloat16)
    spread = lax.all_to_all(
        jnp.broadcast_to(reduced[None], (columns,) + reduced.shape), "col", 0, 0, tiled=True
    )
    core_index = col_index % 2
    partner = [(c, c ^ 1) for c in range(columns)]

    def gather_halves(block):
        rows_here, cols_here = block.shape
        slab = lax.all_to_all(
            jnp.broadcast_to(block[None], (columns, rows_here, cols_here)), "col", 0, 0, tiled=True
        )
        slab = slab.transpose(1, 0, 2).reshape(rows_here, columns * cols_here)
        slab, _ = lax.optimization_barrier((slab, received))
        half = slab.shape[1] // 2
        own = lax.dynamic_slice_in_dim(slab, core_index * half, half, axis=1)
        own = lax.all_gather(own, "row", axis=0, tiled=True)
        other = lax.ppermute(own, "col", partner)
        return own, other

    def times_halves(inputs, halves):
        own, other = halves
        half = own.shape[1]
        placed = jnp.zeros((inputs.shape[0], 2 * half), jnp.float32)
        placed = lax.dynamic_update_slice_in_dim(
            placed, jnp.dot(inputs, own, preferred_element_type=jnp.float32), core_index * half, 1
        )
        return lax.dynamic_update_slice_in_dim(
            placed,
            jnp.dot(inputs, other, preferred_element_type=jnp.float32),
            (1 - core_index) * half,
            1,
        )

    qkv_halves = gather_halves(projection_weight)
    out_halves = gather_halves(output_weight)
    maps = spread.reshape(picked_shape)
    widths = [table.shape[-1] for table in tables]
    bounds = [sum(widths[:i]) for i in range(len(widths) + 1)]
    projection_down_map, projection_up_map, output_down_map, output_up_map = [
        maps[..., bounds[i] : bounds[i + 1]] for i in range(len(tables))
    ]
    normalized = rms_scaled(hidden_input, attention_norm_gain)
    projection_all = times_halves(normalized, qkv_halves)
    projection_all = projection_all + adapter_scale * adapter_change(
        normalized, within_prompt, projection_down_map, projection_up_map
    )
    query_slice = apply_rotary(
        projection_all[:, : QUERY_HEADS * HEAD_SIZE].reshape(token_rows, QUERY_HEADS, HEAD_SIZE),
        token_positions,
    ).astype(jnp.bfloat16)
    key_slice = apply_rotary(
        projection_all[:, QUERY_HEADS * HEAD_SIZE : (QUERY_HEADS + KEY_HEADS) * HEAD_SIZE].reshape(
            token_rows, KEY_HEADS, HEAD_SIZE
        ),
        token_positions,
    ).astype(jnp.bfloat16)
    value_slice = projection_all[:, (QUERY_HEADS + KEY_HEADS) * HEAD_SIZE :].astype(jnp.bfloat16)
    flattened_keys = key_slice.reshape(token_rows, KEY_HEADS * HEAD_SIZE)
    grouped = (
        query_slice.reshape(token_rows, KEY_HEADS, QUERY_PER_KEY, HEAD_SIZE)
        .transpose(1, 2, 0, 3)
        .reshape(KEY_HEADS, QUERY_PER_KEY * token_rows, HEAD_SIZE)
    )
    query_index = jnp.tile(tok_index, QUERY_PER_KEY)
    query_prompt = jnp.tile(prompt_of, QUERY_PER_KEY)
    key_value_piece = jnp.concatenate([flattened_keys, value_slice], axis=1)
    key_value = lax.all_to_all(
        jnp.broadcast_to(key_value_piece[None], (columns,) + key_value_piece.shape),
        "col",
        0,
        0,
        tiled=True,
    ).reshape(columns * token_rows, key_value_piece.shape[1])
    segments = (key_value[:, : KEY_HEADS * HEAD_SIZE], key_value[:, KEY_HEADS * HEAD_SIZE :])
    best_experts = jnp.full((KEY_HEADS, QUERY_PER_KEY * token_rows), -1e30, jnp.float32)
    segment_length = segments[0].shape[0]
    key_lines = segments[0].reshape(segment_length, KEY_HEADS, HEAD_SIZE).transpose(1, 0, 2)
    value_lines = segments[1].reshape(segment_length, KEY_HEADS, HEAD_SIZE).transpose(1, 0, 2)
    key_index = jnp.arange(segment_length, dtype=jnp.int32)
    key_prompt = prompt_layout(lengths_row, key_index)[0]
    allowed = (key_prompt[None, :] == query_prompt[:, None]) & (
        key_index[None, :] <= query_index[:, None]
    )
    scores = jnp.einsum(
        "hqd,hkd->hqk", grouped, key_lines, preferred_element_type=jnp.float32
    ) * HEAD_SIZE ** (-0.5)
    masked = jnp.where(allowed[None], scores, -1e30)
    fresh = jnp.maximum(best_experts, jnp.max(masked, axis=-1))
    weights = jnp.where(allowed[None], jnp.exp(scores - fresh[..., None]), 0.0)
    running_new = jnp.sum(weights, axis=-1)
    accum_new = jnp.einsum(
        "hqk,hkd->hqd",
        weights.astype(jnp.bfloat16),
        value_lines,
        preferred_element_type=jnp.float32,
    )
    mixed_output = accum_new / running_new[..., None]
    attention_result = (
        mixed_output.reshape(KEY_HEADS, QUERY_PER_KEY, token_rows, HEAD_SIZE)
        .transpose(2, 0, 1, 3)
        .reshape(token_rows, QUERY_HEADS * HEAD_SIZE)
        .astype(jnp.bfloat16)
    )
    projected_rows = times_halves(attention_result, out_halves)
    projected_rows = projected_rows + adapter_scale * adapter_change(
        attention_result, within_prompt, output_down_map, output_up_map
    )
    residual = (hidden_input.astype(jnp.float32) + projected_rows).astype(jnp.bfloat16)
    normed_two = rms_scaled(residual, expert_norm_gain)
    logits = jnp.dot(normed_two, router, preferred_element_type=jnp.float32)
    squashed = jax.nn.sigmoid(jnp.take_along_axis(logits, routes, axis=1))
    mixing = squashed / jnp.sum(squashed, axis=1, keepdims=True)
    expert_total = router.shape[1]
    local_experts = expert_gate_weight.shape[0]
    flat_routes = routes.reshape(-1)
    slots = route_slots(flat_routes, expert_total)
    slot_total = expert_total * CAP
    route_id = (flat_routes * CAP + slots).reshape(token_rows, routes.shape[1])
    matches = route_id[:, :, None] == jnp.arange(slot_total, dtype=jnp.int32)[None, None, :]
    picks = jnp.sum(matches.astype(jnp.float32), axis=1)
    dispatch_rows = jnp.dot(
        picks.T.astype(jnp.bfloat16), normed_two, preferred_element_type=jnp.float32
    ).astype(jnp.bfloat16)
    sending = dispatch_rows.reshape(columns, local_experts, CAP, model_width)
    arrived = lax.all_to_all(sending, "col", split_axis=0, concat_axis=0, tiled=True)
    gate_vals = jnp.einsum(
        "sjcd,jdf->sjcf", arrived, expert_gate_weight, preferred_element_type=jnp.float32
    )
    up_vals = jnp.einsum(
        "sjcd,jdf->sjcf", arrived, expert_up_weight, preferred_element_type=jnp.float32
    )
    hidden_vals = (jnp.maximum(gate_vals, 0.0) * up_vals).astype(jnp.bfloat16)
    answered = jnp.einsum(
        "sjcf,jfd->sjcd", hidden_vals, expert_down_weight, preferred_element_type=jnp.float32
    ).astype(jnp.bfloat16)
    returned = lax.all_to_all(answered, "col", split_axis=0, concat_axis=0, tiled=True)
    returned_rows = returned.reshape(slot_total, model_width)
    mix_matrix = jnp.sum(jnp.where(matches, mixing[:, :, None], 0.0), axis=1)
    mix_high = mix_matrix.astype(jnp.bfloat16)
    mix_low = (mix_matrix - mix_high.astype(jnp.float32)).astype(jnp.bfloat16)
    combined = jnp.dot(mix_high, returned_rows, preferred_element_type=jnp.float32) + jnp.dot(
        mix_low, returned_rows, preferred_element_type=jnp.float32
    )
    return (residual.astype(jnp.float32) + combined).astype(jnp.bfloat16)


def solution(mesh):
    placed = (
        P(("row", "col"), None),
        P(),
        P(),
        P(("row", "col"), None),
        P(),
        P(),
        P("row", "col"),
        P("row", "col"),
        P(),
        P("col", None, None),
        P("col", None, None),
        P("col", None, None),
        P("col", None, None),
        P("col", None, None),
        P("col", None, None),
        P("col", None, None),
    )
    return jax.shard_map(
        local, mesh=mesh, in_specs=placed, out_specs=P(("row", "col"), None), check_vma=False
    )
```

```python
import jax
import jax.numpy as jnp
from jax import lax
from jax.sharding import PartitionSpec as P

QUERY_HEADS = 12
KEY_HEADS = 2
HEAD_SIZE = 128
QUERY_PER_KEY = 6
CAP = 40


norm_eps = 1e-06
rope_base = 1000000.0
adapter_scale = 0.5


def rms_scaled(value_tensor, norm_gain):
    widened = value_tensor.astype(jnp.float32)
    inverse = lax.rsqrt(jnp.mean(widened * widened, axis=-1, keepdims=True) + norm_eps)
    return (widened * inverse * norm_gain.astype(jnp.float32)).astype(jnp.bfloat16)


def prompt_layout(lengths_row, tok_index):
    prompt_ends = jnp.cumsum(lengths_row)
    starts = prompt_ends - lengths_row
    prompt_of = jnp.sum((tok_index[:, None] >= prompt_ends[None, :]).astype(jnp.int32), axis=1)
    within_prompt = prompt_of[:, None] == jnp.arange(lengths_row.shape[0], dtype=jnp.int32)[None, :]
    token_positions = tok_index - jnp.sum(jnp.where(within_prompt, starts[None, :], 0), axis=1)
    return (prompt_of, within_prompt, token_positions)


def apply_rotary(value_tensor, token_positions):
    half_width = value_tensor.shape[-1] // 2
    frequency = rope_base ** (
        -2.0 * jnp.arange(half_width, dtype=jnp.float32) / value_tensor.shape[-1]
    )
    angles = token_positions.astype(jnp.float32)[:, None] * frequency[None, :]
    cosine = jnp.cos(angles)[:, None, :]
    sine_part = jnp.sin(angles)[:, None, :]
    front_half = value_tensor[..., :half_width]
    back_half = value_tensor[..., half_width:]
    return jnp.concatenate(
        [front_half * cosine - back_half * sine_part, back_half * cosine + front_half * sine_part],
        axis=-1,
    )


def adapter_change(inputs, within_prompt, downs, ups):
    low_rank = jnp.einsum("nk,prk->npr", inputs, downs, preferred_element_type=jnp.float32)
    low_rank = jnp.where(within_prompt[:, :, None], low_rank, 0.0).astype(jnp.bfloat16)
    return jnp.einsum("npr,pro->no", low_rank, ups, preferred_element_type=jnp.float32)


def route_slots(flat_routes, expert_total):
    marks = (flat_routes[:, None] == jnp.arange(expert_total, dtype=jnp.int32)[None, :]).astype(
        jnp.int32
    )
    before = jnp.cumsum(marks, axis=0) - marks
    return jnp.sum(before * marks, axis=1)


def local(
    hidden_input,
    lengths,
    prompt_adapter,
    routes,
    attention_norm_gain,
    expert_norm_gain,
    projection_weight,
    output_weight,
    router,
    adapter_projection_down,
    adapter_projection_up,
    adapter_output_down,
    adapter_output_up,
    expert_gate_weight,
    expert_up_weight,
    expert_down_weight,
):
    token_rows = hidden_input.shape[0]
    model_width = hidden_input.shape[1]
    columns = lax.axis_size("col")
    row_index = lax.axis_index("row")
    col_index = lax.axis_index("col")
    lengths_row = lax.dynamic_index_in_dim(lengths, row_index, 0, keepdims=False)
    adapter_row = lax.dynamic_index_in_dim(prompt_adapter, row_index, 0, keepdims=False)
    tok_index = col_index * token_rows + jnp.arange(token_rows, dtype=jnp.int32)
    prompt_of, within_prompt, token_positions = prompt_layout(lengths_row, tok_index)
    local_adapters = adapter_projection_down.shape[0]
    owner_column = adapter_row // local_adapters
    nearby_slot = adapter_row % local_adapters
    owned_here = (owner_column == col_index)[:, None, None]
    tables = (adapter_projection_down, adapter_projection_up, adapter_output_down, adapter_output_up)
    picked = jnp.concatenate(
        [
            jnp.where(owned_here, jnp.take(table, nearby_slot, axis=0), jnp.zeros((), table.dtype))
            for table in tables
        ],
        axis=-1,
    )
    picked_shape = picked.shape
    lane = 128
    chunks = picked.reshape(columns, -1, lane)
    blocks = (projection_weight, output_weight)
    flat_blocks = [block.reshape(-1, lane) for block in blocks]
    sizes = [chunks.shape[1]] + [flat.shape[0] for flat in flat_blocks]
    starts = [sum(sizes[:i]) for i in range(len(sizes) + 1)]
    bundle = jnp.concatenate(
        [chunks] + [jnp.broadcast_to(flat[None], (columns,) + flat.shape) for flat in flat_blocks],
        axis=1,
    )
    bundle = lax.all_to_all(bundle, "col", 0, 0, tiled=True)
    received = bundle[:, starts[0] : starts[1]]
    slabs = []
    for i, block in enumerate(blocks):
        rows_here, cols_here = block.shape
        piece = bundle[:, starts[i + 1] : starts[i + 2]].reshape(columns, rows_here, cols_here)
        slabs.append(piece.transpose(1, 0, 2).reshape(rows_here, columns * cols_here))
    reduced = jnp.sum(received.astype(jnp.float32), axis=0).astype(jnp.bfloat16)
    spread = lax.all_to_all(
        jnp.broadcast_to(reduced[None], (columns,) + reduced.shape), "col", 0, 0, tiled=True
    )
    core_index = col_index % 2
    partner = [(c, c ^ 1) for c in range(columns)]

    def gather_halves(slab):
        half = slab.shape[1] // 2
        own = lax.dynamic_slice_in_dim(slab, core_index * half, half, axis=1)
        own = lax.all_gather(own, "row", axis=0, tiled=True)
        other = lax.ppermute(own, "col", partner)
        return own, other

    def times_halves(inputs, halves):
        own, other = halves
        half = own.shape[1]
        placed = jnp.zeros((inputs.shape[0], 2 * half), jnp.float32)
        placed = lax.dynamic_update_slice_in_dim(
            placed, jnp.dot(inputs, own, preferred_element_type=jnp.float32), core_index * half, 1
        )
        return lax.dynamic_update_slice_in_dim(
            placed,
            jnp.dot(inputs, other, preferred_element_type=jnp.float32),
            (1 - core_index) * half,
            1,
        )

    qkv_halves = gather_halves(slabs[0])
    out_halves = gather_halves(slabs[1])
    maps = spread.reshape(picked_shape)
    widths = [table.shape[-1] for table in tables]
    bounds = [sum(widths[:i]) for i in range(len(widths) + 1)]
    projection_down_map, projection_up_map, output_down_map, output_up_map = [
        maps[..., bounds[i] : bounds[i + 1]] for i in range(len(tables))
    ]
    normalized = rms_scaled(hidden_input, attention_norm_gain)
    projection_all = times_halves(normalized, qkv_halves)
    projection_all = projection_all + adapter_scale * adapter_change(
        normalized, within_prompt, projection_down_map, projection_up_map
    )
    query_slice = apply_rotary(
        projection_all[:, : QUERY_HEADS * HEAD_SIZE].reshape(token_rows, QUERY_HEADS, HEAD_SIZE),
        token_positions,
    ).astype(jnp.bfloat16)
    key_slice = apply_rotary(
        projection_all[:, QUERY_HEADS * HEAD_SIZE : (QUERY_HEADS + KEY_HEADS) * HEAD_SIZE].reshape(
            token_rows, KEY_HEADS, HEAD_SIZE
        ),
        token_positions,
    ).astype(jnp.bfloat16)
    value_slice = projection_all[:, (QUERY_HEADS + KEY_HEADS) * HEAD_SIZE :].astype(jnp.bfloat16)
    flattened_keys = key_slice.reshape(token_rows, KEY_HEADS * HEAD_SIZE)
    grouped = (
        query_slice.reshape(token_rows, KEY_HEADS, QUERY_PER_KEY, HEAD_SIZE)
        .transpose(1, 2, 0, 3)
        .reshape(KEY_HEADS, QUERY_PER_KEY * token_rows, HEAD_SIZE)
    )
    query_index = jnp.tile(tok_index, QUERY_PER_KEY)
    query_prompt = jnp.tile(prompt_of, QUERY_PER_KEY)
    key_value_piece = jnp.concatenate([flattened_keys, value_slice], axis=1)
    key_value = lax.all_to_all(
        jnp.broadcast_to(key_value_piece[None], (columns,) + key_value_piece.shape),
        "col",
        0,
        0,
        tiled=True,
    ).reshape(columns * token_rows, key_value_piece.shape[1])
    segments = (key_value[:, : KEY_HEADS * HEAD_SIZE], key_value[:, KEY_HEADS * HEAD_SIZE :])
    best_experts = jnp.full((KEY_HEADS, QUERY_PER_KEY * token_rows), -1e30, jnp.float32)
    segment_length = segments[0].shape[0]
    key_lines = segments[0].reshape(segment_length, KEY_HEADS, HEAD_SIZE).transpose(1, 0, 2)
    value_lines = segments[1].reshape(segment_length, KEY_HEADS, HEAD_SIZE).transpose(1, 0, 2)
    key_index = jnp.arange(segment_length, dtype=jnp.int32)
    key_prompt = prompt_layout(lengths_row, key_index)[0]
    allowed = (key_prompt[None, :] == query_prompt[:, None]) & (
        key_index[None, :] <= query_index[:, None]
    )
    scores = jnp.einsum(
        "hqd,hkd->hqk", grouped, key_lines, preferred_element_type=jnp.float32
    ) * HEAD_SIZE ** (-0.5)
    masked = jnp.where(allowed[None], scores, -1e30)
    fresh = jnp.maximum(best_experts, jnp.max(masked, axis=-1))
    weights = jnp.where(allowed[None], jnp.exp(scores - fresh[..., None]), 0.0)
    running_new = jnp.sum(weights, axis=-1)
    accum_new = jnp.einsum(
        "hqk,hkd->hqd",
        weights.astype(jnp.bfloat16),
        value_lines,
        preferred_element_type=jnp.float32,
    )
    mixed_output = accum_new / running_new[..., None]
    attention_result = (
        mixed_output.reshape(KEY_HEADS, QUERY_PER_KEY, token_rows, HEAD_SIZE)
        .transpose(2, 0, 1, 3)
        .reshape(token_rows, QUERY_HEADS * HEAD_SIZE)
        .astype(jnp.bfloat16)
    )
    projected_rows = times_halves(attention_result, out_halves)
    projected_rows = projected_rows + adapter_scale * adapter_change(
        attention_result, within_prompt, output_down_map, output_up_map
    )
    residual = (hidden_input.astype(jnp.float32) + projected_rows).astype(jnp.bfloat16)
    normed_two = rms_scaled(residual, expert_norm_gain)
    logits = jnp.dot(normed_two, router, preferred_element_type=jnp.float32)
    squashed = jax.nn.sigmoid(jnp.take_along_axis(logits, routes, axis=1))
    mixing = squashed / jnp.sum(squashed, axis=1, keepdims=True)
    expert_total = router.shape[1]
    local_experts = expert_gate_weight.shape[0]
    flat_routes = routes.reshape(-1)
    slots = route_slots(flat_routes, expert_total)
    slot_total = expert_total * CAP
    route_id = (flat_routes * CAP + slots).reshape(token_rows, routes.shape[1])
    matches = route_id[:, :, None] == jnp.arange(slot_total, dtype=jnp.int32)[None, None, :]
    picks = jnp.sum(matches.astype(jnp.float32), axis=1)
    dispatch_rows = jnp.dot(
        picks.T.astype(jnp.bfloat16), normed_two, preferred_element_type=jnp.float32
    ).astype(jnp.bfloat16)
    sending = dispatch_rows.reshape(columns, local_experts, CAP, model_width)
    arrived = lax.all_to_all(sending, "col", split_axis=0, concat_axis=0, tiled=True)
    gate_vals = jnp.einsum(
        "sjcd,jdf->sjcf", arrived, expert_gate_weight, preferred_element_type=jnp.float32
    )
    up_vals = jnp.einsum(
        "sjcd,jdf->sjcf", arrived, expert_up_weight, preferred_element_type=jnp.float32
    )
    hidden_vals = (jnp.maximum(gate_vals, 0.0) * up_vals).astype(jnp.bfloat16)
    answered = jnp.einsum(
        "sjcf,jfd->sjcd", hidden_vals, expert_down_weight, preferred_element_type=jnp.float32
    ).astype(jnp.bfloat16)
    returned = lax.all_to_all(answered, "col", split_axis=0, concat_axis=0, tiled=True)
    returned_rows = returned.reshape(slot_total, model_width)
    mix_matrix = jnp.sum(jnp.where(matches, mixing[:, :, None], 0.0), axis=1)
    mix_high = mix_matrix.astype(jnp.bfloat16)
    mix_low = (mix_matrix - mix_high.astype(jnp.float32)).astype(jnp.bfloat16)
    combined = jnp.dot(mix_high, returned_rows, preferred_element_type=jnp.float32) + jnp.dot(
        mix_low, returned_rows, preferred_element_type=jnp.float32
    )
    return (residual.astype(jnp.float32) + combined).astype(jnp.bfloat16)


def solution(mesh):
    placed = (
        P(("row", "col"), None),
        P(),
        P(),
        P(("row", "col"), None),
        P(),
        P(),
        P("row", "col"),
        P("row", "col"),
        P(),
        P("col", None, None),
        P("col", None, None),
        P("col", None, None),
        P("col", None, None),
        P("col", None, None),
        P("col", None, None),
        P("col", None, None),
    )
    return jax.shard_map(
        local, mesh=mesh, in_specs=placed, out_specs=P(("row", "col"), None), check_vma=False
    )
```

```python
import jax
import jax.numpy as jnp
from jax import lax
from jax.sharding import PartitionSpec as P

QUERY_HEADS = 12
KEY_HEADS = 2
HEAD_SIZE = 128
QUERY_PER_KEY = 6
CAP = 40


norm_eps = 1e-06
rope_base = 1000000.0
adapter_scale = 0.5


def rms_scaled(value_tensor, norm_gain):
    widened = value_tensor.astype(jnp.float32)
    inverse = lax.rsqrt(jnp.mean(widened * widened, axis=-1, keepdims=True) + norm_eps)
    return (widened * inverse * norm_gain.astype(jnp.float32)).astype(jnp.bfloat16)


def prompt_layout(lengths_row, tok_index):
    prompt_ends = jnp.cumsum(lengths_row)
    starts = prompt_ends - lengths_row
    prompt_of = jnp.sum((tok_index[:, None] >= prompt_ends[None, :]).astype(jnp.int32), axis=1)
    within_prompt = prompt_of[:, None] == jnp.arange(lengths_row.shape[0], dtype=jnp.int32)[None, :]
    token_positions = tok_index - jnp.sum(jnp.where(within_prompt, starts[None, :], 0), axis=1)
    return (prompt_of, within_prompt, token_positions)


def apply_rotary(value_tensor, token_positions):
    half_width = value_tensor.shape[-1] // 2
    frequency = rope_base ** (
        -2.0 * jnp.arange(half_width, dtype=jnp.float32) / value_tensor.shape[-1]
    )
    angles = token_positions.astype(jnp.float32)[:, None] * frequency[None, :]
    cosine = jnp.cos(angles)[:, None, :]
    sine_part = jnp.sin(angles)[:, None, :]
    front_half = value_tensor[..., :half_width]
    back_half = value_tensor[..., half_width:]
    return jnp.concatenate(
        [front_half * cosine - back_half * sine_part, back_half * cosine + front_half * sine_part],
        axis=-1,
    )


def adapter_change(inputs, within_prompt, downs, ups):
    low_rank = jnp.einsum("nk,prk->npr", inputs, downs, preferred_element_type=jnp.float32)
    low_rank = jnp.where(within_prompt[:, :, None], low_rank, 0.0).astype(jnp.bfloat16)
    return jnp.einsum("npr,pro->no", low_rank, ups, preferred_element_type=jnp.float32)


def route_slots(flat_routes, expert_total):
    marks = (flat_routes[:, None] == jnp.arange(expert_total, dtype=jnp.int32)[None, :]).astype(
        jnp.int32
    )
    before = jnp.cumsum(marks, axis=0) - marks
    return jnp.sum(before * marks, axis=1)


def local(
    hidden_input,
    lengths,
    prompt_adapter,
    routes,
    attention_norm_gain,
    expert_norm_gain,
    projection_weight,
    output_weight,
    router,
    adapter_projection_down,
    adapter_projection_up,
    adapter_output_down,
    adapter_output_up,
    expert_gate_weight,
    expert_up_weight,
    expert_down_weight,
):
    token_rows = hidden_input.shape[0]
    model_width = hidden_input.shape[1]
    columns = lax.axis_size("col")
    row_index = lax.axis_index("row")
    col_index = lax.axis_index("col")
    lengths_row = lax.dynamic_index_in_dim(lengths, row_index, 0, keepdims=False)
    adapter_row = lax.dynamic_index_in_dim(prompt_adapter, row_index, 0, keepdims=False)
    tok_index = col_index * token_rows + jnp.arange(token_rows, dtype=jnp.int32)
    prompt_of, within_prompt, token_positions = prompt_layout(lengths_row, tok_index)
    local_adapters = adapter_projection_down.shape[0]
    owner_column = adapter_row // local_adapters
    nearby_slot = adapter_row % local_adapters
    owned_here = (owner_column == col_index)[:, None, None]
    tables = (adapter_projection_down, adapter_projection_up, adapter_output_down, adapter_output_up)
    picked = jnp.concatenate(
        [
            jnp.where(owned_here, jnp.take(table, nearby_slot, axis=0), jnp.zeros((), table.dtype))
            for table in tables
        ],
        axis=-1,
    )
    picked_shape = picked.shape
    lane = 128
    chunks = picked.reshape(columns, -1, lane)
    blocks = (projection_weight, output_weight)
    flat_blocks = [block.reshape(-1, lane) for block in blocks]
    sizes = [chunks.shape[1]] + [flat.shape[0] for flat in flat_blocks]
    starts = [sum(sizes[:i]) for i in range(len(sizes) + 1)]
    received = lax.all_to_all(chunks, "col", 0, 0, tiled=True)
    reduced = jnp.sum(received.astype(jnp.float32), axis=0).astype(jnp.bfloat16)
    bundle = jnp.concatenate(
        [jnp.broadcast_to(reduced[None], (columns,) + reduced.shape)]
        + [jnp.broadcast_to(flat[None], (columns,) + flat.shape) for flat in flat_blocks],
        axis=1,
    )
    bundle = lax.all_to_all(bundle, "col", 0, 0, tiled=True)
    spread = bundle[:, starts[0] : starts[1]]
    slabs = []
    for i, block in enumerate(blocks):
        rows_here, cols_here = block.shape
        piece = bundle[:, starts[i + 1] : starts[i + 2]].reshape(columns, rows_here, cols_here)
        slabs.append(piece.transpose(1, 0, 2).reshape(rows_here, columns * cols_here))
    core_index = col_index % 2
    partner = [(c, c ^ 1) for c in range(columns)]

    def gather_halves(slab):
        half = slab.shape[1] // 2
        own = lax.dynamic_slice_in_dim(slab, core_index * half, half, axis=1)
        own = lax.all_gather(own, "row", axis=0, tiled=True)
        other = lax.ppermute(own, "col", partner)
        return own, other

    def times_halves(inputs, halves):
        own, other = halves
        half = own.shape[1]
        placed = jnp.zeros((inputs.shape[0], 2 * half), jnp.float32)
        placed = lax.dynamic_update_slice_in_dim(
            placed, jnp.dot(inputs, own, preferred_element_type=jnp.float32), core_index * half, 1
        )
        return lax.dynamic_update_slice_in_dim(
            placed,
            jnp.dot(inputs, other, preferred_element_type=jnp.float32),
            (1 - core_index) * half,
            1,
        )

    qkv_halves = gather_halves(slabs[0])
    out_halves = gather_halves(slabs[1])
    maps = spread.reshape(picked_shape)
    widths = [table.shape[-1] for table in tables]
    bounds = [sum(widths[:i]) for i in range(len(widths) + 1)]
    projection_down_map, projection_up_map, output_down_map, output_up_map = [
        maps[..., bounds[i] : bounds[i + 1]] for i in range(len(tables))
    ]
    normalized = rms_scaled(hidden_input, attention_norm_gain)
    projection_all = times_halves(normalized, qkv_halves)
    projection_all = projection_all + adapter_scale * adapter_change(
        normalized, within_prompt, projection_down_map, projection_up_map
    )
    query_slice = apply_rotary(
        projection_all[:, : QUERY_HEADS * HEAD_SIZE].reshape(token_rows, QUERY_HEADS, HEAD_SIZE),
        token_positions,
    ).astype(jnp.bfloat16)
    key_slice = apply_rotary(
        projection_all[:, QUERY_HEADS * HEAD_SIZE : (QUERY_HEADS + KEY_HEADS) * HEAD_SIZE].reshape(
            token_rows, KEY_HEADS, HEAD_SIZE
        ),
        token_positions,
    ).astype(jnp.bfloat16)
    value_slice = projection_all[:, (QUERY_HEADS + KEY_HEADS) * HEAD_SIZE :].astype(jnp.bfloat16)
    flattened_keys = key_slice.reshape(token_rows, KEY_HEADS * HEAD_SIZE)
    grouped = (
        query_slice.reshape(token_rows, KEY_HEADS, QUERY_PER_KEY, HEAD_SIZE)
        .transpose(1, 2, 0, 3)
        .reshape(KEY_HEADS, QUERY_PER_KEY * token_rows, HEAD_SIZE)
    )
    query_index = jnp.tile(tok_index, QUERY_PER_KEY)
    query_prompt = jnp.tile(prompt_of, QUERY_PER_KEY)
    key_value_piece = jnp.concatenate([flattened_keys, value_slice], axis=1)
    key_value = lax.all_to_all(
        jnp.broadcast_to(key_value_piece[None], (columns,) + key_value_piece.shape),
        "col",
        0,
        0,
        tiled=True,
    ).reshape(columns * token_rows, key_value_piece.shape[1])
    segments = (key_value[:, : KEY_HEADS * HEAD_SIZE], key_value[:, KEY_HEADS * HEAD_SIZE :])
    best_experts = jnp.full((KEY_HEADS, QUERY_PER_KEY * token_rows), -1e30, jnp.float32)
    segment_length = segments[0].shape[0]
    key_lines = segments[0].reshape(segment_length, KEY_HEADS, HEAD_SIZE).transpose(1, 0, 2)
    value_lines = segments[1].reshape(segment_length, KEY_HEADS, HEAD_SIZE).transpose(1, 0, 2)
    key_index = jnp.arange(segment_length, dtype=jnp.int32)
    key_prompt = prompt_layout(lengths_row, key_index)[0]
    allowed = (key_prompt[None, :] == query_prompt[:, None]) & (
        key_index[None, :] <= query_index[:, None]
    )
    scores = jnp.einsum(
        "hqd,hkd->hqk", grouped, key_lines, preferred_element_type=jnp.float32
    ) * HEAD_SIZE ** (-0.5)
    masked = jnp.where(allowed[None], scores, -1e30)
    fresh = jnp.maximum(best_experts, jnp.max(masked, axis=-1))
    weights = jnp.where(allowed[None], jnp.exp(scores - fresh[..., None]), 0.0)
    running_new = jnp.sum(weights, axis=-1)
    accum_new = jnp.einsum(
        "hqk,hkd->hqd",
        weights.astype(jnp.bfloat16),
        value_lines,
        preferred_element_type=jnp.float32,
    )
    mixed_output = accum_new / running_new[..., None]
    attention_result = (
        mixed_output.reshape(KEY_HEADS, QUERY_PER_KEY, token_rows, HEAD_SIZE)
        .transpose(2, 0, 1, 3)
        .reshape(token_rows, QUERY_HEADS * HEAD_SIZE)
        .astype(jnp.bfloat16)
    )
    projected_rows = times_halves(attention_result, out_halves)
    projected_rows = projected_rows + adapter_scale * adapter_change(
        attention_result, within_prompt, output_down_map, output_up_map
    )
    residual = (hidden_input.astype(jnp.float32) + projected_rows).astype(jnp.bfloat16)
    normed_two = rms_scaled(residual, expert_norm_gain)
    logits = jnp.dot(normed_two, router, preferred_element_type=jnp.float32)
    squashed = jax.nn.sigmoid(jnp.take_along_axis(logits, routes, axis=1))
    mixing = squashed / jnp.sum(squashed, axis=1, keepdims=True)
    expert_total = router.shape[1]
    local_experts = expert_gate_weight.shape[0]
    flat_routes = routes.reshape(-1)
    slots = route_slots(flat_routes, expert_total)
    slot_total = expert_total * CAP
    route_id = (flat_routes * CAP + slots).reshape(token_rows, routes.shape[1])
    matches = route_id[:, :, None] == jnp.arange(slot_total, dtype=jnp.int32)[None, None, :]
    picks = jnp.sum(matches.astype(jnp.float32), axis=1)
    dispatch_rows = jnp.dot(
        picks.T.astype(jnp.bfloat16), normed_two, preferred_element_type=jnp.float32
    ).astype(jnp.bfloat16)
    sending = dispatch_rows.reshape(columns, local_experts, CAP, model_width)
    arrived = lax.all_to_all(sending, "col", split_axis=0, concat_axis=0, tiled=True)
    gate_vals = jnp.einsum(
        "sjcd,jdf->sjcf", arrived, expert_gate_weight, preferred_element_type=jnp.float32
    )
    up_vals = jnp.einsum(
        "sjcd,jdf->sjcf", arrived, expert_up_weight, preferred_element_type=jnp.float32
    )
    hidden_vals = (jnp.maximum(gate_vals, 0.0) * up_vals).astype(jnp.bfloat16)
    answered = jnp.einsum(
        "sjcf,jfd->sjcd", hidden_vals, expert_down_weight, preferred_element_type=jnp.float32
    ).astype(jnp.bfloat16)
    returned = lax.all_to_all(answered, "col", split_axis=0, concat_axis=0, tiled=True)
    returned_rows = returned.reshape(slot_total, model_width)
    mix_matrix = jnp.sum(jnp.where(matches, mixing[:, :, None], 0.0), axis=1)
    mix_high = mix_matrix.astype(jnp.bfloat16)
    mix_low = (mix_matrix - mix_high.astype(jnp.float32)).astype(jnp.bfloat16)
    combined = jnp.dot(mix_high, returned_rows, preferred_element_type=jnp.float32) + jnp.dot(
        mix_low, returned_rows, preferred_element_type=jnp.float32
    )
    return (residual.astype(jnp.float32) + combined).astype(jnp.bfloat16)


def solution(mesh):
    placed = (
        P(("row", "col"), None),
        P(),
        P(),
        P(("row", "col"), None),
        P(),
        P(),
        P("row", "col"),
        P("row", "col"),
        P(),
        P("col", None, None),
        P("col", None, None),
        P("col", None, None),
        P("col", None, None),
        P("col", None, None),
        P("col", None, None),
        P("col", None, None),
    )
    return jax.shard_map(
        local, mesh=mesh, in_specs=placed, out_specs=P(("row", "col"), None), check_vma=False
    )
```

```python
import jax
import jax.numpy as jnp
from jax import lax
from jax.sharding import PartitionSpec as P

QUERY_HEADS = 12
KEY_HEADS = 2
HEAD_SIZE = 128
QUERY_PER_KEY = 6
CAP = 40


norm_eps = 1e-06
rope_base = 1000000.0
adapter_scale = 0.5


def rms_scaled(value_tensor, norm_gain):
    widened = value_tensor.astype(jnp.float32)
    inverse = lax.rsqrt(jnp.mean(widened * widened, axis=-1, keepdims=True) + norm_eps)
    return (widened * inverse * norm_gain.astype(jnp.float32)).astype(jnp.bfloat16)


def prompt_layout(lengths_row, tok_index):
    prompt_ends = jnp.cumsum(lengths_row)
    starts = prompt_ends - lengths_row
    prompt_of = jnp.sum((tok_index[:, None] >= prompt_ends[None, :]).astype(jnp.int32), axis=1)
    within_prompt = prompt_of[:, None] == jnp.arange(lengths_row.shape[0], dtype=jnp.int32)[None, :]
    token_positions = tok_index - jnp.sum(jnp.where(within_prompt, starts[None, :], 0), axis=1)
    return (prompt_of, within_prompt, token_positions)


def apply_rotary(value_tensor, token_positions):
    half_width = value_tensor.shape[-1] // 2
    frequency = rope_base ** (
        -2.0 * jnp.arange(half_width, dtype=jnp.float32) / value_tensor.shape[-1]
    )
    angles = token_positions.astype(jnp.float32)[:, None] * frequency[None, :]
    cosine = jnp.cos(angles)[:, None, :]
    sine_part = jnp.sin(angles)[:, None, :]
    front_half = value_tensor[..., :half_width]
    back_half = value_tensor[..., half_width:]
    return jnp.concatenate(
        [front_half * cosine - back_half * sine_part, back_half * cosine + front_half * sine_part],
        axis=-1,
    )


def adapter_change(inputs, within_prompt, downs, ups):
    low_rank = jnp.einsum("nk,prk->npr", inputs, downs, preferred_element_type=jnp.float32)
    low_rank = jnp.where(within_prompt[:, :, None], low_rank, 0.0).astype(jnp.bfloat16)
    return jnp.einsum("npr,pro->no", low_rank, ups, preferred_element_type=jnp.float32)


def route_slots(flat_routes, expert_total):
    marks = (flat_routes[:, None] == jnp.arange(expert_total, dtype=jnp.int32)[None, :]).astype(
        jnp.int32
    )
    before = jnp.cumsum(marks, axis=0) - marks
    return jnp.sum(before * marks, axis=1)


def local(
    hidden_input,
    lengths,
    prompt_adapter,
    routes,
    attention_norm_gain,
    expert_norm_gain,
    projection_weight,
    output_weight,
    router,
    adapter_projection_down,
    adapter_projection_up,
    adapter_output_down,
    adapter_output_up,
    expert_gate_weight,
    expert_up_weight,
    expert_down_weight,
):
    token_rows = hidden_input.shape[0]
    model_width = hidden_input.shape[1]
    columns = lax.axis_size("col")
    row_index = lax.axis_index("row")
    col_index = lax.axis_index("col")
    lengths_row = lax.dynamic_index_in_dim(lengths, row_index, 0, keepdims=False)
    adapter_row = lax.dynamic_index_in_dim(prompt_adapter, row_index, 0, keepdims=False)
    tok_index = col_index * token_rows + jnp.arange(token_rows, dtype=jnp.int32)
    prompt_of, within_prompt, token_positions = prompt_layout(lengths_row, tok_index)
    local_adapters = adapter_projection_down.shape[0]
    owner_column = adapter_row // local_adapters
    nearby_slot = adapter_row % local_adapters
    owned_here = (owner_column == col_index)[:, None, None]
    tables = (adapter_projection_down, adapter_projection_up, adapter_output_down, adapter_output_up)
    picked = jnp.concatenate(
        [
            jnp.where(owned_here, jnp.take(table, nearby_slot, axis=0), jnp.zeros((), table.dtype))
            for table in tables
        ],
        axis=-1,
    )
    picked_shape = picked.shape
    lane = 128
    chunks = picked.reshape(columns, -1, lane)
    blocks = (projection_weight, output_weight)
    flat_blocks = [block.reshape(-1, lane) for block in blocks]
    sizes = [chunks.shape[1]] + [flat.shape[0] for flat in flat_blocks]
    starts = [sum(sizes[:i]) for i in range(len(sizes) + 1)]
    bundle = jnp.concatenate(
        [chunks] + [jnp.broadcast_to(flat[None], (columns,) + flat.shape) for flat in flat_blocks],
        axis=1,
    )
    bundle = lax.all_to_all(bundle, "col", 0, 0, tiled=True)
    received = bundle[:, starts[0] : starts[1]]
    slabs = []
    for i, block in enumerate(blocks):
        rows_here, cols_here = block.shape
        piece = bundle[:, starts[i + 1] : starts[i + 2]].reshape(columns, rows_here, cols_here)
        slabs.append(piece.transpose(1, 0, 2).reshape(rows_here, columns * cols_here))
    reduced = jnp.sum(received.astype(jnp.float32), axis=0).astype(jnp.bfloat16)
    spread = lax.all_to_all(
        jnp.broadcast_to(reduced[None], (columns,) + reduced.shape), "col", 0, 0, tiled=True
    )
    core_index = col_index % 2
    partner = [(c, c ^ 1) for c in range(columns)]

    def gather_halves(slab):
        half = slab.shape[1] // 2
        own = lax.dynamic_slice_in_dim(slab, core_index * half, half, axis=1)
        own = lax.all_gather(own, "row", axis=0, tiled=True)
        other = lax.ppermute(own, "col", partner)
        return own, other

    def times_halves(inputs, halves):
        own, other = halves
        half = own.shape[1]
        placed = jnp.zeros((inputs.shape[0], 2 * half), jnp.float32)
        placed = lax.dynamic_update_slice_in_dim(
            placed, jnp.dot(inputs, own, preferred_element_type=jnp.float32), core_index * half, 1
        )
        return lax.dynamic_update_slice_in_dim(
            placed,
            jnp.dot(inputs, other, preferred_element_type=jnp.float32),
            (1 - core_index) * half,
            1,
        )

    qkv_halves = gather_halves(slabs[0])
    out_halves = gather_halves(slabs[1])
    maps = spread.reshape(picked_shape)
    widths = [table.shape[-1] for table in tables]
    bounds = [sum(widths[:i]) for i in range(len(widths) + 1)]
    projection_down_map, projection_up_map, output_down_map, output_up_map = [
        maps[..., bounds[i] : bounds[i + 1]] for i in range(len(tables))
    ]
    normalized = rms_scaled(hidden_input, attention_norm_gain)
    projection_all = times_halves(normalized, qkv_halves)
    projection_all = projection_all + adapter_scale * adapter_change(
        normalized, within_prompt, projection_down_map, projection_up_map
    )
    query_slice = apply_rotary(
        projection_all[:, : QUERY_HEADS * HEAD_SIZE].reshape(token_rows, QUERY_HEADS, HEAD_SIZE),
        token_positions,
    ).astype(jnp.bfloat16)
    key_slice = apply_rotary(
        projection_all[:, QUERY_HEADS * HEAD_SIZE : (QUERY_HEADS + KEY_HEADS) * HEAD_SIZE].reshape(
            token_rows, KEY_HEADS, HEAD_SIZE
        ),
        token_positions,
    ).astype(jnp.bfloat16)
    value_slice = projection_all[:, (QUERY_HEADS + KEY_HEADS) * HEAD_SIZE :].astype(jnp.bfloat16)
    flattened_keys = key_slice.reshape(token_rows, KEY_HEADS * HEAD_SIZE)
    grouped = (
        query_slice.reshape(token_rows, KEY_HEADS, QUERY_PER_KEY, HEAD_SIZE)
        .transpose(1, 2, 0, 3)
        .reshape(KEY_HEADS, QUERY_PER_KEY * token_rows, HEAD_SIZE)
    )
    query_index = jnp.tile(tok_index, QUERY_PER_KEY)
    query_prompt = jnp.tile(prompt_of, QUERY_PER_KEY)
    key_value_piece = jnp.concatenate([flattened_keys, value_slice], axis=1)
    key_value = lax.all_to_all(
        jnp.broadcast_to(key_value_piece[None], (columns,) + key_value_piece.shape),
        "col",
        0,
        0,
        tiled=True,
    ).reshape(columns * token_rows, key_value_piece.shape[1])
    segments = (key_value[:, : KEY_HEADS * HEAD_SIZE], key_value[:, KEY_HEADS * HEAD_SIZE :])
    best_experts = jnp.full((KEY_HEADS, QUERY_PER_KEY * token_rows), -1e30, jnp.float32)
    segment_length = segments[0].shape[0]
    key_lines = segments[0].reshape(segment_length, KEY_HEADS, HEAD_SIZE).transpose(1, 0, 2)
    value_lines = segments[1].reshape(segment_length, KEY_HEADS, HEAD_SIZE).transpose(1, 0, 2)
    key_index = jnp.arange(segment_length, dtype=jnp.int32)
    key_prompt = prompt_layout(lengths_row, key_index)[0]
    allowed = (key_prompt[None, :] == query_prompt[:, None]) & (
        key_index[None, :] <= query_index[:, None]
    )
    scores = jnp.einsum(
        "hqd,hkd->hqk", grouped, key_lines, preferred_element_type=jnp.float32
    ) * HEAD_SIZE ** (-0.5)
    masked = jnp.where(allowed[None], scores, -1e30)
    fresh = jnp.maximum(best_experts, jnp.max(masked, axis=-1))
    weights = jnp.where(allowed[None], jnp.exp(scores - fresh[..., None]), 0.0)
    running_new = jnp.sum(weights, axis=-1)
    accum_new = jnp.einsum(
        "hqk,hkd->hqd",
        weights.astype(jnp.bfloat16),
        value_lines,
        preferred_element_type=jnp.float32,
    )
    mixed_output = accum_new / running_new[..., None]
    attention_result = (
        mixed_output.reshape(KEY_HEADS, QUERY_PER_KEY, token_rows, HEAD_SIZE)
        .transpose(2, 0, 1, 3)
        .reshape(token_rows, QUERY_HEADS * HEAD_SIZE)
        .astype(jnp.bfloat16)
    )
    projected_rows = times_halves(attention_result, out_halves)
    projected_rows = projected_rows + adapter_scale * adapter_change(
        attention_result, within_prompt, output_down_map, output_up_map
    )
    residual = (hidden_input.astype(jnp.float32) + projected_rows).astype(jnp.bfloat16)
    normed_two = rms_scaled(residual, expert_norm_gain)
    logits = jnp.dot(normed_two, router, preferred_element_type=jnp.float32)
    squashed = jax.nn.sigmoid(jnp.take_along_axis(logits, routes, axis=1))
    mixing = squashed / jnp.sum(squashed, axis=1, keepdims=True)
    expert_total = router.shape[1]
    local_experts = expert_gate_weight.shape[0]
    flat_routes = routes.reshape(-1)
    slots = route_slots(flat_routes, expert_total)
    slot_total = expert_total * CAP
    device_slots = local_experts * CAP
    shift_of = (flat_routes // local_experts - col_index) % columns
    route_id = (shift_of * device_slots + (flat_routes % local_experts) * CAP + slots).reshape(
        token_rows, routes.shape[1]
    )
    matches = route_id[:, :, None] == jnp.arange(slot_total, dtype=jnp.int32)[None, None, :]
    picks = jnp.sum(matches.astype(jnp.float32), axis=1)
    dispatch_rows = jnp.dot(
        picks.T.astype(jnp.bfloat16), normed_two, preferred_element_type=jnp.float32
    ).astype(jnp.bfloat16)
    sending = dispatch_rows.reshape(columns, local_experts, CAP, model_width)

    def exchange(pieces, direction):
        moved = [pieces[0]]
        for s in range(1, columns):
            pairs = [(c, (c + direction * s) % columns) for c in range(columns)]
            moved.append(lax.ppermute(pieces[s], "col", pairs))
        return jnp.stack(moved)

    arrived = exchange(sending, 1)
    gate_vals = jnp.einsum(
        "sjcd,jdf->sjcf", arrived, expert_gate_weight, preferred_element_type=jnp.float32
    )
    up_vals = jnp.einsum(
        "sjcd,jdf->sjcf", arrived, expert_up_weight, preferred_element_type=jnp.float32
    )
    hidden_vals = (jnp.maximum(gate_vals, 0.0) * up_vals).astype(jnp.bfloat16)
    answered = jnp.einsum(
        "sjcf,jfd->sjcd", hidden_vals, expert_down_weight, preferred_element_type=jnp.float32
    ).astype(jnp.bfloat16)
    returned = exchange(answered, -1)
    returned_rows = returned.reshape(slot_total, model_width)
    mix_matrix = jnp.sum(jnp.where(matches, mixing[:, :, None], 0.0), axis=1)
    mix_high = mix_matrix.astype(jnp.bfloat16)
    mix_low = (mix_matrix - mix_high.astype(jnp.float32)).astype(jnp.bfloat16)
    combined = jnp.dot(mix_high, returned_rows, preferred_element_type=jnp.float32) + jnp.dot(
        mix_low, returned_rows, preferred_element_type=jnp.float32
    )
    return (residual.astype(jnp.float32) + combined).astype(jnp.bfloat16)


def solution(mesh):
    placed = (
        P(("row", "col"), None),
        P(),
        P(),
        P(("row", "col"), None),
        P(),
        P(),
        P("row", "col"),
        P("row", "col"),
        P(),
        P("col", None, None),
        P("col", None, None),
        P("col", None, None),
        P("col", None, None),
        P("col", None, None),
        P("col", None, None),
        P("col", None, None),
    )
    return jax.shard_map(
        local, mesh=mesh, in_specs=placed, out_specs=P(("row", "col"), None), check_vma=False
    )
```

```python
import jax
import jax.numpy as jnp
from jax import lax
from jax.sharding import PartitionSpec as P

QUERY_HEADS = 12
KEY_HEADS = 2
HEAD_SIZE = 128
QUERY_PER_KEY = 6
CAP = 40
LONGEST_PROMPT = 1536


norm_eps = 1e-06
rope_base = 1000000.0
adapter_scale = 0.5


def rms_scaled(value_tensor, norm_gain):
    widened = value_tensor.astype(jnp.float32)
    inverse = lax.rsqrt(jnp.mean(widened * widened, axis=-1, keepdims=True) + norm_eps)
    return (widened * inverse * norm_gain.astype(jnp.float32)).astype(jnp.bfloat16)


def prompt_layout(lengths_row, tok_index):
    prompt_ends = jnp.cumsum(lengths_row)
    starts = prompt_ends - lengths_row
    prompt_of = jnp.sum((tok_index[:, None] >= prompt_ends[None, :]).astype(jnp.int32), axis=1)
    within_prompt = prompt_of[:, None] == jnp.arange(lengths_row.shape[0], dtype=jnp.int32)[None, :]
    token_positions = tok_index - jnp.sum(jnp.where(within_prompt, starts[None, :], 0), axis=1)
    return (prompt_of, within_prompt, token_positions)


def apply_rotary(value_tensor, token_positions):
    half_width = value_tensor.shape[-1] // 2
    frequency = rope_base ** (
        -2.0 * jnp.arange(half_width, dtype=jnp.float32) / value_tensor.shape[-1]
    )
    angles = token_positions.astype(jnp.float32)[:, None] * frequency[None, :]
    cosine = jnp.cos(angles)[:, None, :]
    sine_part = jnp.sin(angles)[:, None, :]
    front_half = value_tensor[..., :half_width]
    back_half = value_tensor[..., half_width:]
    return jnp.concatenate(
        [front_half * cosine - back_half * sine_part, back_half * cosine + front_half * sine_part],
        axis=-1,
    )


def adapter_change(inputs, within_prompt, downs, ups):
    low_rank = jnp.einsum("nk,prk->npr", inputs, downs, preferred_element_type=jnp.float32)
    low_rank = jnp.where(within_prompt[:, :, None], low_rank, 0.0).astype(jnp.bfloat16)
    return jnp.einsum("npr,pro->no", low_rank, ups, preferred_element_type=jnp.float32)


def route_slots(flat_routes, expert_total):
    marks = (flat_routes[:, None] == jnp.arange(expert_total, dtype=jnp.int32)[None, :]).astype(
        jnp.int32
    )
    before = jnp.cumsum(marks, axis=0) - marks
    return jnp.sum(before * marks, axis=1)


def local(
    hidden_input,
    lengths,
    prompt_adapter,
    routes,
    attention_norm_gain,
    expert_norm_gain,
    projection_weight,
    output_weight,
    router,
    adapter_projection_down,
    adapter_projection_up,
    adapter_output_down,
    adapter_output_up,
    expert_gate_weight,
    expert_up_weight,
    expert_down_weight,
):
    token_rows = hidden_input.shape[0]
    model_width = hidden_input.shape[1]
    columns = lax.axis_size("col")
    row_index = lax.axis_index("row")
    col_index = lax.axis_index("col")
    lengths_row = lax.dynamic_index_in_dim(lengths, row_index, 0, keepdims=False)
    adapter_row = lax.dynamic_index_in_dim(prompt_adapter, row_index, 0, keepdims=False)
    tok_index = col_index * token_rows + jnp.arange(token_rows, dtype=jnp.int32)
    prompt_of, within_prompt, token_positions = prompt_layout(lengths_row, tok_index)
    local_adapters = adapter_projection_down.shape[0]
    owner_column = adapter_row // local_adapters
    nearby_slot = adapter_row % local_adapters
    owned_here = (owner_column == col_index)[:, None, None]
    tables = (adapter_projection_down, adapter_projection_up, adapter_output_down, adapter_output_up)
    picked = jnp.concatenate(
        [
            jnp.where(owned_here, jnp.take(table, nearby_slot, axis=0), jnp.zeros((), table.dtype))
            for table in tables
        ],
        axis=-1,
    )
    picked_shape = picked.shape
    lane = 128
    chunks = picked.reshape(columns, -1, lane)
    blocks = (projection_weight, output_weight)
    flat_blocks = [block.reshape(-1, lane) for block in blocks]
    sizes = [chunks.shape[1]] + [flat.shape[0] for flat in flat_blocks]
    starts = [sum(sizes[:i]) for i in range(len(sizes) + 1)]
    bundle = jnp.concatenate(
        [chunks] + [jnp.broadcast_to(flat[None], (columns,) + flat.shape) for flat in flat_blocks],
        axis=1,
    )
    bundle = lax.all_to_all(bundle, "col", 0, 0, tiled=True)
    received = bundle[:, starts[0] : starts[1]]
    slabs = []
    for i, block in enumerate(blocks):
        rows_here, cols_here = block.shape
        piece = bundle[:, starts[i + 1] : starts[i + 2]].reshape(columns, rows_here, cols_here)
        slabs.append(piece.transpose(1, 0, 2).reshape(rows_here, columns * cols_here))
    reduced = jnp.sum(received.astype(jnp.float32), axis=0).astype(jnp.bfloat16)
    spread = lax.all_to_all(
        jnp.broadcast_to(reduced[None], (columns,) + reduced.shape), "col", 0, 0, tiled=True
    )
    core_index = col_index % 2
    partner = [(c, c ^ 1) for c in range(columns)]

    def gather_halves(slab):
        half = slab.shape[1] // 2
        own = lax.dynamic_slice_in_dim(slab, core_index * half, half, axis=1)
        own = lax.all_gather(own, "row", axis=0, tiled=True)
        other = lax.ppermute(own, "col", partner)
        return own, other

    def times_halves(inputs, halves):
        own, other = halves
        half = own.shape[1]
        placed = jnp.zeros((inputs.shape[0], 2 * half), jnp.float32)
        placed = lax.dynamic_update_slice_in_dim(
            placed, jnp.dot(inputs, own, preferred_element_type=jnp.float32), core_index * half, 1
        )
        return lax.dynamic_update_slice_in_dim(
            placed,
            jnp.dot(inputs, other, preferred_element_type=jnp.float32),
            (1 - core_index) * half,
            1,
        )

    qkv_halves = gather_halves(slabs[0])
    out_halves = gather_halves(slabs[1])
    maps = spread.reshape(picked_shape)
    widths = [table.shape[-1] for table in tables]
    bounds = [sum(widths[:i]) for i in range(len(widths) + 1)]
    projection_down_map, projection_up_map, output_down_map, output_up_map = [
        maps[..., bounds[i] : bounds[i + 1]] for i in range(len(tables))
    ]
    normalized = rms_scaled(hidden_input, attention_norm_gain)
    projection_all = times_halves(normalized, qkv_halves)
    projection_all = projection_all + adapter_scale * adapter_change(
        normalized, within_prompt, projection_down_map, projection_up_map
    )
    query_slice = apply_rotary(
        projection_all[:, : QUERY_HEADS * HEAD_SIZE].reshape(token_rows, QUERY_HEADS, HEAD_SIZE),
        token_positions,
    ).astype(jnp.bfloat16)
    key_slice = apply_rotary(
        projection_all[:, QUERY_HEADS * HEAD_SIZE : (QUERY_HEADS + KEY_HEADS) * HEAD_SIZE].reshape(
            token_rows, KEY_HEADS, HEAD_SIZE
        ),
        token_positions,
    ).astype(jnp.bfloat16)
    value_slice = projection_all[:, (QUERY_HEADS + KEY_HEADS) * HEAD_SIZE :].astype(jnp.bfloat16)
    flattened_keys = key_slice.reshape(token_rows, KEY_HEADS * HEAD_SIZE)
    grouped = (
        query_slice.reshape(token_rows, KEY_HEADS, QUERY_PER_KEY, HEAD_SIZE)
        .transpose(1, 2, 0, 3)
        .reshape(KEY_HEADS, QUERY_PER_KEY * token_rows, HEAD_SIZE)
    )
    query_index = jnp.tile(tok_index, QUERY_PER_KEY)
    query_prompt = jnp.tile(prompt_of, QUERY_PER_KEY)
    key_value_piece = jnp.concatenate([flattened_keys, value_slice], axis=1)
    key_value = lax.all_to_all(
        jnp.broadcast_to(key_value_piece[None], (columns,) + key_value_piece.shape),
        "col",
        0,
        0,
        tiled=True,
    ).reshape(columns * token_rows, key_value_piece.shape[1])
    block_tokens = key_value.shape[0]
    window = min(block_tokens, LONGEST_PROMPT + token_rows)
    window_start = jnp.clip((col_index + 1) * token_rows - window, 0, block_tokens - window)
    key_value = lax.dynamic_slice_in_dim(key_value, window_start, window, axis=0)
    segments = (key_value[:, : KEY_HEADS * HEAD_SIZE], key_value[:, KEY_HEADS * HEAD_SIZE :])
    best_experts = jnp.full((KEY_HEADS, QUERY_PER_KEY * token_rows), -1e30, jnp.float32)
    segment_length = segments[0].shape[0]
    key_lines = segments[0].reshape(segment_length, KEY_HEADS, HEAD_SIZE).transpose(1, 0, 2)
    value_lines = segments[1].reshape(segment_length, KEY_HEADS, HEAD_SIZE).transpose(1, 0, 2)
    key_index = window_start + jnp.arange(segment_length, dtype=jnp.int32)
    key_prompt = prompt_layout(lengths_row, key_index)[0]
    allowed = (key_prompt[None, :] == query_prompt[:, None]) & (
        key_index[None, :] <= query_index[:, None]
    )
    scores = jnp.einsum(
        "hqd,hkd->hqk", grouped, key_lines, preferred_element_type=jnp.float32
    ) * HEAD_SIZE ** (-0.5)
    masked = jnp.where(allowed[None], scores, -1e30)
    fresh = jnp.maximum(best_experts, jnp.max(masked, axis=-1))
    weights = jnp.where(allowed[None], jnp.exp(scores - fresh[..., None]), 0.0)
    running_new = jnp.sum(weights, axis=-1)
    accum_new = jnp.einsum(
        "hqk,hkd->hqd",
        weights.astype(jnp.bfloat16),
        value_lines,
        preferred_element_type=jnp.float32,
    )
    mixed_output = accum_new / running_new[..., None]
    attention_result = (
        mixed_output.reshape(KEY_HEADS, QUERY_PER_KEY, token_rows, HEAD_SIZE)
        .transpose(2, 0, 1, 3)
        .reshape(token_rows, QUERY_HEADS * HEAD_SIZE)
        .astype(jnp.bfloat16)
    )
    projected_rows = times_halves(attention_result, out_halves)
    projected_rows = projected_rows + adapter_scale * adapter_change(
        attention_result, within_prompt, output_down_map, output_up_map
    )
    residual = (hidden_input.astype(jnp.float32) + projected_rows).astype(jnp.bfloat16)
    normed_two = rms_scaled(residual, expert_norm_gain)
    logits = jnp.dot(normed_two, router, preferred_element_type=jnp.float32)
    squashed = jax.nn.sigmoid(jnp.take_along_axis(logits, routes, axis=1))
    mixing = squashed / jnp.sum(squashed, axis=1, keepdims=True)
    expert_total = router.shape[1]
    local_experts = expert_gate_weight.shape[0]
    flat_routes = routes.reshape(-1)
    slots = route_slots(flat_routes, expert_total)
    slot_total = expert_total * CAP
    route_id = (flat_routes * CAP + slots).reshape(token_rows, routes.shape[1])
    matches = route_id[:, :, None] == jnp.arange(slot_total, dtype=jnp.int32)[None, None, :]
    picks = jnp.sum(matches.astype(jnp.float32), axis=1)
    dispatch_rows = jnp.dot(
        picks.T.astype(jnp.bfloat16), normed_two, preferred_element_type=jnp.float32
    ).astype(jnp.bfloat16)
    sending = dispatch_rows.reshape(columns, local_experts, CAP, model_width)
    arrived = lax.all_to_all(sending, "col", split_axis=0, concat_axis=0, tiled=True)
    gate_vals = jnp.einsum(
        "sjcd,jdf->sjcf", arrived, expert_gate_weight, preferred_element_type=jnp.float32
    )
    up_vals = jnp.einsum(
        "sjcd,jdf->sjcf", arrived, expert_up_weight, preferred_element_type=jnp.float32
    )
    hidden_vals = (jnp.maximum(gate_vals, 0.0) * up_vals).astype(jnp.bfloat16)
    answered = jnp.einsum(
        "sjcf,jfd->sjcd", hidden_vals, expert_down_weight, preferred_element_type=jnp.float32
    ).astype(jnp.bfloat16)
    returned = lax.all_to_all(answered, "col", split_axis=0, concat_axis=0, tiled=True)
    returned_rows = returned.reshape(slot_total, model_width)
    mix_matrix = jnp.sum(jnp.where(matches, mixing[:, :, None], 0.0), axis=1)
    mix_high = mix_matrix.astype(jnp.bfloat16)
    mix_low = (mix_matrix - mix_high.astype(jnp.float32)).astype(jnp.bfloat16)
    combined = jnp.dot(mix_high, returned_rows, preferred_element_type=jnp.float32) + jnp.dot(
        mix_low, returned_rows, preferred_element_type=jnp.float32
    )
    return (residual.astype(jnp.float32) + combined).astype(jnp.bfloat16)


def solution(mesh):
    placed = (
        P(("row", "col"), None),
        P(),
        P(),
        P(("row", "col"), None),
        P(),
        P(),
        P("row", "col"),
        P("row", "col"),
        P(),
        P("col", None, None),
        P("col", None, None),
        P("col", None, None),
        P("col", None, None),
        P("col", None, None),
        P("col", None, None),
        P("col", None, None),
    )
    return jax.shard_map(
        local, mesh=mesh, in_specs=placed, out_specs=P(("row", "col"), None), check_vma=False
    )
```

```python
import jax
import jax.numpy as jnp
from jax import lax
from jax.sharding import PartitionSpec as P

QUERY_HEADS = 12
KEY_HEADS = 2
HEAD_SIZE = 128
QUERY_PER_KEY = 6
CAP = 40
LONGEST_PROMPT = 1536


norm_eps = 1e-06
rope_base = 1000000.0
adapter_scale = 0.5


def rms_scaled(value_tensor, norm_gain):
    widened = value_tensor.astype(jnp.float32)
    inverse = lax.rsqrt(jnp.mean(widened * widened, axis=-1, keepdims=True) + norm_eps)
    return (widened * inverse * norm_gain.astype(jnp.float32)).astype(jnp.bfloat16)


def prompt_layout(lengths_row, tok_index):
    prompt_ends = jnp.cumsum(lengths_row)
    starts = prompt_ends - lengths_row
    prompt_of = jnp.sum((tok_index[:, None] >= prompt_ends[None, :]).astype(jnp.int32), axis=1)
    within_prompt = prompt_of[:, None] == jnp.arange(lengths_row.shape[0], dtype=jnp.int32)[None, :]
    token_positions = tok_index - jnp.sum(jnp.where(within_prompt, starts[None, :], 0), axis=1)
    return (prompt_of, within_prompt, token_positions)


def apply_rotary(value_tensor, token_positions):
    half_width = value_tensor.shape[-1] // 2
    frequency = rope_base ** (
        -2.0 * jnp.arange(half_width, dtype=jnp.float32) / value_tensor.shape[-1]
    )
    angles = token_positions.astype(jnp.float32)[:, None] * frequency[None, :]
    cosine = jnp.cos(angles)[:, None, :]
    sine_part = jnp.sin(angles)[:, None, :]
    front_half = value_tensor[..., :half_width]
    back_half = value_tensor[..., half_width:]
    return jnp.concatenate(
        [front_half * cosine - back_half * sine_part, back_half * cosine + front_half * sine_part],
        axis=-1,
    )


def adapter_change(inputs, within_prompt, downs, ups):
    low_rank = jnp.einsum("nk,prk->npr", inputs, downs, preferred_element_type=jnp.float32)
    low_rank = jnp.where(within_prompt[:, :, None], low_rank, 0.0).astype(jnp.bfloat16)
    return jnp.einsum("npr,pro->no", low_rank, ups, preferred_element_type=jnp.float32)


def route_slots(flat_routes, expert_total):
    marks = (flat_routes[:, None] == jnp.arange(expert_total, dtype=jnp.int32)[None, :]).astype(
        jnp.int32
    )
    before = jnp.cumsum(marks, axis=0) - marks
    return jnp.sum(before * marks, axis=1)


def local(
    hidden_input,
    lengths,
    prompt_adapter,
    routes,
    attention_norm_gain,
    expert_norm_gain,
    projection_weight,
    output_weight,
    router,
    adapter_projection_down,
    adapter_projection_up,
    adapter_output_down,
    adapter_output_up,
    expert_gate_weight,
    expert_up_weight,
    expert_down_weight,
):
    token_rows = hidden_input.shape[0]
    model_width = hidden_input.shape[1]
    columns = lax.axis_size("col")
    row_index = lax.axis_index("row")
    col_index = lax.axis_index("col")
    lengths_row = lax.dynamic_index_in_dim(lengths, row_index, 0, keepdims=False)
    adapter_row = lax.dynamic_index_in_dim(prompt_adapter, row_index, 0, keepdims=False)
    tok_index = col_index * token_rows + jnp.arange(token_rows, dtype=jnp.int32)
    prompt_of, within_prompt, token_positions = prompt_layout(lengths_row, tok_index)
    local_adapters = adapter_projection_down.shape[0]
    owner_column = adapter_row // local_adapters
    nearby_slot = adapter_row % local_adapters
    owned_here = (owner_column == col_index)[:, None, None]
    tables = (adapter_projection_down, adapter_projection_up, adapter_output_down, adapter_output_up)
    picked = jnp.concatenate(
        [
            jnp.where(owned_here, jnp.take(table, nearby_slot, axis=0), jnp.zeros((), table.dtype))
            for table in tables
        ],
        axis=-1,
    )
    picked_shape = picked.shape
    lane = 128
    chunks = picked.reshape(columns, -1, lane)
    blocks = (projection_weight, output_weight)
    flat_blocks = [block.reshape(-1, lane) for block in blocks]
    sizes = [chunks.shape[1]] + [flat.shape[0] for flat in flat_blocks]
    starts = [sum(sizes[:i]) for i in range(len(sizes) + 1)]
    bundle = jnp.concatenate(
        [chunks] + [jnp.broadcast_to(flat[None], (columns,) + flat.shape) for flat in flat_blocks],
        axis=1,
    )
    bundle = lax.all_to_all(bundle, "col", 0, 0, tiled=True)
    received = bundle[:, starts[0] : starts[1]]
    slabs = []
    for i, block in enumerate(blocks):
        rows_here, cols_here = block.shape
        piece = bundle[:, starts[i + 1] : starts[i + 2]].reshape(columns, rows_here, cols_here)
        slabs.append(piece.transpose(1, 0, 2).reshape(rows_here, columns * cols_here))
    reduced = jnp.sum(received.astype(jnp.float32), axis=0).astype(jnp.bfloat16)
    spread = lax.all_to_all(
        jnp.broadcast_to(reduced[None], (columns,) + reduced.shape), "col", 0, 0, tiled=True
    )
    core_index = col_index % 2
    partner = [(c, c ^ 1) for c in range(columns)]

    def gather_halves(slab):
        half = slab.shape[1] // 2
        own = lax.dynamic_slice_in_dim(slab, core_index * half, half, axis=1)
        own = lax.all_gather(own, "row", axis=0, tiled=True)
        other = lax.ppermute(own, "col", partner)
        return own, other

    def times_halves(inputs, halves):
        own, other = halves
        half = own.shape[1]
        placed = jnp.zeros((inputs.shape[0], 2 * half), jnp.float32)
        placed = lax.dynamic_update_slice_in_dim(
            placed, jnp.dot(inputs, own, preferred_element_type=jnp.float32), core_index * half, 1
        )
        return lax.dynamic_update_slice_in_dim(
            placed,
            jnp.dot(inputs, other, preferred_element_type=jnp.float32),
            (1 - core_index) * half,
            1,
        )

    qkv_halves = gather_halves(slabs[0])
    out_halves = gather_halves(slabs[1])
    maps = spread.reshape(picked_shape)
    widths = [table.shape[-1] for table in tables]
    bounds = [sum(widths[:i]) for i in range(len(widths) + 1)]
    projection_down_map, projection_up_map, output_down_map, output_up_map = [
        maps[..., bounds[i] : bounds[i + 1]] for i in range(len(tables))
    ]
    normalized = rms_scaled(hidden_input, attention_norm_gain)
    projection_all = times_halves(normalized, qkv_halves)
    projection_all = projection_all + adapter_scale * adapter_change(
        normalized, within_prompt, projection_down_map, projection_up_map
    )
    query_slice = apply_rotary(
        projection_all[:, : QUERY_HEADS * HEAD_SIZE].reshape(token_rows, QUERY_HEADS, HEAD_SIZE),
        token_positions,
    ).astype(jnp.bfloat16)
    key_slice = apply_rotary(
        projection_all[:, QUERY_HEADS * HEAD_SIZE : (QUERY_HEADS + KEY_HEADS) * HEAD_SIZE].reshape(
            token_rows, KEY_HEADS, HEAD_SIZE
        ),
        token_positions,
    ).astype(jnp.bfloat16)
    value_slice = projection_all[:, (QUERY_HEADS + KEY_HEADS) * HEAD_SIZE :].astype(jnp.bfloat16)
    flattened_keys = key_slice.reshape(token_rows, KEY_HEADS * HEAD_SIZE)
    grouped = (
        query_slice.reshape(token_rows, KEY_HEADS, QUERY_PER_KEY, HEAD_SIZE)
        .transpose(1, 2, 0, 3)
        .reshape(KEY_HEADS, QUERY_PER_KEY * token_rows, HEAD_SIZE)
    )
    query_index = jnp.tile(tok_index, QUERY_PER_KEY)
    query_prompt = jnp.tile(prompt_of, QUERY_PER_KEY)
    key_value_piece = jnp.concatenate([flattened_keys, value_slice], axis=1)
    key_value = lax.all_to_all(
        jnp.broadcast_to(key_value_piece[None], (columns,) + key_value_piece.shape),
        "col",
        0,
        0,
        tiled=True,
    ).reshape(columns * token_rows, key_value_piece.shape[1])
    block_tokens = key_value.shape[0]
    window = min(block_tokens, LONGEST_PROMPT + token_rows)
    window_start = jnp.clip((col_index + 1) * token_rows - window, 0, block_tokens - window)
    key_value = lax.dynamic_slice_in_dim(key_value, window_start, window, axis=0)
    segments = (key_value[:, : KEY_HEADS * HEAD_SIZE], key_value[:, KEY_HEADS * HEAD_SIZE :])
    best_experts = jnp.full((KEY_HEADS, QUERY_PER_KEY * token_rows), -1e30, jnp.float32)
    segment_length = segments[0].shape[0]
    key_lines = segments[0].reshape(segment_length, KEY_HEADS, HEAD_SIZE).transpose(1, 0, 2)
    value_lines = segments[1].reshape(segment_length, KEY_HEADS, HEAD_SIZE).transpose(1, 0, 2)
    key_index = window_start + jnp.arange(segment_length, dtype=jnp.int32)
    key_prompt = prompt_layout(lengths_row, key_index)[0]
    allowed = (key_prompt[None, :] == query_prompt[:, None]) & (
        key_index[None, :] <= query_index[:, None]
    )
    scores = jnp.einsum(
        "hqd,hkd->hqk", grouped, key_lines, preferred_element_type=jnp.float32
    ) * HEAD_SIZE ** (-0.5)
    masked = jnp.where(allowed[None], scores, -1e30)
    fresh = jnp.maximum(best_experts, jnp.max(masked, axis=-1))
    weights = jnp.where(allowed[None], jnp.exp(scores - fresh[..., None]), 0.0)
    running_new = jnp.sum(weights, axis=-1)
    accum_new = jnp.einsum(
        "hqk,hkd->hqd",
        weights.astype(jnp.bfloat16),
        value_lines,
        preferred_element_type=jnp.float32,
    )
    mixed_output = accum_new / running_new[..., None]
    attention_result = (
        mixed_output.reshape(KEY_HEADS, QUERY_PER_KEY, token_rows, HEAD_SIZE)
        .transpose(2, 0, 1, 3)
        .reshape(token_rows, QUERY_HEADS * HEAD_SIZE)
        .astype(jnp.bfloat16)
    )
    projected_rows = times_halves(attention_result, out_halves)
    projected_rows = projected_rows + adapter_scale * adapter_change(
        attention_result, within_prompt, output_down_map, output_up_map
    )
    residual = (hidden_input.astype(jnp.float32) + projected_rows).astype(jnp.bfloat16)
    normed_two = rms_scaled(residual, expert_norm_gain)
    logits = jnp.dot(normed_two, router, preferred_element_type=jnp.float32)
    squashed = jax.nn.sigmoid(jnp.take_along_axis(logits, routes, axis=1))
    mixing = squashed / jnp.sum(squashed, axis=1, keepdims=True)
    expert_total = router.shape[1]
    local_experts = expert_gate_weight.shape[0]
    flat_routes = routes.reshape(-1)
    slots = route_slots(flat_routes, expert_total)
    slot_total = expert_total * CAP
    route_id = (flat_routes * CAP + slots).reshape(token_rows, routes.shape[1])
    matches = route_id[:, :, None] == jnp.arange(slot_total, dtype=jnp.int32)[None, None, :]
    picks = jnp.sum(matches.astype(jnp.float32), axis=1)
    dispatch_rows = jnp.dot(
        picks.T.astype(jnp.bfloat16), normed_two, preferred_element_type=jnp.float32
    ).astype(jnp.bfloat16)
    sending = dispatch_rows.reshape(columns, local_experts, CAP, model_width)
    answers = []
    for j in range(local_experts):
        arrived = lax.all_to_all(sending[:, j], "col", split_axis=0, concat_axis=0, tiled=True)
        gate_vals = jnp.einsum(
            "scd,df->scf", arrived, expert_gate_weight[j], preferred_element_type=jnp.float32
        )
        up_vals = jnp.einsum(
            "scd,df->scf", arrived, expert_up_weight[j], preferred_element_type=jnp.float32
        )
        hidden_vals = (jnp.maximum(gate_vals, 0.0) * up_vals).astype(jnp.bfloat16)
        answered = jnp.einsum(
            "scf,fd->scd", hidden_vals, expert_down_weight[j], preferred_element_type=jnp.float32
        ).astype(jnp.bfloat16)
        answers.append(lax.all_to_all(answered, "col", split_axis=0, concat_axis=0, tiled=True))
    returned = jnp.stack(answers, axis=1)
    returned_rows = returned.reshape(slot_total, model_width)
    mix_matrix = jnp.sum(jnp.where(matches, mixing[:, :, None], 0.0), axis=1)
    mix_high = mix_matrix.astype(jnp.bfloat16)
    mix_low = (mix_matrix - mix_high.astype(jnp.float32)).astype(jnp.bfloat16)
    combined = jnp.dot(mix_high, returned_rows, preferred_element_type=jnp.float32) + jnp.dot(
        mix_low, returned_rows, preferred_element_type=jnp.float32
    )
    return (residual.astype(jnp.float32) + combined).astype(jnp.bfloat16)


def solution(mesh):
    placed = (
        P(("row", "col"), None),
        P(),
        P(),
        P(("row", "col"), None),
        P(),
        P(),
        P("row", "col"),
        P("row", "col"),
        P(),
        P("col", None, None),
        P("col", None, None),
        P("col", None, None),
        P("col", None, None),
        P("col", None, None),
        P("col", None, None),
        P("col", None, None),
    )
    return jax.shard_map(
        local, mesh=mesh, in_specs=placed, out_specs=P(("row", "col"), None), check_vma=False
    )
```

```python
import jax
import jax.numpy as jnp
from jax import lax
from jax.sharding import PartitionSpec as P

QUERY_HEADS = 12
KEY_HEADS = 2
HEAD_SIZE = 128
QUERY_PER_KEY = 6
CAP = 40
LONGEST_PROMPT = 1536


norm_eps = 1e-06
rope_base = 1000000.0
adapter_scale = 0.5


def rms_scaled(value_tensor, norm_gain):
    widened = value_tensor.astype(jnp.float32)
    inverse = lax.rsqrt(jnp.mean(widened * widened, axis=-1, keepdims=True) + norm_eps)
    return (widened * inverse * norm_gain.astype(jnp.float32)).astype(jnp.bfloat16)


def prompt_layout(lengths_row, tok_index):
    prompt_ends = jnp.cumsum(lengths_row)
    starts = prompt_ends - lengths_row
    prompt_of = jnp.sum((tok_index[:, None] >= prompt_ends[None, :]).astype(jnp.int32), axis=1)
    within_prompt = prompt_of[:, None] == jnp.arange(lengths_row.shape[0], dtype=jnp.int32)[None, :]
    token_positions = tok_index - jnp.sum(jnp.where(within_prompt, starts[None, :], 0), axis=1)
    return (prompt_of, within_prompt, token_positions)


def apply_rotary(value_tensor, token_positions):
    half_width = value_tensor.shape[-1] // 2
    frequency = rope_base ** (
        -2.0 * jnp.arange(half_width, dtype=jnp.float32) / value_tensor.shape[-1]
    )
    angles = token_positions.astype(jnp.float32)[:, None] * frequency[None, :]
    cosine = jnp.cos(angles)[:, None, :]
    sine_part = jnp.sin(angles)[:, None, :]
    front_half = value_tensor[..., :half_width]
    back_half = value_tensor[..., half_width:]
    return jnp.concatenate(
        [front_half * cosine - back_half * sine_part, back_half * cosine + front_half * sine_part],
        axis=-1,
    )


def adapter_change(inputs, within_prompt, downs, ups):
    low_rank = jnp.einsum("nk,prk->npr", inputs, downs, preferred_element_type=jnp.float32)
    low_rank = jnp.where(within_prompt[:, :, None], low_rank, 0.0).astype(jnp.bfloat16)
    return jnp.einsum("npr,pro->no", low_rank, ups, preferred_element_type=jnp.float32)


def route_slots(flat_routes, expert_total):
    marks = (flat_routes[:, None] == jnp.arange(expert_total, dtype=jnp.int32)[None, :]).astype(
        jnp.int32
    )
    before = jnp.cumsum(marks, axis=0) - marks
    return jnp.sum(before * marks, axis=1)


def local(
    hidden_input,
    lengths,
    prompt_adapter,
    routes,
    attention_norm_gain,
    expert_norm_gain,
    projection_weight,
    output_weight,
    router,
    adapter_projection_down,
    adapter_projection_up,
    adapter_output_down,
    adapter_output_up,
    expert_gate_weight,
    expert_up_weight,
    expert_down_weight,
):
    token_rows = hidden_input.shape[0]
    model_width = hidden_input.shape[1]
    columns = lax.axis_size("col")
    row_index = lax.axis_index("row")
    col_index = lax.axis_index("col")
    lengths_row = lax.dynamic_index_in_dim(lengths, row_index, 0, keepdims=False)
    adapter_row = lax.dynamic_index_in_dim(prompt_adapter, row_index, 0, keepdims=False)
    tok_index = col_index * token_rows + jnp.arange(token_rows, dtype=jnp.int32)
    prompt_of, within_prompt, token_positions = prompt_layout(lengths_row, tok_index)
    local_adapters = adapter_projection_down.shape[0]
    owner_column = adapter_row // local_adapters
    nearby_slot = adapter_row % local_adapters
    owned_here = (owner_column == col_index)[:, None, None]
    tables = (adapter_projection_down, adapter_projection_up, adapter_output_down, adapter_output_up)
    picked = jnp.concatenate(
        [
            jnp.where(owned_here, jnp.take(table, nearby_slot, axis=0), jnp.zeros((), table.dtype))
            for table in tables
        ],
        axis=-1,
    )
    picked_shape = picked.shape
    lane = 128
    chunks = picked.reshape(columns, -1, lane)
    blocks = (projection_weight, output_weight)
    flat_blocks = [block.reshape(-1, lane) for block in blocks]
    sizes = [chunks.shape[1]] + [flat.shape[0] for flat in flat_blocks]
    starts = [sum(sizes[:i]) for i in range(len(sizes) + 1)]
    bundle = jnp.concatenate(
        [chunks] + [jnp.broadcast_to(flat[None], (columns,) + flat.shape) for flat in flat_blocks],
        axis=1,
    )
    bundle = lax.all_to_all(bundle, "col", 0, 0, tiled=True)
    received = bundle[:, starts[0] : starts[1]]
    slabs = []
    for i, block in enumerate(blocks):
        rows_here, cols_here = block.shape
        piece = bundle[:, starts[i + 1] : starts[i + 2]].reshape(columns, rows_here, cols_here)
        slabs.append(piece.transpose(1, 0, 2).reshape(rows_here, columns * cols_here))
    reduced = jnp.sum(received.astype(jnp.float32), axis=0).astype(jnp.bfloat16)
    spread = lax.all_to_all(
        jnp.broadcast_to(reduced[None], (columns,) + reduced.shape), "col", 0, 0, tiled=True
    )
    core_index = col_index % 2
    partner = [(c, c ^ 1) for c in range(columns)]

    def gather_halves(slab_list):
        owns = []
        for slab in slab_list:
            half = slab.shape[1] // 2
            owns.append(lax.dynamic_slice_in_dim(slab, core_index * half, half, axis=1))
        widths_own = [own.shape[1] for own in owns]
        joined = lax.all_gather(jnp.concatenate(owns, axis=1), "row", axis=0, tiled=True)
        swapped = lax.ppermute(joined, "col", partner)
        cuts = [sum(widths_own[:i]) for i in range(len(widths_own) + 1)]
        return [
            (joined[:, cuts[i] : cuts[i + 1]], swapped[:, cuts[i] : cuts[i + 1]])
            for i in range(len(owns))
        ]

    def times_halves(inputs, halves):
        own, other = halves
        half = own.shape[1]
        placed = jnp.zeros((inputs.shape[0], 2 * half), jnp.float32)
        placed = lax.dynamic_update_slice_in_dim(
            placed, jnp.dot(inputs, own, preferred_element_type=jnp.float32), core_index * half, 1
        )
        return lax.dynamic_update_slice_in_dim(
            placed,
            jnp.dot(inputs, other, preferred_element_type=jnp.float32),
            (1 - core_index) * half,
            1,
        )

    qkv_halves, out_halves = gather_halves(slabs)
    maps = spread.reshape(picked_shape)
    widths = [table.shape[-1] for table in tables]
    bounds = [sum(widths[:i]) for i in range(len(widths) + 1)]
    projection_down_map, projection_up_map, output_down_map, output_up_map = [
        maps[..., bounds[i] : bounds[i + 1]] for i in range(len(tables))
    ]
    normalized = rms_scaled(hidden_input, attention_norm_gain)
    projection_all = times_halves(normalized, qkv_halves)
    projection_all = projection_all + adapter_scale * adapter_change(
        normalized, within_prompt, projection_down_map, projection_up_map
    )
    query_slice = apply_rotary(
        projection_all[:, : QUERY_HEADS * HEAD_SIZE].reshape(token_rows, QUERY_HEADS, HEAD_SIZE),
        token_positions,
    ).astype(jnp.bfloat16)
    key_slice = apply_rotary(
        projection_all[:, QUERY_HEADS * HEAD_SIZE : (QUERY_HEADS + KEY_HEADS) * HEAD_SIZE].reshape(
            token_rows, KEY_HEADS, HEAD_SIZE
        ),
        token_positions,
    ).astype(jnp.bfloat16)
    value_slice = projection_all[:, (QUERY_HEADS + KEY_HEADS) * HEAD_SIZE :].astype(jnp.bfloat16)
    flattened_keys = key_slice.reshape(token_rows, KEY_HEADS * HEAD_SIZE)
    grouped = (
        query_slice.reshape(token_rows, KEY_HEADS, QUERY_PER_KEY, HEAD_SIZE)
        .transpose(1, 2, 0, 3)
        .reshape(KEY_HEADS, QUERY_PER_KEY * token_rows, HEAD_SIZE)
    )
    query_index = jnp.tile(tok_index, QUERY_PER_KEY)
    query_prompt = jnp.tile(prompt_of, QUERY_PER_KEY)
    key_value_piece = jnp.concatenate([flattened_keys, value_slice], axis=1)
    key_value = lax.all_to_all(
        jnp.broadcast_to(key_value_piece[None], (columns,) + key_value_piece.shape),
        "col",
        0,
        0,
        tiled=True,
    ).reshape(columns * token_rows, key_value_piece.shape[1])
    block_tokens = key_value.shape[0]
    window = min(block_tokens, LONGEST_PROMPT + token_rows)
    window_start = jnp.clip((col_index + 1) * token_rows - window, 0, block_tokens - window)
    key_value = lax.dynamic_slice_in_dim(key_value, window_start, window, axis=0)
    segments = (key_value[:, : KEY_HEADS * HEAD_SIZE], key_value[:, KEY_HEADS * HEAD_SIZE :])
    best_experts = jnp.full((KEY_HEADS, QUERY_PER_KEY * token_rows), -1e30, jnp.float32)
    segment_length = segments[0].shape[0]
    key_lines = segments[0].reshape(segment_length, KEY_HEADS, HEAD_SIZE).transpose(1, 0, 2)
    value_lines = segments[1].reshape(segment_length, KEY_HEADS, HEAD_SIZE).transpose(1, 0, 2)
    key_index = window_start + jnp.arange(segment_length, dtype=jnp.int32)
    key_prompt = prompt_layout(lengths_row, key_index)[0]
    allowed = (key_prompt[None, :] == query_prompt[:, None]) & (
        key_index[None, :] <= query_index[:, None]
    )
    scores = jnp.einsum(
        "hqd,hkd->hqk", grouped, key_lines, preferred_element_type=jnp.float32
    ) * HEAD_SIZE ** (-0.5)
    masked = jnp.where(allowed[None], scores, -1e30)
    fresh = jnp.maximum(best_experts, jnp.max(masked, axis=-1))
    weights = jnp.where(allowed[None], jnp.exp(scores - fresh[..., None]), 0.0)
    running_new = jnp.sum(weights, axis=-1)
    accum_new = jnp.einsum(
        "hqk,hkd->hqd",
        weights.astype(jnp.bfloat16),
        value_lines,
        preferred_element_type=jnp.float32,
    )
    mixed_output = accum_new / running_new[..., None]
    attention_result = (
        mixed_output.reshape(KEY_HEADS, QUERY_PER_KEY, token_rows, HEAD_SIZE)
        .transpose(2, 0, 1, 3)
        .reshape(token_rows, QUERY_HEADS * HEAD_SIZE)
        .astype(jnp.bfloat16)
    )
    projected_rows = times_halves(attention_result, out_halves)
    projected_rows = projected_rows + adapter_scale * adapter_change(
        attention_result, within_prompt, output_down_map, output_up_map
    )
    residual = (hidden_input.astype(jnp.float32) + projected_rows).astype(jnp.bfloat16)
    normed_two = rms_scaled(residual, expert_norm_gain)
    logits = jnp.dot(normed_two, router, preferred_element_type=jnp.float32)
    squashed = jax.nn.sigmoid(jnp.take_along_axis(logits, routes, axis=1))
    mixing = squashed / jnp.sum(squashed, axis=1, keepdims=True)
    expert_total = router.shape[1]
    local_experts = expert_gate_weight.shape[0]
    flat_routes = routes.reshape(-1)
    slots = route_slots(flat_routes, expert_total)
    slot_total = expert_total * CAP
    route_id = (flat_routes * CAP + slots).reshape(token_rows, routes.shape[1])
    matches = route_id[:, :, None] == jnp.arange(slot_total, dtype=jnp.int32)[None, None, :]
    picks = jnp.sum(matches.astype(jnp.float32), axis=1)
    dispatch_rows = jnp.dot(
        picks.T.astype(jnp.bfloat16), normed_two, preferred_element_type=jnp.float32
    ).astype(jnp.bfloat16)
    sending = dispatch_rows.reshape(columns, local_experts, CAP, model_width)
    arrived = lax.all_to_all(sending, "col", split_axis=0, concat_axis=0, tiled=True)
    gate_vals = jnp.einsum(
        "sjcd,jdf->sjcf", arrived, expert_gate_weight, preferred_element_type=jnp.float32
    )
    up_vals = jnp.einsum(
        "sjcd,jdf->sjcf", arrived, expert_up_weight, preferred_element_type=jnp.float32
    )
    hidden_vals = (jnp.maximum(gate_vals, 0.0) * up_vals).astype(jnp.bfloat16)
    answered = jnp.einsum(
        "sjcf,jfd->sjcd", hidden_vals, expert_down_weight, preferred_element_type=jnp.float32
    ).astype(jnp.bfloat16)
    returned = lax.all_to_all(answered, "col", split_axis=0, concat_axis=0, tiled=True)
    returned_rows = returned.reshape(slot_total, model_width)
    mix_matrix = jnp.sum(jnp.where(matches, mixing[:, :, None], 0.0), axis=1)
    mix_high = mix_matrix.astype(jnp.bfloat16)
    mix_low = (mix_matrix - mix_high.astype(jnp.float32)).astype(jnp.bfloat16)
    combined = jnp.dot(mix_high, returned_rows, preferred_element_type=jnp.float32) + jnp.dot(
        mix_low, returned_rows, preferred_element_type=jnp.float32
    )
    return (residual.astype(jnp.float32) + combined).astype(jnp.bfloat16)


def solution(mesh):
    placed = (
        P(("row", "col"), None),
        P(),
        P(),
        P(("row", "col"), None),
        P(),
        P(),
        P("row", "col"),
        P("row", "col"),
        P(),
        P("col", None, None),
        P("col", None, None),
        P("col", None, None),
        P("col", None, None),
        P("col", None, None),
        P("col", None, None),
        P("col", None, None),
    )
    return jax.shard_map(
        local, mesh=mesh, in_specs=placed, out_specs=P(("row", "col"), None), check_vma=False
    )
```

```python
import jax
import jax.numpy as jnp
from jax import lax
from jax.sharding import PartitionSpec as P

QUERY_HEADS = 12
KEY_HEADS = 2
HEAD_SIZE = 128
QUERY_PER_KEY = 6
CAP = 40
LONGEST_PROMPT = 1536


norm_eps = 1e-06
rope_base = 1000000.0
adapter_scale = 0.5


def rms_scaled(value_tensor, norm_gain):
    widened = value_tensor.astype(jnp.float32)
    inverse = lax.rsqrt(jnp.mean(widened * widened, axis=-1, keepdims=True) + norm_eps)
    return (widened * inverse * norm_gain.astype(jnp.float32)).astype(jnp.bfloat16)


def prompt_layout(lengths_row, tok_index):
    prompt_ends = jnp.cumsum(lengths_row)
    starts = prompt_ends - lengths_row
    prompt_of = jnp.sum((tok_index[:, None] >= prompt_ends[None, :]).astype(jnp.int32), axis=1)
    within_prompt = prompt_of[:, None] == jnp.arange(lengths_row.shape[0], dtype=jnp.int32)[None, :]
    token_positions = tok_index - jnp.sum(jnp.where(within_prompt, starts[None, :], 0), axis=1)
    return (prompt_of, within_prompt, token_positions)


def apply_rotary(value_tensor, token_positions):
    half_width = value_tensor.shape[-1] // 2
    frequency = rope_base ** (
        -2.0 * jnp.arange(half_width, dtype=jnp.float32) / value_tensor.shape[-1]
    )
    angles = token_positions.astype(jnp.float32)[:, None] * frequency[None, :]
    cosine = jnp.cos(angles)[:, None, :]
    sine_part = jnp.sin(angles)[:, None, :]
    front_half = value_tensor[..., :half_width]
    back_half = value_tensor[..., half_width:]
    return jnp.concatenate(
        [front_half * cosine - back_half * sine_part, back_half * cosine + front_half * sine_part],
        axis=-1,
    )


def adapter_change(inputs, within_prompt, downs, ups):
    low_rank = jnp.einsum("nk,prk->npr", inputs, downs, preferred_element_type=jnp.float32)
    low_rank = jnp.where(within_prompt[:, :, None], low_rank, 0.0).astype(jnp.bfloat16)
    return jnp.einsum("npr,pro->no", low_rank, ups, preferred_element_type=jnp.float32)


def route_slots(flat_routes, expert_total):
    marks = (flat_routes[:, None] == jnp.arange(expert_total, dtype=jnp.int32)[None, :]).astype(
        jnp.int32
    )
    before = jnp.cumsum(marks, axis=0) - marks
    return jnp.sum(before * marks, axis=1)


def local(
    hidden_input,
    lengths,
    prompt_adapter,
    routes,
    attention_norm_gain,
    expert_norm_gain,
    projection_weight,
    output_weight,
    router,
    adapter_projection_down,
    adapter_projection_up,
    adapter_output_down,
    adapter_output_up,
    expert_gate_weight,
    expert_up_weight,
    expert_down_weight,
):
    token_rows = hidden_input.shape[0]
    model_width = hidden_input.shape[1]
    columns = lax.axis_size("col")
    row_index = lax.axis_index("row")
    col_index = lax.axis_index("col")
    lengths_row = lax.dynamic_index_in_dim(lengths, row_index, 0, keepdims=False)
    adapter_row = lax.dynamic_index_in_dim(prompt_adapter, row_index, 0, keepdims=False)
    tok_index = col_index * token_rows + jnp.arange(token_rows, dtype=jnp.int32)
    prompt_of, within_prompt, token_positions = prompt_layout(lengths_row, tok_index)
    local_adapters = adapter_projection_down.shape[0]
    owner_column = adapter_row // local_adapters
    nearby_slot = adapter_row % local_adapters
    owned_here = (owner_column == col_index)[:, None, None]
    tables = (adapter_projection_down, adapter_projection_up, adapter_output_down, adapter_output_up)
    picked = jnp.concatenate(
        [
            jnp.where(owned_here, jnp.take(table, nearby_slot, axis=0), jnp.zeros((), table.dtype))
            for table in tables
        ],
        axis=-1,
    )
    picked_shape = picked.shape
    lane = 128
    chunks = picked.reshape(columns, -1, lane)
    blocks = (projection_weight, output_weight)
    dest_parity = jnp.arange(columns, dtype=jnp.int32) % 2
    flat_blocks = []
    for block in blocks:
        rows_here, cols_here = block.shape
        split = block.reshape(rows_here, 2, cols_here // 2)
        chosen = jnp.take(split, dest_parity, axis=1).transpose(1, 0, 2)
        flat_blocks.append(chosen.reshape(columns, -1, lane))
    sizes = [chunks.shape[1]] + [flat.shape[1] for flat in flat_blocks]
    starts = [sum(sizes[:i]) for i in range(len(sizes) + 1)]
    bundle = jnp.concatenate([chunks] + flat_blocks, axis=1)
    bundle = lax.all_to_all(bundle, "col", 0, 0, tiled=True)
    received = bundle[:, starts[0] : starts[1]]
    slabs = []
    for i, block in enumerate(blocks):
        rows_here, cols_here = block.shape
        piece = bundle[:, starts[i + 1] : starts[i + 2]].reshape(columns, rows_here, cols_here // 2)
        slabs.append(piece.transpose(1, 0, 2).reshape(rows_here, columns * (cols_here // 2)))
    reduced = jnp.sum(received.astype(jnp.float32), axis=0).astype(jnp.bfloat16)
    spread = lax.all_to_all(
        jnp.broadcast_to(reduced[None], (columns,) + reduced.shape), "col", 0, 0, tiled=True
    )
    core_index = col_index % 2
    partner = [(c, c ^ 1) for c in range(columns)]

    def gather_halves(slab):
        own = lax.all_gather(slab, "row", axis=0, tiled=True)
        other = lax.ppermute(own, "col", partner)
        return own, other

    def times_halves(inputs, halves):
        own, other = halves
        piece = own.shape[1] // columns
        own_part = jnp.dot(inputs, own, preferred_element_type=jnp.float32)
        other_part = jnp.dot(inputs, other, preferred_element_type=jnp.float32)
        own_part = own_part.reshape(inputs.shape[0], columns, piece)
        other_part = other_part.reshape(inputs.shape[0], columns, piece)
        first = jnp.where(core_index == 0, own_part, other_part)
        second = jnp.where(core_index == 0, other_part, own_part)
        return jnp.stack([first, second], axis=2).reshape(inputs.shape[0], 2 * own.shape[1])

    qkv_halves = gather_halves(slabs[0])
    out_halves = gather_halves(slabs[1])
    maps = spread.reshape(picked_shape)
    widths = [table.shape[-1] for table in tables]
    bounds = [sum(widths[:i]) for i in range(len(widths) + 1)]
    projection_down_map, projection_up_map, output_down_map, output_up_map = [
        maps[..., bounds[i] : bounds[i + 1]] for i in range(len(tables))
    ]
    normalized = rms_scaled(hidden_input, attention_norm_gain)
    projection_all = times_halves(normalized, qkv_halves)
    projection_all = projection_all + adapter_scale * adapter_change(
        normalized, within_prompt, projection_down_map, projection_up_map
    )
    query_slice = apply_rotary(
        projection_all[:, : QUERY_HEADS * HEAD_SIZE].reshape(token_rows, QUERY_HEADS, HEAD_SIZE),
        token_positions,
    ).astype(jnp.bfloat16)
    key_slice = apply_rotary(
        projection_all[:, QUERY_HEADS * HEAD_SIZE : (QUERY_HEADS + KEY_HEADS) * HEAD_SIZE].reshape(
            token_rows, KEY_HEADS, HEAD_SIZE
        ),
        token_positions,
    ).astype(jnp.bfloat16)
    value_slice = projection_all[:, (QUERY_HEADS + KEY_HEADS) * HEAD_SIZE :].astype(jnp.bfloat16)
    flattened_keys = key_slice.reshape(token_rows, KEY_HEADS * HEAD_SIZE)
    grouped = (
        query_slice.reshape(token_rows, KEY_HEADS, QUERY_PER_KEY, HEAD_SIZE)
        .transpose(1, 2, 0, 3)
        .reshape(KEY_HEADS, QUERY_PER_KEY * token_rows, HEAD_SIZE)
    )
    query_index = jnp.tile(tok_index, QUERY_PER_KEY)
    query_prompt = jnp.tile(prompt_of, QUERY_PER_KEY)
    key_value_piece = jnp.concatenate([flattened_keys, value_slice], axis=1)
    key_value = lax.all_to_all(
        jnp.broadcast_to(key_value_piece[None], (columns,) + key_value_piece.shape),
        "col",
        0,
        0,
        tiled=True,
    ).reshape(columns * token_rows, key_value_piece.shape[1])
    block_tokens = key_value.shape[0]
    window = min(block_tokens, LONGEST_PROMPT + token_rows)
    window_start = jnp.clip((col_index + 1) * token_rows - window, 0, block_tokens - window)
    key_value = lax.dynamic_slice_in_dim(key_value, window_start, window, axis=0)
    segments = (key_value[:, : KEY_HEADS * HEAD_SIZE], key_value[:, KEY_HEADS * HEAD_SIZE :])
    best_experts = jnp.full((KEY_HEADS, QUERY_PER_KEY * token_rows), -1e30, jnp.float32)
    segment_length = segments[0].shape[0]
    key_lines = segments[0].reshape(segment_length, KEY_HEADS, HEAD_SIZE).transpose(1, 0, 2)
    value_lines = segments[1].reshape(segment_length, KEY_HEADS, HEAD_SIZE).transpose(1, 0, 2)
    key_index = window_start + jnp.arange(segment_length, dtype=jnp.int32)
    key_prompt = prompt_layout(lengths_row, key_index)[0]
    allowed = (key_prompt[None, :] == query_prompt[:, None]) & (
        key_index[None, :] <= query_index[:, None]
    )
    scores = jnp.einsum(
        "hqd,hkd->hqk", grouped, key_lines, preferred_element_type=jnp.float32
    ) * HEAD_SIZE ** (-0.5)
    masked = jnp.where(allowed[None], scores, -1e30)
    fresh = jnp.maximum(best_experts, jnp.max(masked, axis=-1))
    weights = jnp.where(allowed[None], jnp.exp(scores - fresh[..., None]), 0.0)
    running_new = jnp.sum(weights, axis=-1)
    accum_new = jnp.einsum(
        "hqk,hkd->hqd",
        weights.astype(jnp.bfloat16),
        value_lines,
        preferred_element_type=jnp.float32,
    )
    mixed_output = accum_new / running_new[..., None]
    attention_result = (
        mixed_output.reshape(KEY_HEADS, QUERY_PER_KEY, token_rows, HEAD_SIZE)
        .transpose(2, 0, 1, 3)
        .reshape(token_rows, QUERY_HEADS * HEAD_SIZE)
        .astype(jnp.bfloat16)
    )
    projected_rows = times_halves(attention_result, out_halves)
    projected_rows = projected_rows + adapter_scale * adapter_change(
        attention_result, within_prompt, output_down_map, output_up_map
    )
    residual = (hidden_input.astype(jnp.float32) + projected_rows).astype(jnp.bfloat16)
    normed_two = rms_scaled(residual, expert_norm_gain)
    logits = jnp.dot(normed_two, router, preferred_element_type=jnp.float32)
    squashed = jax.nn.sigmoid(jnp.take_along_axis(logits, routes, axis=1))
    mixing = squashed / jnp.sum(squashed, axis=1, keepdims=True)
    expert_total = router.shape[1]
    local_experts = expert_gate_weight.shape[0]
    flat_routes = routes.reshape(-1)
    slots = route_slots(flat_routes, expert_total)
    slot_total = expert_total * CAP
    route_id = (flat_routes * CAP + slots).reshape(token_rows, routes.shape[1])
    matches = route_id[:, :, None] == jnp.arange(slot_total, dtype=jnp.int32)[None, None, :]
    picks = jnp.sum(matches.astype(jnp.float32), axis=1)
    dispatch_rows = jnp.dot(
        picks.T.astype(jnp.bfloat16), normed_two, preferred_element_type=jnp.float32
    ).astype(jnp.bfloat16)
    sending = dispatch_rows.reshape(columns, local_experts, CAP, model_width)
    arrived = lax.all_to_all(sending, "col", split_axis=0, concat_axis=0, tiled=True)
    gate_vals = jnp.einsum(
        "sjcd,jdf->sjcf", arrived, expert_gate_weight, preferred_element_type=jnp.float32
    )
    up_vals = jnp.einsum(
        "sjcd,jdf->sjcf", arrived, expert_up_weight, preferred_element_type=jnp.float32
    )
    hidden_vals = (jnp.maximum(gate_vals, 0.0) * up_vals).astype(jnp.bfloat16)
    answered = jnp.einsum(
        "sjcf,jfd->sjcd", hidden_vals, expert_down_weight, preferred_element_type=jnp.float32
    ).astype(jnp.bfloat16)
    returned = lax.all_to_all(answered, "col", split_axis=0, concat_axis=0, tiled=True)
    returned_rows = returned.reshape(slot_total, model_width)
    mix_matrix = jnp.sum(jnp.where(matches, mixing[:, :, None], 0.0), axis=1)
    mix_high = mix_matrix.astype(jnp.bfloat16)
    mix_low = (mix_matrix - mix_high.astype(jnp.float32)).astype(jnp.bfloat16)
    combined = jnp.dot(mix_high, returned_rows, preferred_element_type=jnp.float32) + jnp.dot(
        mix_low, returned_rows, preferred_element_type=jnp.float32
    )
    return (residual.astype(jnp.float32) + combined).astype(jnp.bfloat16)


def solution(mesh):
    placed = (
        P(("row", "col"), None),
        P(),
        P(),
        P(("row", "col"), None),
        P(),
        P(),
        P("row", "col"),
        P("row", "col"),
        P(),
        P("col", None, None),
        P("col", None, None),
        P("col", None, None),
        P("col", None, None),
        P("col", None, None),
        P("col", None, None),
        P("col", None, None),
    )
    return jax.shard_map(
        local, mesh=mesh, in_specs=placed, out_specs=P(("row", "col"), None), check_vma=False
    )
```

```python
import jax
import jax.numpy as jnp
from jax import lax
from jax.sharding import PartitionSpec as P

QUERY_HEADS = 12
KEY_HEADS = 2
HEAD_SIZE = 128
QUERY_PER_KEY = 6
CAP = 40
LONGEST_PROMPT = 1536


norm_eps = 1e-06
rope_base = 1000000.0
adapter_scale = 0.5


def rms_scaled(value_tensor, norm_gain):
    widened = value_tensor.astype(jnp.float32)
    inverse = lax.rsqrt(jnp.mean(widened * widened, axis=-1, keepdims=True) + norm_eps)
    return (widened * inverse * norm_gain.astype(jnp.float32)).astype(jnp.bfloat16)


def prompt_layout(lengths_row, tok_index):
    prompt_ends = jnp.cumsum(lengths_row)
    starts = prompt_ends - lengths_row
    prompt_of = jnp.sum((tok_index[:, None] >= prompt_ends[None, :]).astype(jnp.int32), axis=1)
    within_prompt = prompt_of[:, None] == jnp.arange(lengths_row.shape[0], dtype=jnp.int32)[None, :]
    token_positions = tok_index - jnp.sum(jnp.where(within_prompt, starts[None, :], 0), axis=1)
    return (prompt_of, within_prompt, token_positions)


def apply_rotary(value_tensor, token_positions):
    half_width = value_tensor.shape[-1] // 2
    frequency = rope_base ** (
        -2.0 * jnp.arange(half_width, dtype=jnp.float32) / value_tensor.shape[-1]
    )
    angles = token_positions.astype(jnp.float32)[:, None] * frequency[None, :]
    cosine = jnp.cos(angles)[:, None, :]
    sine_part = jnp.sin(angles)[:, None, :]
    front_half = value_tensor[..., :half_width]
    back_half = value_tensor[..., half_width:]
    return jnp.concatenate(
        [front_half * cosine - back_half * sine_part, back_half * cosine + front_half * sine_part],
        axis=-1,
    )


def adapter_change(inputs, within_prompt, downs, ups):
    low_rank = jnp.einsum("nk,prk->npr", inputs, downs, preferred_element_type=jnp.float32)
    low_rank = jnp.where(within_prompt[:, :, None], low_rank, 0.0).astype(jnp.bfloat16)
    return jnp.einsum("npr,pro->no", low_rank, ups, preferred_element_type=jnp.float32)


def route_slots(flat_routes, expert_total):
    marks = (flat_routes[:, None] == jnp.arange(expert_total, dtype=jnp.int32)[None, :]).astype(
        jnp.int32
    )
    before = jnp.cumsum(marks, axis=0) - marks
    return jnp.sum(before * marks, axis=1)


def local(
    hidden_input,
    lengths,
    prompt_adapter,
    routes,
    attention_norm_gain,
    expert_norm_gain,
    projection_weight,
    output_weight,
    router,
    adapter_projection_down,
    adapter_projection_up,
    adapter_output_down,
    adapter_output_up,
    expert_gate_weight,
    expert_up_weight,
    expert_down_weight,
):
    token_rows = hidden_input.shape[0]
    model_width = hidden_input.shape[1]
    columns = lax.axis_size("col")
    row_index = lax.axis_index("row")
    col_index = lax.axis_index("col")
    lengths_row = lax.dynamic_index_in_dim(lengths, row_index, 0, keepdims=False)
    adapter_row = lax.dynamic_index_in_dim(prompt_adapter, row_index, 0, keepdims=False)
    tok_index = col_index * token_rows + jnp.arange(token_rows, dtype=jnp.int32)
    prompt_of, within_prompt, token_positions = prompt_layout(lengths_row, tok_index)
    local_adapters = adapter_projection_down.shape[0]
    owner_column = adapter_row // local_adapters
    nearby_slot = adapter_row % local_adapters
    owned_here = (owner_column == col_index)[:, None, None]
    tables = (adapter_projection_down, adapter_projection_up, adapter_output_down, adapter_output_up)
    picked = jnp.concatenate(
        [
            jnp.where(owned_here, jnp.take(table, nearby_slot, axis=0), jnp.zeros((), table.dtype))
            for table in tables
        ],
        axis=-1,
    )
    picked_shape = picked.shape
    lane = 128
    chunks = picked.reshape(columns, -1, lane)
    blocks = (projection_weight, output_weight)
    dest_parity = jnp.arange(columns, dtype=jnp.int32) % 2
    flat_blocks = []
    for i, block in enumerate(blocks):
        rows_here, cols_here = block.shape
        if i == 0:
            split = block.reshape(rows_here, 2, cols_here // 2)
            chosen = jnp.take(split, dest_parity, axis=1).transpose(1, 0, 2)
        else:
            chosen = jnp.broadcast_to(block[None], (columns, rows_here, cols_here))
        flat_blocks.append(chosen.reshape(columns, -1, lane))
    sizes = [chunks.shape[1]] + [flat.shape[1] for flat in flat_blocks]
    starts = [sum(sizes[:i]) for i in range(len(sizes) + 1)]
    bundle = jnp.concatenate([chunks] + flat_blocks, axis=1)
    bundle = lax.all_to_all(bundle, "col", 0, 0, tiled=True)
    received = bundle[:, starts[0] : starts[1]]
    slabs = []
    for i, block in enumerate(blocks):
        rows_here, cols_here = block.shape
        kept = cols_here // 2 if i == 0 else cols_here
        piece = bundle[:, starts[i + 1] : starts[i + 2]].reshape(columns, rows_here, kept)
        slabs.append(piece.transpose(1, 0, 2).reshape(rows_here, columns * kept))
    reduced = jnp.sum(received.astype(jnp.float32), axis=0).astype(jnp.bfloat16)
    spread = lax.all_to_all(
        jnp.broadcast_to(reduced[None], (columns,) + reduced.shape), "col", 0, 0, tiled=True
    )
    core_index = col_index % 2
    partner = [(c, c ^ 1) for c in range(columns)]

    def gather_halves(slab):
        own = lax.all_gather(slab, "row", axis=0, tiled=True)
        other = lax.ppermute(own, "col", partner)
        return own, other

    def times_halves(inputs, halves):
        own, other = halves
        piece = own.shape[1] // columns
        own_part = jnp.dot(inputs, own, preferred_element_type=jnp.float32)
        other_part = jnp.dot(inputs, other, preferred_element_type=jnp.float32)
        own_part = own_part.reshape(inputs.shape[0], columns, piece)
        other_part = other_part.reshape(inputs.shape[0], columns, piece)
        first = jnp.where(core_index == 0, own_part, other_part)
        second = jnp.where(core_index == 0, other_part, own_part)
        return jnp.stack([first, second], axis=2).reshape(inputs.shape[0], 2 * own.shape[1])

    qkv_halves = gather_halves(slabs[0])
    out_half = slabs[1].shape[1] // 2
    out_halves = gather_halves(
        lax.dynamic_slice_in_dim(slabs[1], core_index * out_half, out_half, axis=1)
    )

    def times_blocks(inputs, halves):
        own, other = halves
        half = own.shape[1]
        placed = jnp.zeros((inputs.shape[0], 2 * half), jnp.float32)
        placed = lax.dynamic_update_slice_in_dim(
            placed, jnp.dot(inputs, own, preferred_element_type=jnp.float32), core_index * half, 1
        )
        return lax.dynamic_update_slice_in_dim(
            placed,
            jnp.dot(inputs, other, preferred_element_type=jnp.float32),
            (1 - core_index) * half,
            1,
        )

    maps = spread.reshape(picked_shape)
    widths = [table.shape[-1] for table in tables]
    bounds = [sum(widths[:i]) for i in range(len(widths) + 1)]
    projection_down_map, projection_up_map, output_down_map, output_up_map = [
        maps[..., bounds[i] : bounds[i + 1]] for i in range(len(tables))
    ]
    normalized = rms_scaled(hidden_input, attention_norm_gain)
    projection_all = times_halves(normalized, qkv_halves)
    projection_all = projection_all + adapter_scale * adapter_change(
        normalized, within_prompt, projection_down_map, projection_up_map
    )
    query_slice = apply_rotary(
        projection_all[:, : QUERY_HEADS * HEAD_SIZE].reshape(token_rows, QUERY_HEADS, HEAD_SIZE),
        token_positions,
    ).astype(jnp.bfloat16)
    key_slice = apply_rotary(
        projection_all[:, QUERY_HEADS * HEAD_SIZE : (QUERY_HEADS + KEY_HEADS) * HEAD_SIZE].reshape(
            token_rows, KEY_HEADS, HEAD_SIZE
        ),
        token_positions,
    ).astype(jnp.bfloat16)
    value_slice = projection_all[:, (QUERY_HEADS + KEY_HEADS) * HEAD_SIZE :].astype(jnp.bfloat16)
    flattened_keys = key_slice.reshape(token_rows, KEY_HEADS * HEAD_SIZE)
    grouped = (
        query_slice.reshape(token_rows, KEY_HEADS, QUERY_PER_KEY, HEAD_SIZE)
        .transpose(1, 2, 0, 3)
        .reshape(KEY_HEADS, QUERY_PER_KEY * token_rows, HEAD_SIZE)
    )
    query_index = jnp.tile(tok_index, QUERY_PER_KEY)
    query_prompt = jnp.tile(prompt_of, QUERY_PER_KEY)
    key_value_piece = jnp.concatenate([flattened_keys, value_slice], axis=1)
    key_value = lax.all_to_all(
        jnp.broadcast_to(key_value_piece[None], (columns,) + key_value_piece.shape),
        "col",
        0,
        0,
        tiled=True,
    ).reshape(columns * token_rows, key_value_piece.shape[1])
    block_tokens = key_value.shape[0]
    window = min(block_tokens, LONGEST_PROMPT + token_rows)
    window_start = jnp.clip((col_index + 1) * token_rows - window, 0, block_tokens - window)
    key_value = lax.dynamic_slice_in_dim(key_value, window_start, window, axis=0)
    segments = (key_value[:, : KEY_HEADS * HEAD_SIZE], key_value[:, KEY_HEADS * HEAD_SIZE :])
    best_experts = jnp.full((KEY_HEADS, QUERY_PER_KEY * token_rows), -1e30, jnp.float32)
    segment_length = segments[0].shape[0]
    key_lines = segments[0].reshape(segment_length, KEY_HEADS, HEAD_SIZE).transpose(1, 0, 2)
    value_lines = segments[1].reshape(segment_length, KEY_HEADS, HEAD_SIZE).transpose(1, 0, 2)
    key_index = window_start + jnp.arange(segment_length, dtype=jnp.int32)
    key_prompt = prompt_layout(lengths_row, key_index)[0]
    allowed = (key_prompt[None, :] == query_prompt[:, None]) & (
        key_index[None, :] <= query_index[:, None]
    )
    scores = jnp.einsum(
        "hqd,hkd->hqk", grouped, key_lines, preferred_element_type=jnp.float32
    ) * HEAD_SIZE ** (-0.5)
    masked = jnp.where(allowed[None], scores, -1e30)
    fresh = jnp.maximum(best_experts, jnp.max(masked, axis=-1))
    weights = jnp.where(allowed[None], jnp.exp(scores - fresh[..., None]), 0.0)
    running_new = jnp.sum(weights, axis=-1)
    accum_new = jnp.einsum(
        "hqk,hkd->hqd",
        weights.astype(jnp.bfloat16),
        value_lines,
        preferred_element_type=jnp.float32,
    )
    mixed_output = accum_new / running_new[..., None]
    attention_result = (
        mixed_output.reshape(KEY_HEADS, QUERY_PER_KEY, token_rows, HEAD_SIZE)
        .transpose(2, 0, 1, 3)
        .reshape(token_rows, QUERY_HEADS * HEAD_SIZE)
        .astype(jnp.bfloat16)
    )
    projected_rows = times_blocks(attention_result, out_halves)
    projected_rows = projected_rows + adapter_scale * adapter_change(
        attention_result, within_prompt, output_down_map, output_up_map
    )
    residual = (hidden_input.astype(jnp.float32) + projected_rows).astype(jnp.bfloat16)
    normed_two = rms_scaled(residual, expert_norm_gain)
    logits = jnp.dot(normed_two, router, preferred_element_type=jnp.float32)
    squashed = jax.nn.sigmoid(jnp.take_along_axis(logits, routes, axis=1))
    mixing = squashed / jnp.sum(squashed, axis=1, keepdims=True)
    expert_total = router.shape[1]
    local_experts = expert_gate_weight.shape[0]
    flat_routes = routes.reshape(-1)
    slots = route_slots(flat_routes, expert_total)
    slot_total = expert_total * CAP
    route_id = (flat_routes * CAP + slots).reshape(token_rows, routes.shape[1])
    matches = route_id[:, :, None] == jnp.arange(slot_total, dtype=jnp.int32)[None, None, :]
    picks = jnp.sum(matches.astype(jnp.float32), axis=1)
    dispatch_rows = jnp.dot(
        picks.T.astype(jnp.bfloat16), normed_two, preferred_element_type=jnp.float32
    ).astype(jnp.bfloat16)
    sending = dispatch_rows.reshape(columns, local_experts, CAP, model_width)
    arrived = lax.all_to_all(sending, "col", split_axis=0, concat_axis=0, tiled=True)
    gate_vals = jnp.einsum(
        "sjcd,jdf->sjcf", arrived, expert_gate_weight, preferred_element_type=jnp.float32
    )
    up_vals = jnp.einsum(
        "sjcd,jdf->sjcf", arrived, expert_up_weight, preferred_element_type=jnp.float32
    )
    hidden_vals = (jnp.maximum(gate_vals, 0.0) * up_vals).astype(jnp.bfloat16)
    answered = jnp.einsum(
        "sjcf,jfd->sjcd", hidden_vals, expert_down_weight, preferred_element_type=jnp.float32
    ).astype(jnp.bfloat16)
    returned = lax.all_to_all(answered, "col", split_axis=0, concat_axis=0, tiled=True)
    returned_rows = returned.reshape(slot_total, model_width)
    mix_matrix = jnp.sum(jnp.where(matches, mixing[:, :, None], 0.0), axis=1)
    mix_high = mix_matrix.astype(jnp.bfloat16)
    mix_low = (mix_matrix - mix_high.astype(jnp.float32)).astype(jnp.bfloat16)
    combined = jnp.dot(mix_high, returned_rows, preferred_element_type=jnp.float32) + jnp.dot(
        mix_low, returned_rows, preferred_element_type=jnp.float32
    )
    return (residual.astype(jnp.float32) + combined).astype(jnp.bfloat16)


def solution(mesh):
    placed = (
        P(("row", "col"), None),
        P(),
        P(),
        P(("row", "col"), None),
        P(),
        P(),
        P("row", "col"),
        P("row", "col"),
        P(),
        P("col", None, None),
        P("col", None, None),
        P("col", None, None),
        P("col", None, None),
        P("col", None, None),
        P("col", None, None),
        P("col", None, None),
    )
    return jax.shard_map(
        local, mesh=mesh, in_specs=placed, out_specs=P(("row", "col"), None), check_vma=False
    )
```

```python
import jax
import jax.numpy as jnp
from jax import lax
from jax.sharding import PartitionSpec as P

QUERY_HEADS = 12
KEY_HEADS = 2
HEAD_SIZE = 128
QUERY_PER_KEY = 6
CAP = 40
LONGEST_PROMPT = 1536


norm_eps = 1e-06
rope_base = 1000000.0
adapter_scale = 0.5


def rms_scaled(value_tensor, norm_gain):
    widened = value_tensor.astype(jnp.float32)
    inverse = lax.rsqrt(jnp.mean(widened * widened, axis=-1, keepdims=True) + norm_eps)
    return (widened * inverse * norm_gain.astype(jnp.float32)).astype(jnp.bfloat16)


def prompt_layout(lengths_row, tok_index):
    prompt_ends = jnp.cumsum(lengths_row)
    starts = prompt_ends - lengths_row
    prompt_of = jnp.sum((tok_index[:, None] >= prompt_ends[None, :]).astype(jnp.int32), axis=1)
    within_prompt = prompt_of[:, None] == jnp.arange(lengths_row.shape[0], dtype=jnp.int32)[None, :]
    token_positions = tok_index - jnp.sum(jnp.where(within_prompt, starts[None, :], 0), axis=1)
    return (prompt_of, within_prompt, token_positions)


def apply_rotary(value_tensor, token_positions):
    half_width = value_tensor.shape[-1] // 2
    frequency = rope_base ** (
        -2.0 * jnp.arange(half_width, dtype=jnp.float32) / value_tensor.shape[-1]
    )
    angles = token_positions.astype(jnp.float32)[:, None] * frequency[None, :]
    cosine = jnp.cos(angles)[:, None, :]
    sine_part = jnp.sin(angles)[:, None, :]
    front_half = value_tensor[..., :half_width]
    back_half = value_tensor[..., half_width:]
    return jnp.concatenate(
        [front_half * cosine - back_half * sine_part, back_half * cosine + front_half * sine_part],
        axis=-1,
    )


def adapter_change(inputs, within_prompt, downs, ups):
    low_rank = jnp.einsum("nk,prk->npr", inputs, downs, preferred_element_type=jnp.float32)
    low_rank = jnp.where(within_prompt[:, :, None], low_rank, 0.0).astype(jnp.bfloat16)
    return jnp.einsum("npr,pro->no", low_rank, ups, preferred_element_type=jnp.float32)


def route_slots(flat_routes, expert_total):
    marks = (flat_routes[:, None] == jnp.arange(expert_total, dtype=jnp.int32)[None, :]).astype(
        jnp.int32
    )
    before = jnp.cumsum(marks, axis=0) - marks
    return jnp.sum(before * marks, axis=1)


def local(
    hidden_input,
    lengths,
    prompt_adapter,
    routes,
    attention_norm_gain,
    expert_norm_gain,
    projection_weight,
    output_weight,
    router,
    adapter_projection_down,
    adapter_projection_up,
    adapter_output_down,
    adapter_output_up,
    expert_gate_weight,
    expert_up_weight,
    expert_down_weight,
):
    token_rows = hidden_input.shape[0]
    model_width = hidden_input.shape[1]
    columns = lax.axis_size("col")
    row_index = lax.axis_index("row")
    col_index = lax.axis_index("col")
    lengths_row = lax.dynamic_index_in_dim(lengths, row_index, 0, keepdims=False)
    adapter_row = lax.dynamic_index_in_dim(prompt_adapter, row_index, 0, keepdims=False)
    tok_index = col_index * token_rows + jnp.arange(token_rows, dtype=jnp.int32)
    prompt_of, within_prompt, token_positions = prompt_layout(lengths_row, tok_index)
    local_adapters = adapter_projection_down.shape[0]
    owner_column = adapter_row // local_adapters
    nearby_slot = adapter_row % local_adapters
    owned_here = (owner_column == col_index)[:, None, None]
    tables = (adapter_projection_down, adapter_projection_up, adapter_output_down, adapter_output_up)
    picked = jnp.concatenate(
        [
            jnp.where(owned_here, jnp.take(table, nearby_slot, axis=0), jnp.zeros((), table.dtype))
            for table in tables
        ],
        axis=-1,
    )
    picked_shape = picked.shape
    lane = 128
    chunks = picked.reshape(columns, -1, lane)
    blocks = (projection_weight, output_weight)
    dest_parity = jnp.arange(columns, dtype=jnp.int32) % 2
    flat_blocks = []
    for i, block in enumerate(blocks):
        rows_here, cols_here = block.shape
        if i == 0:
            split = block.reshape(rows_here, 2, cols_here // 2)
            chosen = jnp.take(split, dest_parity, axis=1).transpose(1, 0, 2)
        else:
            chosen = jnp.broadcast_to(block[None], (columns, rows_here, cols_here))
        flat_blocks.append(chosen.reshape(columns, -1, lane))
    sizes = [chunks.shape[1]] + [flat.shape[1] for flat in flat_blocks]
    starts = [sum(sizes[:i]) for i in range(len(sizes) + 1)]
    bundle = jnp.concatenate([chunks] + flat_blocks, axis=1)
    bundle = lax.all_to_all(bundle, "col", 0, 0, tiled=True)
    received = bundle[:, starts[0] : starts[1]]
    slabs = []
    for i, block in enumerate(blocks):
        rows_here, cols_here = block.shape
        kept = cols_here // 2 if i == 0 else cols_here
        piece = bundle[:, starts[i + 1] : starts[i + 2]].reshape(columns, rows_here, kept)
        slabs.append(piece.transpose(1, 0, 2).reshape(rows_here, columns * kept))
    reduced = jnp.sum(received.astype(jnp.float32), axis=0).astype(jnp.bfloat16)
    spread = lax.all_to_all(
        jnp.broadcast_to(reduced[None], (columns,) + reduced.shape), "col", 0, 0, tiled=True
    )
    core_index = col_index % 2
    partner = [(c, c ^ 1) for c in range(columns)]

    def gather_halves(slab):
        own = lax.all_gather(slab, "row", axis=0, tiled=True)
        other = lax.ppermute(own, "col", partner)
        return own, other

    def times_halves(inputs, halves):
        own, other = halves
        piece = own.shape[1] // columns
        own_part = jnp.dot(inputs, own, preferred_element_type=jnp.float32)
        other_part = jnp.dot(inputs, other, preferred_element_type=jnp.float32)
        own_part = own_part.reshape(inputs.shape[0], columns, piece)
        other_part = other_part.reshape(inputs.shape[0], columns, piece)
        first = jnp.where(core_index == 0, own_part, other_part)
        second = jnp.where(core_index == 0, other_part, own_part)
        return jnp.stack([first, second], axis=2).reshape(inputs.shape[0], 2 * own.shape[1])

    qkv_halves = gather_halves(slabs[0])
    out_half = slabs[1].shape[1] // 2
    out_halves = gather_halves(
        lax.dynamic_slice_in_dim(slabs[1], core_index * out_half, out_half, axis=1)
    )

    def times_blocks(inputs, halves):
        own, other = halves
        half = own.shape[1]
        placed = jnp.zeros((inputs.shape[0], 2 * half), jnp.float32)
        placed = lax.dynamic_update_slice_in_dim(
            placed, jnp.dot(inputs, own, preferred_element_type=jnp.float32), core_index * half, 1
        )
        return lax.dynamic_update_slice_in_dim(
            placed,
            jnp.dot(inputs, other, preferred_element_type=jnp.float32),
            (1 - core_index) * half,
            1,
        )

    maps = spread.reshape(picked_shape)
    widths = [table.shape[-1] for table in tables]
    bounds = [sum(widths[:i]) for i in range(len(widths) + 1)]
    projection_down_map, projection_up_map, output_down_map, output_up_map = [
        maps[..., bounds[i] : bounds[i + 1]] for i in range(len(tables))
    ]
    normalized = rms_scaled(hidden_input, attention_norm_gain)
    projection_all = times_halves(normalized, qkv_halves)
    projection_all = projection_all + adapter_scale * adapter_change(
        normalized, within_prompt, projection_down_map, projection_up_map
    )
    query_slice = apply_rotary(
        projection_all[:, : QUERY_HEADS * HEAD_SIZE].reshape(token_rows, QUERY_HEADS, HEAD_SIZE),
        token_positions,
    ).astype(jnp.bfloat16)
    key_slice = apply_rotary(
        projection_all[:, QUERY_HEADS * HEAD_SIZE : (QUERY_HEADS + KEY_HEADS) * HEAD_SIZE].reshape(
            token_rows, KEY_HEADS, HEAD_SIZE
        ),
        token_positions,
    ).astype(jnp.bfloat16)
    value_slice = projection_all[:, (QUERY_HEADS + KEY_HEADS) * HEAD_SIZE :].astype(jnp.bfloat16)
    flattened_keys = key_slice.reshape(token_rows, KEY_HEADS * HEAD_SIZE)
    grouped = (
        query_slice.reshape(token_rows, KEY_HEADS, QUERY_PER_KEY, HEAD_SIZE)
        .transpose(1, 2, 0, 3)
        .reshape(KEY_HEADS, QUERY_PER_KEY * token_rows, HEAD_SIZE)
    )
    query_index = jnp.tile(tok_index, QUERY_PER_KEY)
    query_prompt = jnp.tile(prompt_of, QUERY_PER_KEY)
    key_value_piece = jnp.concatenate([flattened_keys, value_slice], axis=1)
    key_value = lax.all_to_all(
        jnp.broadcast_to(key_value_piece[None], (columns,) + key_value_piece.shape),
        "col",
        0,
        0,
        tiled=True,
    ).reshape(columns * token_rows, key_value_piece.shape[1])
    block_tokens = key_value.shape[0]
    window = min(block_tokens, LONGEST_PROMPT + token_rows)
    window_start = jnp.clip((col_index + 1) * token_rows - window, 0, block_tokens - window)
    key_value = lax.dynamic_slice_in_dim(key_value, window_start, window, axis=0)
    segments = (key_value[:, : KEY_HEADS * HEAD_SIZE], key_value[:, KEY_HEADS * HEAD_SIZE :])
    best_experts = jnp.full((KEY_HEADS, QUERY_PER_KEY * token_rows), -1e30, jnp.float32)
    segment_length = segments[0].shape[0]
    key_lines = segments[0].reshape(segment_length, KEY_HEADS, HEAD_SIZE).transpose(1, 0, 2)
    value_lines = segments[1].reshape(segment_length, KEY_HEADS, HEAD_SIZE).transpose(1, 0, 2)
    key_index = window_start + jnp.arange(segment_length, dtype=jnp.int32)
    key_prompt = prompt_layout(lengths_row, key_index)[0]
    allowed = (key_prompt[None, :] == query_prompt[:, None]) & (
        key_index[None, :] <= query_index[:, None]
    )
    scores = jnp.einsum(
        "hqd,hkd->hqk", grouped, key_lines, preferred_element_type=jnp.float32
    ) * HEAD_SIZE ** (-0.5)
    masked = jnp.where(allowed[None], scores, -1e30)
    fresh = jnp.maximum(best_experts, jnp.max(masked, axis=-1))
    weights = jnp.where(allowed[None], jnp.exp(scores - fresh[..., None]), 0.0)
    running_new = jnp.sum(weights, axis=-1)
    accum_new = jnp.einsum(
        "hqk,hkd->hqd",
        weights.astype(jnp.bfloat16),
        value_lines,
        preferred_element_type=jnp.float32,
    )
    mixed_output = accum_new / running_new[..., None]
    attention_result = (
        mixed_output.reshape(KEY_HEADS, QUERY_PER_KEY, token_rows, HEAD_SIZE)
        .transpose(2, 0, 1, 3)
        .reshape(token_rows, QUERY_HEADS * HEAD_SIZE)
        .astype(jnp.bfloat16)
    )
    projected_rows = times_blocks(attention_result, out_halves)
    projected_rows = projected_rows + adapter_scale * adapter_change(
        attention_result, within_prompt, output_down_map, output_up_map
    )
    residual = (hidden_input.astype(jnp.float32) + projected_rows).astype(jnp.bfloat16)
    normed_two = rms_scaled(residual, expert_norm_gain)
    logits = jnp.dot(normed_two, router, preferred_element_type=jnp.float32)
    squashed = jax.nn.sigmoid(jnp.take_along_axis(logits, routes, axis=1))
    mixing = squashed / jnp.sum(squashed, axis=1, keepdims=True)
    expert_total = router.shape[1]
    local_experts = expert_gate_weight.shape[0]
    flat_routes = routes.reshape(-1)
    slots = route_slots(flat_routes, expert_total)
    slot_total = expert_total * CAP
    route_id = (flat_routes * CAP + slots).reshape(token_rows, routes.shape[1])
    matches = route_id[:, :, None] == jnp.arange(slot_total, dtype=jnp.int32)[None, None, :]
    picks = jnp.sum(matches.astype(jnp.float32), axis=1)
    dispatch_rows = jnp.dot(
        picks.T.astype(jnp.bfloat16), normed_two, preferred_element_type=jnp.float32
    ).astype(jnp.bfloat16)
    sending = dispatch_rows.reshape(columns, local_experts, CAP, model_width)
    arrived = lax.all_to_all(sending, "col", split_axis=0, concat_axis=0, tiled=True)
    expert_rows = arrived.transpose(1, 0, 2, 3).reshape(local_experts, columns * CAP, model_width)
    gate_vals = jnp.einsum(
        "jnd,jdf->jnf", expert_rows, expert_gate_weight, preferred_element_type=jnp.float32
    )
    up_vals = jnp.einsum(
        "jnd,jdf->jnf", expert_rows, expert_up_weight, preferred_element_type=jnp.float32
    )
    hidden_vals = (jnp.maximum(gate_vals, 0.0) * up_vals).astype(jnp.bfloat16)
    answered = jnp.einsum(
        "jnf,jfd->jnd", hidden_vals, expert_down_weight, preferred_element_type=jnp.float32
    ).astype(jnp.bfloat16)
    answered = answered.reshape(local_experts, columns, CAP, model_width).transpose(1, 0, 2, 3)
    returned = lax.all_to_all(answered, "col", split_axis=0, concat_axis=0, tiled=True)
    returned_rows = returned.reshape(slot_total, model_width)
    mix_matrix = jnp.sum(jnp.where(matches, mixing[:, :, None], 0.0), axis=1)
    mix_high = mix_matrix.astype(jnp.bfloat16)
    mix_low = (mix_matrix - mix_high.astype(jnp.float32)).astype(jnp.bfloat16)
    combined = jnp.dot(mix_high, returned_rows, preferred_element_type=jnp.float32) + jnp.dot(
        mix_low, returned_rows, preferred_element_type=jnp.float32
    )
    return (residual.astype(jnp.float32) + combined).astype(jnp.bfloat16)


def solution(mesh):
    placed = (
        P(("row", "col"), None),
        P(),
        P(),
        P(("row", "col"), None),
        P(),
        P(),
        P("row", "col"),
        P("row", "col"),
        P(),
        P("col", None, None),
        P("col", None, None),
        P("col", None, None),
        P("col", None, None),
        P("col", None, None),
        P("col", None, None),
        P("col", None, None),
    )
    return jax.shard_map(
        local, mesh=mesh, in_specs=placed, out_specs=P(("row", "col"), None), check_vma=False
    )
```

```python
import jax
import jax.numpy as jnp
from jax import lax
from jax.sharding import PartitionSpec as P

QUERY_HEADS = 12
KEY_HEADS = 2
HEAD_SIZE = 128
QUERY_PER_KEY = 6
CAP = 40
LONGEST_PROMPT = 1536


norm_eps = 1e-06
rope_base = 1000000.0
adapter_scale = 0.5


def rms_scaled(value_tensor, norm_gain):
    widened = value_tensor.astype(jnp.float32)
    inverse = lax.rsqrt(jnp.mean(widened * widened, axis=-1, keepdims=True) + norm_eps)
    return (widened * inverse * norm_gain.astype(jnp.float32)).astype(jnp.bfloat16)


def prompt_layout(lengths_row, tok_index):
    prompt_ends = jnp.cumsum(lengths_row)
    starts = prompt_ends - lengths_row
    prompt_of = jnp.sum((tok_index[:, None] >= prompt_ends[None, :]).astype(jnp.int32), axis=1)
    within_prompt = prompt_of[:, None] == jnp.arange(lengths_row.shape[0], dtype=jnp.int32)[None, :]
    token_positions = tok_index - jnp.sum(jnp.where(within_prompt, starts[None, :], 0), axis=1)
    return (prompt_of, within_prompt, token_positions)


def apply_rotary(value_tensor, token_positions):
    half_width = value_tensor.shape[-1] // 2
    frequency = rope_base ** (
        -2.0 * jnp.arange(half_width, dtype=jnp.float32) / value_tensor.shape[-1]
    )
    angles = token_positions.astype(jnp.float32)[:, None] * frequency[None, :]
    cosine = jnp.cos(angles)[:, None, :]
    sine_part = jnp.sin(angles)[:, None, :]
    front_half = value_tensor[..., :half_width]
    back_half = value_tensor[..., half_width:]
    return jnp.concatenate(
        [front_half * cosine - back_half * sine_part, back_half * cosine + front_half * sine_part],
        axis=-1,
    )


def adapter_change(inputs, within_prompt, downs, ups):
    low_rank = jnp.einsum("nk,prk->npr", inputs, downs, preferred_element_type=jnp.float32)
    low_rank = jnp.where(within_prompt[:, :, None], low_rank, 0.0).astype(jnp.bfloat16)
    return jnp.einsum("npr,pro->no", low_rank, ups, preferred_element_type=jnp.float32)


def route_slots(flat_routes, expert_total):
    marks = (flat_routes[:, None] == jnp.arange(expert_total, dtype=jnp.int32)[None, :]).astype(
        jnp.int32
    )
    before = jnp.cumsum(marks, axis=0) - marks
    return jnp.sum(before * marks, axis=1)


def local(
    hidden_input,
    lengths,
    prompt_adapter,
    routes,
    attention_norm_gain,
    expert_norm_gain,
    projection_weight,
    output_weight,
    router,
    adapter_projection_down,
    adapter_projection_up,
    adapter_output_down,
    adapter_output_up,
    expert_gate_weight,
    expert_up_weight,
    expert_down_weight,
):
    token_rows = hidden_input.shape[0]
    model_width = hidden_input.shape[1]
    columns = lax.axis_size("col")
    row_index = lax.axis_index("row")
    col_index = lax.axis_index("col")
    lengths_row = lax.dynamic_index_in_dim(lengths, row_index, 0, keepdims=False)
    adapter_row = lax.dynamic_index_in_dim(prompt_adapter, row_index, 0, keepdims=False)
    tok_index = col_index * token_rows + jnp.arange(token_rows, dtype=jnp.int32)
    prompt_of, within_prompt, token_positions = prompt_layout(lengths_row, tok_index)
    local_adapters = adapter_projection_down.shape[0]
    owner_column = adapter_row // local_adapters
    nearby_slot = adapter_row % local_adapters
    owned_here = (owner_column == col_index)[:, None, None]
    tables = (adapter_projection_down, adapter_projection_up, adapter_output_down, adapter_output_up)
    picked = jnp.concatenate(
        [
            jnp.where(owned_here, jnp.take(table, nearby_slot, axis=0), jnp.zeros((), table.dtype))
            for table in tables
        ],
        axis=-1,
    )
    picked_shape = picked.shape
    lane = 128
    chunks = picked.reshape(columns, -1, lane)
    blocks = (projection_weight, output_weight)
    dest_parity = jnp.arange(columns, dtype=jnp.int32) % 2
    flat_blocks = []
    for i, block in enumerate(blocks):
        rows_here, cols_here = block.shape
        if i == 0:
            split = block.reshape(rows_here, 2, cols_here // 2)
            chosen = jnp.take(split, dest_parity, axis=1).transpose(1, 0, 2)
        else:
            chosen = jnp.broadcast_to(block[None], (columns, rows_here, cols_here))
        flat_blocks.append(chosen.reshape(columns, -1, lane))
    sizes = [chunks.shape[1]] + [flat.shape[1] for flat in flat_blocks]
    starts = [sum(sizes[:i]) for i in range(len(sizes) + 1)]
    bundle = jnp.concatenate([chunks] + flat_blocks, axis=1)
    bundle = lax.all_to_all(bundle, "col", 0, 0, tiled=True)
    received = bundle[:, starts[0] : starts[1]]
    slabs = []
    for i, block in enumerate(blocks):
        rows_here, cols_here = block.shape
        kept = cols_here // 2 if i == 0 else cols_here
        piece = bundle[:, starts[i + 1] : starts[i + 2]].reshape(columns, rows_here, kept)
        slabs.append(piece.transpose(1, 0, 2).reshape(rows_here, columns * kept))
    reduced = jnp.sum(received.astype(jnp.float32), axis=0).astype(jnp.bfloat16)
    spread = lax.all_to_all(
        jnp.broadcast_to(reduced[None], (columns,) + reduced.shape), "col", 0, 0, tiled=True
    )
    core_index = col_index % 2
    partner = [(c, c ^ 1) for c in range(columns)]

    def gather_halves(slab):
        own = lax.all_gather(slab, "row", axis=0, tiled=True)
        other = lax.ppermute(own, "col", partner)
        return own, other

    def times_halves(inputs, halves):
        own, other = halves
        piece = own.shape[1] // columns
        own_part = jnp.dot(inputs, own, preferred_element_type=jnp.float32)
        other_part = jnp.dot(inputs, other, preferred_element_type=jnp.float32)
        own_part = own_part.reshape(inputs.shape[0], columns, piece)
        other_part = other_part.reshape(inputs.shape[0], columns, piece)
        first = jnp.where(core_index == 0, own_part, other_part)
        second = jnp.where(core_index == 0, other_part, own_part)
        return jnp.stack([first, second], axis=2).reshape(inputs.shape[0], 2 * own.shape[1])

    qkv_halves = gather_halves(slabs[0])
    out_half = slabs[1].shape[1] // 2
    out_halves = gather_halves(
        lax.dynamic_slice_in_dim(slabs[1], core_index * out_half, out_half, axis=1)
    )

    def times_blocks(inputs, halves):
        own, other = halves
        half = own.shape[1]
        placed = jnp.zeros((inputs.shape[0], 2 * half), jnp.float32)
        placed = lax.dynamic_update_slice_in_dim(
            placed, jnp.dot(inputs, own, preferred_element_type=jnp.float32), core_index * half, 1
        )
        return lax.dynamic_update_slice_in_dim(
            placed,
            jnp.dot(inputs, other, preferred_element_type=jnp.float32),
            (1 - core_index) * half,
            1,
        )

    maps = spread.reshape(picked_shape)
    widths = [table.shape[-1] for table in tables]
    bounds = [sum(widths[:i]) for i in range(len(widths) + 1)]
    projection_down_map, projection_up_map, output_down_map, output_up_map = [
        maps[..., bounds[i] : bounds[i + 1]] for i in range(len(tables))
    ]
    normalized = rms_scaled(hidden_input, attention_norm_gain)
    projection_all = times_halves(normalized, qkv_halves)
    projection_all = projection_all + adapter_scale * adapter_change(
        normalized, within_prompt, projection_down_map, projection_up_map
    )
    query_slice = apply_rotary(
        projection_all[:, : QUERY_HEADS * HEAD_SIZE].reshape(token_rows, QUERY_HEADS, HEAD_SIZE),
        token_positions,
    ).astype(jnp.bfloat16)
    key_slice = apply_rotary(
        projection_all[:, QUERY_HEADS * HEAD_SIZE : (QUERY_HEADS + KEY_HEADS) * HEAD_SIZE].reshape(
            token_rows, KEY_HEADS, HEAD_SIZE
        ),
        token_positions,
    ).astype(jnp.bfloat16)
    value_slice = projection_all[:, (QUERY_HEADS + KEY_HEADS) * HEAD_SIZE :].astype(jnp.bfloat16)
    flattened_keys = key_slice.reshape(token_rows, KEY_HEADS * HEAD_SIZE)
    grouped = (
        query_slice.reshape(token_rows, KEY_HEADS, QUERY_PER_KEY, HEAD_SIZE)
        .transpose(1, 2, 0, 3)
        .reshape(KEY_HEADS, QUERY_PER_KEY * token_rows, HEAD_SIZE)
    )
    query_index = jnp.tile(tok_index, QUERY_PER_KEY)
    query_prompt = jnp.tile(prompt_of, QUERY_PER_KEY)
    key_value_piece = jnp.concatenate([flattened_keys, value_slice], axis=1)
    key_value = lax.all_to_all(
        jnp.broadcast_to(key_value_piece[None], (columns,) + key_value_piece.shape),
        "col",
        0,
        0,
        tiled=True,
    ).reshape(columns * token_rows, key_value_piece.shape[1])
    block_tokens = key_value.shape[0]
    window = min(block_tokens, LONGEST_PROMPT + token_rows)
    window_start = jnp.clip((col_index + 1) * token_rows - window, 0, block_tokens - window)
    key_value = lax.dynamic_slice_in_dim(key_value, window_start, window, axis=0)
    segments = (key_value[:, : KEY_HEADS * HEAD_SIZE], key_value[:, KEY_HEADS * HEAD_SIZE :])
    best_experts = jnp.full((KEY_HEADS, QUERY_PER_KEY * token_rows), -1e30, jnp.float32)
    segment_length = segments[0].shape[0]
    key_lines = segments[0].reshape(segment_length, KEY_HEADS, HEAD_SIZE).transpose(1, 0, 2)
    value_lines = segments[1].reshape(segment_length, KEY_HEADS, HEAD_SIZE).transpose(1, 0, 2)
    key_index = window_start + jnp.arange(segment_length, dtype=jnp.int32)
    key_prompt = prompt_layout(lengths_row, key_index)[0]
    allowed = (key_prompt[None, :] == query_prompt[:, None]) & (
        key_index[None, :] <= query_index[:, None]
    )
    scores = jnp.einsum(
        "hqd,hkd->hqk", grouped, key_lines, preferred_element_type=jnp.float32
    ) * HEAD_SIZE ** (-0.5)
    masked = jnp.where(allowed[None], scores, -1e30)
    fresh = jnp.maximum(best_experts, jnp.max(masked, axis=-1))
    weights = jnp.where(allowed[None], jnp.exp(scores - fresh[..., None]), 0.0)
    running_new = jnp.sum(weights, axis=-1)
    accum_new = jnp.einsum(
        "hqk,hkd->hqd",
        weights.astype(jnp.bfloat16),
        value_lines,
        preferred_element_type=jnp.float32,
    )
    mixed_output = accum_new / running_new[..., None]
    attention_result = (
        mixed_output.reshape(KEY_HEADS, QUERY_PER_KEY, token_rows, HEAD_SIZE)
        .transpose(2, 0, 1, 3)
        .reshape(token_rows, QUERY_HEADS * HEAD_SIZE)
        .astype(jnp.bfloat16)
    )
    projected_rows = times_blocks(attention_result, out_halves)
    projected_rows = projected_rows + adapter_scale * adapter_change(
        attention_result, within_prompt, output_down_map, output_up_map
    )
    residual = (hidden_input.astype(jnp.float32) + projected_rows).astype(jnp.bfloat16)
    normed_two = rms_scaled(residual, expert_norm_gain)
    logits = jnp.dot(normed_two, router, preferred_element_type=jnp.float32)
    route_hits = routes[:, :, None] == jnp.arange(logits.shape[1], dtype=jnp.int32)[None, None, :]
    picked_logits = jnp.sum(jnp.where(route_hits, logits[:, None, :], 0.0), axis=2)
    squashed = jax.nn.sigmoid(picked_logits)
    mixing = squashed / jnp.sum(squashed, axis=1, keepdims=True)
    expert_total = router.shape[1]
    local_experts = expert_gate_weight.shape[0]
    flat_routes = routes.reshape(-1)
    slots = route_slots(flat_routes, expert_total)
    slot_total = expert_total * CAP
    route_id = (flat_routes * CAP + slots).reshape(token_rows, routes.shape[1])
    matches = route_id[:, :, None] == jnp.arange(slot_total, dtype=jnp.int32)[None, None, :]
    picks = jnp.sum(matches.astype(jnp.float32), axis=1)
    dispatch_rows = jnp.dot(
        picks.T.astype(jnp.bfloat16), normed_two, preferred_element_type=jnp.float32
    ).astype(jnp.bfloat16)
    sending = dispatch_rows.reshape(columns, local_experts, CAP, model_width)
    arrived = lax.all_to_all(sending, "col", split_axis=0, concat_axis=0, tiled=True)
    gate_vals = jnp.einsum(
        "sjcd,jdf->sjcf", arrived, expert_gate_weight, preferred_element_type=jnp.float32
    )
    up_vals = jnp.einsum(
        "sjcd,jdf->sjcf", arrived, expert_up_weight, preferred_element_type=jnp.float32
    )
    hidden_vals = (jnp.maximum(gate_vals, 0.0) * up_vals).astype(jnp.bfloat16)
    answered = jnp.einsum(
        "sjcf,jfd->sjcd", hidden_vals, expert_down_weight, preferred_element_type=jnp.float32
    ).astype(jnp.bfloat16)
    returned = lax.all_to_all(answered, "col", split_axis=0, concat_axis=0, tiled=True)
    returned_rows = returned.reshape(slot_total, model_width)
    mix_matrix = jnp.sum(jnp.where(matches, mixing[:, :, None], 0.0), axis=1)
    mix_high = mix_matrix.astype(jnp.bfloat16)
    mix_low = (mix_matrix - mix_high.astype(jnp.float32)).astype(jnp.bfloat16)
    combined = jnp.dot(mix_high, returned_rows, preferred_element_type=jnp.float32) + jnp.dot(
        mix_low, returned_rows, preferred_element_type=jnp.float32
    )
    return (residual.astype(jnp.float32) + combined).astype(jnp.bfloat16)


def solution(mesh):
    placed = (
        P(("row", "col"), None),
        P(),
        P(),
        P(("row", "col"), None),
        P(),
        P(),
        P("row", "col"),
        P("row", "col"),
        P(),
        P("col", None, None),
        P("col", None, None),
        P("col", None, None),
        P("col", None, None),
        P("col", None, None),
        P("col", None, None),
        P("col", None, None),
    )
    return jax.shard_map(
        local, mesh=mesh, in_specs=placed, out_specs=P(("row", "col"), None), check_vma=False
    )
```

```python
import jax
import jax.numpy as jnp
from jax import lax
from jax.sharding import PartitionSpec as P

QUERY_HEADS = 12
KEY_HEADS = 2
HEAD_SIZE = 128
QUERY_PER_KEY = 6
CAP = 40
LONGEST_PROMPT = 1536


norm_eps = 1e-06
rope_base = 1000000.0
adapter_scale = 0.5


def rms_scaled(value_tensor, norm_gain):
    widened = value_tensor.astype(jnp.float32)
    inverse = lax.rsqrt(jnp.mean(widened * widened, axis=-1, keepdims=True) + norm_eps)
    return (widened * inverse * norm_gain.astype(jnp.float32)).astype(jnp.bfloat16)


def prompt_layout(lengths_row, tok_index):
    prompt_ends = jnp.cumsum(lengths_row)
    starts = prompt_ends - lengths_row
    prompt_of = jnp.sum((tok_index[:, None] >= prompt_ends[None, :]).astype(jnp.int32), axis=1)
    within_prompt = prompt_of[:, None] == jnp.arange(lengths_row.shape[0], dtype=jnp.int32)[None, :]
    token_positions = tok_index - jnp.sum(jnp.where(within_prompt, starts[None, :], 0), axis=1)
    return (prompt_of, within_prompt, token_positions)


def apply_rotary(value_tensor, token_positions):
    half_width = value_tensor.shape[-1] // 2
    frequency = rope_base ** (
        -2.0 * jnp.arange(half_width, dtype=jnp.float32) / value_tensor.shape[-1]
    )
    angles = token_positions.astype(jnp.float32)[:, None] * frequency[None, :]
    cosine = jnp.cos(angles)[:, None, :]
    sine_part = jnp.sin(angles)[:, None, :]
    front_half = value_tensor[..., :half_width]
    back_half = value_tensor[..., half_width:]
    return jnp.concatenate(
        [front_half * cosine - back_half * sine_part, back_half * cosine + front_half * sine_part],
        axis=-1,
    )


def adapter_change(inputs, within_prompt, downs, ups):
    low_rank = jnp.einsum("nk,prk->npr", inputs, downs, preferred_element_type=jnp.float32)
    low_rank = jnp.where(within_prompt[:, :, None], low_rank, 0.0).astype(jnp.bfloat16)
    return jnp.einsum("npr,pro->no", low_rank, ups, preferred_element_type=jnp.float32)


def route_slots(flat_routes, expert_total):
    marks = (flat_routes[:, None] == jnp.arange(expert_total, dtype=jnp.int32)[None, :]).astype(
        jnp.int32
    )
    before = jnp.cumsum(marks, axis=0) - marks
    return jnp.sum(before * marks, axis=1)


def local(
    hidden_input,
    lengths,
    prompt_adapter,
    routes,
    attention_norm_gain,
    expert_norm_gain,
    projection_weight,
    output_weight,
    router,
    adapter_projection_down,
    adapter_projection_up,
    adapter_output_down,
    adapter_output_up,
    expert_gate_weight,
    expert_up_weight,
    expert_down_weight,
):
    token_rows = hidden_input.shape[0]
    model_width = hidden_input.shape[1]
    columns = lax.axis_size("col")
    row_index = lax.axis_index("row")
    col_index = lax.axis_index("col")
    lengths_row = lax.dynamic_index_in_dim(lengths, row_index, 0, keepdims=False)
    adapter_row = lax.dynamic_index_in_dim(prompt_adapter, row_index, 0, keepdims=False)
    tok_index = col_index * token_rows + jnp.arange(token_rows, dtype=jnp.int32)
    prompt_of, within_prompt, token_positions = prompt_layout(lengths_row, tok_index)
    local_adapters = adapter_projection_down.shape[0]
    owner_column = adapter_row // local_adapters
    nearby_slot = adapter_row % local_adapters
    owned_here = (owner_column == col_index)[:, None, None]
    slot_hits = nearby_slot[:, None] == jnp.arange(local_adapters, dtype=jnp.int32)[None, :]

    def pick_local(table):
        chosen = jnp.where(slot_hits[:, :, None, None], table[None], jnp.zeros((), table.dtype))
        return jnp.sum(chosen.astype(jnp.float32), axis=1).astype(table.dtype)

    tables = (adapter_projection_down, adapter_projection_up, adapter_output_down, adapter_output_up)
    picked = jnp.concatenate(
        [
            jnp.where(owned_here, pick_local(table), jnp.zeros((), table.dtype))
            for table in tables
        ],
        axis=-1,
    )
    picked_shape = picked.shape
    lane = 128
    chunks = picked.reshape(columns, -1, lane)
    blocks = (projection_weight, output_weight)
    dest_parity = jnp.arange(columns, dtype=jnp.int32) % 2
    flat_blocks = []
    for i, block in enumerate(blocks):
        rows_here, cols_here = block.shape
        if i == 0:
            split = block.reshape(rows_here, 2, cols_here // 2)
            chosen = jnp.take(split, dest_parity, axis=1).transpose(1, 0, 2)
        else:
            chosen = jnp.broadcast_to(block[None], (columns, rows_here, cols_here))
        flat_blocks.append(chosen.reshape(columns, -1, lane))
    sizes = [chunks.shape[1]] + [flat.shape[1] for flat in flat_blocks]
    starts = [sum(sizes[:i]) for i in range(len(sizes) + 1)]
    bundle = jnp.concatenate([chunks] + flat_blocks, axis=1)
    bundle = lax.all_to_all(bundle, "col", 0, 0, tiled=True)
    received = bundle[:, starts[0] : starts[1]]
    slabs = []
    for i, block in enumerate(blocks):
        rows_here, cols_here = block.shape
        kept = cols_here // 2 if i == 0 else cols_here
        piece = bundle[:, starts[i + 1] : starts[i + 2]].reshape(columns, rows_here, kept)
        slabs.append(piece.transpose(1, 0, 2).reshape(rows_here, columns * kept))
    reduced = jnp.sum(received.astype(jnp.float32), axis=0).astype(jnp.bfloat16)
    spread = lax.all_to_all(
        jnp.broadcast_to(reduced[None], (columns,) + reduced.shape), "col", 0, 0, tiled=True
    )
    core_index = col_index % 2
    partner = [(c, c ^ 1) for c in range(columns)]

    def gather_halves(slab):
        own = lax.all_gather(slab, "row", axis=0, tiled=True)
        other = lax.ppermute(own, "col", partner)
        return own, other

    def times_halves(inputs, halves):
        own, other = halves
        piece = own.shape[1] // columns
        own_part = jnp.dot(inputs, own, preferred_element_type=jnp.float32)
        other_part = jnp.dot(inputs, other, preferred_element_type=jnp.float32)
        own_part = own_part.reshape(inputs.shape[0], columns, piece)
        other_part = other_part.reshape(inputs.shape[0], columns, piece)
        first = jnp.where(core_index == 0, own_part, other_part)
        second = jnp.where(core_index == 0, other_part, own_part)
        return jnp.stack([first, second], axis=2).reshape(inputs.shape[0], 2 * own.shape[1])

    qkv_halves = gather_halves(slabs[0])
    out_half = slabs[1].shape[1] // 2
    out_halves = gather_halves(
        lax.dynamic_slice_in_dim(slabs[1], core_index * out_half, out_half, axis=1)
    )

    def times_blocks(inputs, halves):
        own, other = halves
        half = own.shape[1]
        placed = jnp.zeros((inputs.shape[0], 2 * half), jnp.float32)
        placed = lax.dynamic_update_slice_in_dim(
            placed, jnp.dot(inputs, own, preferred_element_type=jnp.float32), core_index * half, 1
        )
        return lax.dynamic_update_slice_in_dim(
            placed,
            jnp.dot(inputs, other, preferred_element_type=jnp.float32),
            (1 - core_index) * half,
            1,
        )

    maps = spread.reshape(picked_shape)
    widths = [table.shape[-1] for table in tables]
    bounds = [sum(widths[:i]) for i in range(len(widths) + 1)]
    projection_down_map, projection_up_map, output_down_map, output_up_map = [
        maps[..., bounds[i] : bounds[i + 1]] for i in range(len(tables))
    ]
    normalized = rms_scaled(hidden_input, attention_norm_gain)
    projection_all = times_halves(normalized, qkv_halves)
    projection_all = projection_all + adapter_scale * adapter_change(
        normalized, within_prompt, projection_down_map, projection_up_map
    )
    query_slice = apply_rotary(
        projection_all[:, : QUERY_HEADS * HEAD_SIZE].reshape(token_rows, QUERY_HEADS, HEAD_SIZE),
        token_positions,
    ).astype(jnp.bfloat16)
    key_slice = apply_rotary(
        projection_all[:, QUERY_HEADS * HEAD_SIZE : (QUERY_HEADS + KEY_HEADS) * HEAD_SIZE].reshape(
            token_rows, KEY_HEADS, HEAD_SIZE
        ),
        token_positions,
    ).astype(jnp.bfloat16)
    value_slice = projection_all[:, (QUERY_HEADS + KEY_HEADS) * HEAD_SIZE :].astype(jnp.bfloat16)
    flattened_keys = key_slice.reshape(token_rows, KEY_HEADS * HEAD_SIZE)
    grouped = (
        query_slice.reshape(token_rows, KEY_HEADS, QUERY_PER_KEY, HEAD_SIZE)
        .transpose(1, 2, 0, 3)
        .reshape(KEY_HEADS, QUERY_PER_KEY * token_rows, HEAD_SIZE)
    )
    query_index = jnp.tile(tok_index, QUERY_PER_KEY)
    query_prompt = jnp.tile(prompt_of, QUERY_PER_KEY)
    key_value_piece = jnp.concatenate([flattened_keys, value_slice], axis=1)
    key_value = lax.all_to_all(
        jnp.broadcast_to(key_value_piece[None], (columns,) + key_value_piece.shape),
        "col",
        0,
        0,
        tiled=True,
    ).reshape(columns * token_rows, key_value_piece.shape[1])
    block_tokens = key_value.shape[0]
    window = min(block_tokens, LONGEST_PROMPT + token_rows)
    window_start = jnp.clip((col_index + 1) * token_rows - window, 0, block_tokens - window)
    key_value = lax.dynamic_slice_in_dim(key_value, window_start, window, axis=0)
    segments = (key_value[:, : KEY_HEADS * HEAD_SIZE], key_value[:, KEY_HEADS * HEAD_SIZE :])
    best_experts = jnp.full((KEY_HEADS, QUERY_PER_KEY * token_rows), -1e30, jnp.float32)
    segment_length = segments[0].shape[0]
    key_lines = segments[0].reshape(segment_length, KEY_HEADS, HEAD_SIZE).transpose(1, 0, 2)
    value_lines = segments[1].reshape(segment_length, KEY_HEADS, HEAD_SIZE).transpose(1, 0, 2)
    key_index = window_start + jnp.arange(segment_length, dtype=jnp.int32)
    key_prompt = prompt_layout(lengths_row, key_index)[0]
    allowed = (key_prompt[None, :] == query_prompt[:, None]) & (
        key_index[None, :] <= query_index[:, None]
    )
    scores = jnp.einsum(
        "hqd,hkd->hqk", grouped, key_lines, preferred_element_type=jnp.float32
    ) * HEAD_SIZE ** (-0.5)
    masked = jnp.where(allowed[None], scores, -1e30)
    fresh = jnp.maximum(best_experts, jnp.max(masked, axis=-1))
    weights = jnp.where(allowed[None], jnp.exp(scores - fresh[..., None]), 0.0)
    running_new = jnp.sum(weights, axis=-1)
    accum_new = jnp.einsum(
        "hqk,hkd->hqd",
        weights.astype(jnp.bfloat16),
        value_lines,
        preferred_element_type=jnp.float32,
    )
    mixed_output = accum_new / running_new[..., None]
    attention_result = (
        mixed_output.reshape(KEY_HEADS, QUERY_PER_KEY, token_rows, HEAD_SIZE)
        .transpose(2, 0, 1, 3)
        .reshape(token_rows, QUERY_HEADS * HEAD_SIZE)
        .astype(jnp.bfloat16)
    )
    projected_rows = times_blocks(attention_result, out_halves)
    projected_rows = projected_rows + adapter_scale * adapter_change(
        attention_result, within_prompt, output_down_map, output_up_map
    )
    residual = (hidden_input.astype(jnp.float32) + projected_rows).astype(jnp.bfloat16)
    normed_two = rms_scaled(residual, expert_norm_gain)
    logits = jnp.dot(normed_two, router, preferred_element_type=jnp.float32)
    route_hits = routes[:, :, None] == jnp.arange(logits.shape[1], dtype=jnp.int32)[None, None, :]
    picked_logits = jnp.sum(jnp.where(route_hits, logits[:, None, :], 0.0), axis=2)
    squashed = jax.nn.sigmoid(picked_logits)
    mixing = squashed / jnp.sum(squashed, axis=1, keepdims=True)
    expert_total = router.shape[1]
    local_experts = expert_gate_weight.shape[0]
    flat_routes = routes.reshape(-1)
    slots = route_slots(flat_routes, expert_total)
    slot_total = expert_total * CAP
    route_id = (flat_routes * CAP + slots).reshape(token_rows, routes.shape[1])
    matches = route_id[:, :, None] == jnp.arange(slot_total, dtype=jnp.int32)[None, None, :]
    picks = jnp.sum(matches.astype(jnp.float32), axis=1)
    dispatch_rows = jnp.dot(
        picks.T.astype(jnp.bfloat16), normed_two, preferred_element_type=jnp.float32
    ).astype(jnp.bfloat16)
    sending = dispatch_rows.reshape(columns, local_experts, CAP, model_width)
    arrived = lax.all_to_all(sending, "col", split_axis=0, concat_axis=0, tiled=True)
    gate_vals = jnp.einsum(
        "sjcd,jdf->sjcf", arrived, expert_gate_weight, preferred_element_type=jnp.float32
    )
    up_vals = jnp.einsum(
        "sjcd,jdf->sjcf", arrived, expert_up_weight, preferred_element_type=jnp.float32
    )
    hidden_vals = (jnp.maximum(gate_vals, 0.0) * up_vals).astype(jnp.bfloat16)
    answered = jnp.einsum(
        "sjcf,jfd->sjcd", hidden_vals, expert_down_weight, preferred_element_type=jnp.float32
    ).astype(jnp.bfloat16)
    returned = lax.all_to_all(answered, "col", split_axis=0, concat_axis=0, tiled=True)
    returned_rows = returned.reshape(slot_total, model_width)
    mix_matrix = jnp.sum(jnp.where(matches, mixing[:, :, None], 0.0), axis=1)
    mix_high = mix_matrix.astype(jnp.bfloat16)
    mix_low = (mix_matrix - mix_high.astype(jnp.float32)).astype(jnp.bfloat16)
    combined = jnp.dot(mix_high, returned_rows, preferred_element_type=jnp.float32) + jnp.dot(
        mix_low, returned_rows, preferred_element_type=jnp.float32
    )
    return (residual.astype(jnp.float32) + combined).astype(jnp.bfloat16)


def solution(mesh):
    placed = (
        P(("row", "col"), None),
        P(),
        P(),
        P(("row", "col"), None),
        P(),
        P(),
        P("row", "col"),
        P("row", "col"),
        P(),
        P("col", None, None),
        P("col", None, None),
        P("col", None, None),
        P("col", None, None),
        P("col", None, None),
        P("col", None, None),
        P("col", None, None),
    )
    return jax.shard_map(
        local, mesh=mesh, in_specs=placed, out_specs=P(("row", "col"), None), check_vma=False
    )
```
